32 devices in a mesh: dom: 32 (over z, y, x, core).
Axes of the slice: x: 2, y: 2, z: 4, core: 2. Of those that a mesh axis runs over, the one named last changes fastest.
Arguments:
- x_block: float32 [8, 49152], P(None, 'dom'), may hold values from -18 to 18
- p_block: float32 [8, 49152], P(None, 'dom'), may hold values from -18 to 18
- stiff_elem: float32 [20, 20, 8192], P(None, None, 'dom'), may hold values from -6 to 12.4, as said below
- mass_elem: float32 [20, 20, 8192], P(None, None, 'dom'), may hold values from -0.03 to 0.7, as said below
- node_elem: float32 [10, 10, 8192], P(None, None, 'dom'), may hold values from -1 to 6.1, as said below
- elem_edge: int32 [20, 8192], P(None, 'dom'), may hold values from 0 to 1919, as said below
- elem_node: int32 [10, 8192], P(None, 'dom'), may hold values from 0 to 575, as said below
- send_edge: int32 [6, 2048], P(None, 'dom'), may hold values from 0 to 1535, as said below
- send_node: int32 [6, 1024], P(None, 'dom'), may hold values from 0 to 383, as said below
- grad_pairs: int32 [2, 49152], P(None, 'dom'), may hold values from 0 to 575, as said below
Outputs:
- w_block: float32 [8, 49152], P(None, 'dom')
- gram_stiff: float32 [24, 24], replicated
- gram_mass: float32 [24, 24], replicated
The draws below stay inside these ranges and needn't reach their ends.
Inputs may be any that keep to these rules, and one draw needn't show every extreme that they name: `stiff_elem`: each element's matrix is symmetric and positive definite. `mass_elem`: each element's matrix is symmetric and positive definite. `node_elem`: each element's matrix is symmetric and positive definite. `elem_edge`: the 20 entries of one element are distinct, and every entry of a subdomain's extended edge list is used by some element of that subdomain. `elem_node`: the 10 entries of one element are distinct, and every entry of a subdomain's extended nodal list is used by some element of that subdomain. `send_edge`: the 64 entries of one direction of one subdomain are distinct. `send_node`: the 32 entries of one direction of one subdomain are distinct. `grad_pairs`: the tail and head of one edge unknown differ.
All inputs are finite; a program needn't handle non-finite values.
Results may differ from the reference program's by a relative error of at most 0.0001.
Values sent between devices are 32-bit elements; how exact they have to be, the bound alone decides.
No kernel may reach another device: no remote copies, remote signals or barrier semaphores. Data moves between devices by JAX's collectives and lax.ppermute only.
A program may use at most 128 MiB of HBM per device.

```python
import math
import jax
import jax.numpy as jnp
import numpy as np
from jax import lax

EL = 256
MODES = 8
EDOF = 20
NDOF = 10
CHEB_DEG = 3
DOMAINS = 32
NEDGE = 1536
NNODE = 384
GE = 64
GN = 32
TOTAL_EL = 8192
TOTAL_EDGE = 49152
TOTAL_NODE = 12288


def device_scale(devices, per_device):
    position = (jnp.arange(devices * per_device) // per_device).astype(jnp.float32)
    return 1.0 + 2.0 * position / max(devices - 1, 1)


def block_draw(key, salt):
    devices = TOTAL_EDGE // NEDGE
    subkeys = jax.random.split(jax.random.fold_in(key, salt), 1)
    values = jnp.clip(jax.random.normal(subkeys[0], (MODES, TOTAL_EDGE), jnp.float32), -5.0, 5.0)
    return values * device_scale(devices, NEDGE)[None, :]


def local_tables():
    tetra_edges = [(0, 1), (0, 2), (0, 3), (1, 2), (1, 3), (2, 3)]
    middle = {}
    for number, couple in enumerate(tetra_edges):
        middle[couple] = 4 + number
    edge_links = []
    for couple in tetra_edges:
        edge_links.append((couple[0], middle[couple]))
        edge_links.append((middle[couple], couple[1]))
    faces = [(0, 1, 2), (0, 1, 3), (0, 2, 3), (1, 2, 3)]
    cycles = []
    for corner_one, corner_two, corner_three in faces:
        front_middle = middle[corner_one, corner_two]
        side_middle = middle[corner_one, corner_three]
        back_middle = middle[corner_two, corner_three]
        edge_links.append((front_middle, side_middle))
        edge_links.append((front_middle, back_middle))
        cycles.append([corner_one, front_middle, side_middle])
        cycles.append([corner_two, back_middle, front_middle])
        cycles.append([corner_three, side_middle, front_middle, back_middle])
    node_rows = np.zeros((len(edge_links), 10), np.float32)
    for row_number, couple in enumerate(edge_links):
        node_rows[row_number, couple[0]] = -1.0
        node_rows[row_number, couple[1]] = 1.0
    curl_rows = np.zeros((len(cycles), 20), np.float32)
    for row_number, cycle_nodes in enumerate(cycles):
        for position in range(len(cycle_nodes)):
            anchor = cycle_nodes[position]
            target = cycle_nodes[(position + 1) % len(cycle_nodes)]
            for number, couple in enumerate(edge_links):
                if couple == (anchor, target):
                    curl_rows[row_number, number] += 1.0
                if couple == (target, anchor):
                    curl_rows[row_number, number] -= 1.0
    return (curl_rows, node_rows)


def operator_draw(key, salt, rows, size, norm, ramped):
    count = rows.shape[0]
    subkeys = jax.random.split(jax.random.fold_in(key, salt), 3)
    weights = jnp.exp(jax.random.uniform(subkeys[0], (count, TOTAL_EL), jnp.float32, 0.0, math.log(10.0)))
    scale = jnp.exp(jax.random.uniform(subkeys[2], (TOTAL_EL,), jnp.float32, 0.0, math.log(10.0)))
    matrix = jnp.zeros((size, size, TOTAL_EL), jnp.float32)
    for row_number in range(count):
        outer_table = np.outer(rows[row_number], rows[row_number]).astype(np.float32)
        matrix = matrix + jnp.asarray(outer_table)[:, :, None] * weights[row_number][None, None, :]
    unit = jnp.eye(size, dtype=jnp.float32)[:, :, None]
    lift = jax.random.uniform(subkeys[1], (size, 1, TOTAL_EL), jnp.float32, 0.3, 0.6)
    matrix = matrix + unit * lift
    if ramped:
        scale = scale * device_scale(TOTAL_EL // EL, EL)
    return matrix * (scale / norm)[None, None, :]


def definite_draw(key, salt, size, lower, upper, ramped):
    subkeys = jax.random.split(jax.random.fold_in(key, salt), 3)
    raw = jax.random.uniform(subkeys[0], (size, size, TOTAL_EL), jnp.float32, -1.0, 1.0)
    scale = jnp.exp(jax.random.uniform(subkeys[2], (TOTAL_EL,), jnp.float32, math.log(lower), math.log(upper)))
    mirror = 0.5 * (raw + jnp.swapaxes(raw, 0, 1))
    unit = jnp.eye(size, dtype=jnp.float32)[:, :, None]
    lift = jax.random.uniform(subkeys[1], (size, 1, TOTAL_EL), jnp.float32, 1.1, 1.4)
    matrix = mirror * (1.0 - unit) + unit * lift * (size - 1)
    if ramped:
        scale = scale * device_scale(TOTAL_EL // EL, EL)
    return matrix * (scale / (8.0 * size))[None, None, :]


def shuffled_lists(key, salt, count, length):
    subkeys = jax.random.split(jax.random.fold_in(key, salt), count)

    def shuffle_single(single):
        return jax.random.permutation(single, length)
    return jax.vmap(shuffle_single)(subkeys)


def connect_draw(key, salt, width, length):
    devices = TOTAL_EL // EL
    shuffled = shuffled_lists(key, salt, devices, length)
    picks = shuffled[:, jnp.arange(EL * width) % length]
    return picks.reshape(devices, EL, width).transpose(2, 0, 1).reshape(width, TOTAL_EL).astype(jnp.int32)


def fresh_connect_draw(key, salt, width, length):
    devices = TOTAL_EL // EL
    rounds = (EL * width + length - 1) // length
    shuffled = shuffled_lists(key, salt, devices * rounds, length).reshape(devices, rounds * length)
    picks = shuffled[:, :EL * width]
    return picks.reshape(devices, EL, width).transpose(2, 0, 1).reshape(width, TOTAL_EL).astype(jnp.int32)


def sends_draw(key, salt, owned, ghosts):
    devices = TOTAL_EL // EL
    shuffled = shuffled_lists(key, salt, 6 * devices, owned)
    return shuffled[:, :ghosts].reshape(6, devices * ghosts).astype(jnp.int32)


def draw_x_block(key, part):
    return block_draw(key, 11)


def draw_p_block(key, part):
    return block_draw(key, 12)


def draw_stiff_elem(key, part):
    curl_rows, node_rows = local_tables()
    return operator_draw(key, 13, curl_rows, EDOF, 50.0, True)


def draw_mass_elem(key, part):
    return definite_draw(key, 14, EDOF, 1.0, 4.0, False)


def draw_node_elem(key, part):
    curl_rows, node_rows = local_tables()
    return operator_draw(key, 15, node_rows, NDOF, 100.0, False)


def draw_elem_edge(key, part):
    return fresh_connect_draw(key, 21, EDOF, NEDGE + 6 * GE)


def draw_elem_node(key, part):
    return connect_draw(key, 22, NDOF, NNODE + 6 * GN)


def draw_send_edge(key, part):
    return sends_draw(key, 23, NEDGE, GE)


def draw_send_node(key, part):
    return sends_draw(key, 24, NNODE, GN)


def draw_grad_pairs(key, part):
    devices = TOTAL_EL // EL
    length = NNODE + 6 * GN
    shuffled = shuffled_lists(key, 25, devices, length)
    offsets = jax.random.randint(jax.random.fold_in(key, 26), (devices, 1), 1, length)
    position = jnp.arange(NEDGE) % length
    tails = shuffled[:, position]
    heads = jnp.take_along_axis(shuffled, (position[None, :] + offsets) % length, axis=1)
    return jnp.stack([tails.reshape(-1), heads.reshape(-1)]).astype(jnp.int32)


def setup_inputs(seed: int = 0) -> dict:
    key_of = jax.random.split(jax.random.key(seed), 11)
    x_block = draw_x_block(jax.random.fold_in(key_of[10], 71), 0)
    p_block = draw_p_block(jax.random.fold_in(key_of[10], 71), 0)
    stiff_elem = draw_stiff_elem(jax.random.fold_in(key_of[10], 71), 0)
    mass_elem = draw_mass_elem(jax.random.fold_in(key_of[10], 71), 0)
    node_elem = draw_node_elem(jax.random.fold_in(key_of[10], 71), 0)
    elem_edge = draw_elem_edge(jax.random.fold_in(key_of[10], 71), 0)
    elem_node = draw_elem_node(jax.random.fold_in(key_of[10], 71), 0)
    send_edge = draw_send_edge(jax.random.fold_in(key_of[10], 71), 0)
    send_node = draw_send_node(jax.random.fold_in(key_of[10], 71), 0)
    grad_pairs = draw_grad_pairs(jax.random.fold_in(key_of[10], 71), 0)
    return {"x_block": x_block, "p_block": p_block, "stiff_elem": stiff_elem, "mass_elem": mass_elem, "node_elem": node_elem, "elem_edge": elem_edge, "elem_node": elem_node, "send_edge": send_edge, "send_node": send_node, "grad_pairs": grad_pairs}


highest = lax.Precision.HIGHEST
OFFSETS = (1, -1, 4, -4, 16, -16)
interval_low = 0.3
interval_high = 1.7
jacobi_weight = 0.7


def ghost_map(send_list, owned, ghosts):
    device_ids = jnp.arange(DOMAINS, dtype=jnp.int32)
    pieces = [device_ids[:, None] * owned + jnp.arange(owned, dtype=jnp.int32)[None, :]]
    shared = send_list.reshape(6, DOMAINS, ghosts)
    for direction in range(6):
        source = (device_ids - OFFSETS[direction]) % DOMAINS
        pieces.append(source[:, None] * owned + shared[direction][source])
    return jnp.concatenate(pieces, axis=1).astype(jnp.int32)


def element_apply(matrices, connect, mapping, vectors):
    def one_device(index, total):
        start = (index * EL).astype(jnp.int32)
        matrix = lax.dynamic_slice_in_dim(matrices, start, EL, 2)
        links = lax.dynamic_slice_in_dim(connect, start, EL, 1)
        columns = mapping[index][links]
        values = vectors[:, columns]
        terms = jnp.einsum("jke,cke->cje", matrix, values, precision=highest)
        return total.at[:, columns].add(terms)

    return lax.fori_loop(0, DOMAINS, one_device, jnp.zeros_like(vectors))


def assemble_diag(matrices, connect, mapping, length):
    def one_device(index, total):
        start = (index * EL).astype(jnp.int32)
        matrix = lax.dynamic_slice_in_dim(matrices, start, EL, 2)
        links = lax.dynamic_slice_in_dim(connect, start, EL, 1)
        columns = mapping[index][links]
        diagonal = jnp.einsum("jje->je", matrix)
        return total.at[columns].add(diagonal)

    return lax.fori_loop(0, DOMAINS, one_device, jnp.zeros((length,), jnp.float32))


def reference(x_block, p_block, stiff_elem, mass_elem, node_elem, elem_edge, elem_node, send_edge, send_node, grad_pairs):
    edge_map = ghost_map(send_edge, NEDGE, GE)
    node_map = ghost_map(send_node, NNODE, GN)
    stiff_x = element_apply(stiff_elem, elem_edge, edge_map, x_block)
    mass_x = element_apply(mass_elem, elem_edge, edge_map, x_block)
    quotient = jnp.sum(x_block * stiff_x, axis=1) / jnp.sum(x_block * mass_x, axis=1)
    residual = stiff_x - quotient[:, None] * mass_x
    edge_diag = assemble_diag(stiff_elem, elem_edge, edge_map, TOTAL_EDGE)
    node_diag = assemble_diag(node_elem, elem_node, node_map, TOTAL_NODE)
    center = 0.5 * (interval_high + interval_low)
    spread = 0.5 * (interval_high - interval_low)
    sigma = center / spread
    rho_now = 1.0 / sigma
    step_dir = residual / (center * edge_diag)
    smooth = step_dir
    for turn in range(CHEB_DEG - 1):
        rho_next = 1.0 / (2.0 * sigma - rho_now)
        remain = residual - element_apply(stiff_elem, elem_edge, edge_map, smooth)
        step_dir = rho_next * rho_now * step_dir + (2.0 * rho_next / spread) * remain / edge_diag
        smooth = smooth + step_dir
        rho_now = rho_next
    after = residual - element_apply(stiff_elem, elem_edge, edge_map, smooth)
    edge_owner = jnp.arange(TOTAL_EDGE, dtype=jnp.int32) // NEDGE
    tails = node_map[edge_owner, grad_pairs[0]]
    heads = node_map[edge_owner, grad_pairs[1]]
    nodal_res = jnp.zeros((MODES, TOTAL_NODE), jnp.float32).at[:, heads].add(after).at[:, tails].add(-after)
    first = jacobi_weight * nodal_res / node_diag
    second = first + jacobi_weight * (nodal_res - element_apply(node_elem, elem_node, node_map, first)) / node_diag
    w_block = smooth + second[:, heads] - second[:, tails]
    basis = jnp.concatenate([x_block, w_block, p_block], axis=0)
    stiff_basis = element_apply(stiff_elem, elem_edge, edge_map, basis)
    mass_basis = element_apply(mass_elem, elem_edge, edge_map, basis)
    gram_stiff = jnp.einsum("cn,dn->cd", basis, stiff_basis, precision=highest) / TOTAL_EDGE
    gram_mass = jnp.einsum("cn,dn->cd", basis, mass_basis, precision=highest) / TOTAL_EDGE
    return w_block, gram_stiff, gram_mass
```

```python
import jax
import jax.numpy as jnp
from jax import lax
from jax.sharding import PartitionSpec as P

CHEB_DEG = 3
NNODE = 384
LANES = 128


highest = lax.Precision.HIGHEST
OFFSETS = (1, -1, 4, -4, 16, -16)
interval_low = 0.3
interval_high = 1.7
jacobi_weight = 0.7


def from_behind(shard, axis, by):
    length = lax.axis_size(axis)
    return lax.ppermute(shard, axis, [(i, (i + by) % length) for i in range(length)])


def index_table(index, length):
    groups = -(-length // LANES)
    lo = index % LANES
    hi = index // LANES
    lo_hot = (lo[:, None] == jnp.arange(LANES, dtype=jnp.int32)[None, :]).astype(jnp.float32)
    hi_mask = (hi[None, :] == jnp.arange(groups, dtype=jnp.int32)[:, None]).astype(jnp.float32)
    return lo_hot, hi_mask, length


def gather_cols(values, table):
    lo_hot, hi_mask, length = table
    groups = hi_mask.shape[0]
    rows = values.shape[0]
    padded = jnp.pad(values, ((0, 0), (0, groups * LANES - length)))
    split = padded.reshape(rows, groups, LANES)
    picked = jnp.einsum("rab,nb->ran", split, lo_hot, precision=highest)
    return jnp.sum(picked * hi_mask[None], axis=1)


def scatter_cols(terms, table):
    lo_hot, hi_mask, length = table
    groups = hi_mask.shape[0]
    rows = terms.shape[0]
    spread = terms[:, None, :] * hi_mask[None]
    summed = jnp.einsum("ran,nb->rab", spread, lo_hot, precision=highest)
    return summed.reshape(rows, groups * LANES)[:, :length]


def extend(values, send_table):
    outgoing = gather_cols(values, send_table)
    ghosts = outgoing.shape[1] // 6
    pieces = [values]
    for direction in range(6):
        piece = outgoing[:, direction * ghosts : (direction + 1) * ghosts]
        pieces.append(from_behind(piece, "dom", OFFSETS[direction]))
    return jnp.concatenate(pieces, axis=1)


def give_back(extended, send_table):
    owned = send_table[2]
    ghosts = (extended.shape[1] - owned) // 6
    backs = []
    for direction in range(6):
        start = owned + direction * ghosts
        backs.append(from_behind(extended[:, start : start + ghosts], "dom", -OFFSETS[direction]))
    return extended[:, :owned] + scatter_cols(jnp.concatenate(backs, axis=1), send_table)


def element_terms(matrices, values):
    return jnp.sum(matrices[None, :, :, :] * values[:, None, :, :], axis=2)


def inner_elements(left, right):
    return jnp.einsum("cke,dke->cd", left, right, precision=highest)


def arrange(pair_part, row_part, modes):
    mode_mode = pair_part[:, :modes, :modes]
    mode_prev = pair_part[:, :modes, modes:]
    prev_mode = pair_part[:, modes:, :modes]
    prev_prev = pair_part[:, modes:, modes:]
    new_mode = jnp.swapaxes(row_part[:, :, :modes], 1, 2)
    new_prev = jnp.swapaxes(row_part[:, :, 2 * modes :], 1, 2)
    upper = jnp.concatenate([mode_mode, new_mode, mode_prev], axis=2)
    lower = jnp.concatenate([prev_mode, new_prev, prev_prev], axis=2)
    return jnp.concatenate([upper, row_part, lower], axis=1)


def shards(
    x_block,
    p_block,
    stiff_elem,
    mass_elem,
    node_elem,
    elem_edge,
    elem_node,
    send_edge,
    send_node,
    grad_pairs,
):
    modes = x_block.shape[0]
    owned_edges = x_block.shape[1]
    edofs, elements = elem_edge.shape
    ndofs = elem_node.shape[0]
    edge_length = owned_edges + 6 * send_edge.shape[1]
    node_length = NNODE + 6 * send_node.shape[1]

    edge_table = index_table(elem_edge.reshape(-1), edge_length)
    node_table = index_table(elem_node.reshape(-1), node_length)
    send_edge_table = index_table(send_edge.reshape(-1), owned_edges)
    send_node_table = index_table(send_node.reshape(-1), NNODE)
    tails = grad_pairs[0]
    heads = grad_pairs[1]
    grad_table = index_table(jnp.concatenate([heads, tails]), node_length)

    def edge_values(extended):
        return gather_cols(extended, edge_table).reshape(extended.shape[0], edofs, elements)

    def edge_sum(terms):
        return scatter_cols(terms.reshape(terms.shape[0], -1), edge_table)

    pair = jnp.concatenate([x_block, p_block], axis=0)
    pair_values = edge_values(extend(pair, send_edge_table))
    stiff_pair = element_terms(stiff_elem, pair_values)
    mass_pair = element_terms(mass_elem, pair_values)
    edge_diag_terms = jnp.einsum("jje->je", stiff_elem)[None]
    images = give_back(
        edge_sum(jnp.concatenate([stiff_pair[:modes], mass_pair[:modes], edge_diag_terms], axis=0)),
        send_edge_table,
    )
    stiff_x = images[:modes]
    mass_x = images[modes : 2 * modes]
    edge_diag = images[2 * modes]
    node_diag_terms = jnp.einsum("jje->je", node_elem).reshape(1, -1)
    node_diag = give_back(scatter_cols(node_diag_terms, node_table), send_node_table)[0]
    numerator, denominator = lax.psum(
        (jnp.sum(x_block * stiff_x, axis=1), jnp.sum(x_block * mass_x, axis=1)), "dom"
    )
    quotient = numerator / denominator
    residual = stiff_x - quotient[:, None] * mass_x

    def stiff_image(vectors):
        values = edge_values(extend(vectors, send_edge_table))
        return give_back(edge_sum(element_terms(stiff_elem, values)), send_edge_table)

    center = 0.5 * (interval_high + interval_low)
    spread = 0.5 * (interval_high - interval_low)
    sigma = center / spread
    rho_now = 1.0 / sigma
    step_dir = residual / (center * edge_diag)
    smooth = step_dir
    for turn in range(CHEB_DEG - 1):
        rho_next = 1.0 / (2.0 * sigma - rho_now)
        remain = residual - stiff_image(smooth)
        step_dir = rho_next * rho_now * step_dir + 2.0 * rho_next / spread * remain / edge_diag
        smooth = smooth + step_dir
        rho_now = rho_next
    after = residual - stiff_image(smooth)
    gathered_res = scatter_cols(jnp.concatenate([after, -after], axis=1), grad_table)
    nodal_res = give_back(gathered_res, send_node_table)
    first = jacobi_weight * nodal_res / node_diag
    first_values = gather_cols(extend(first, send_node_table), node_table).reshape(modes, ndofs, elements)
    node_image = give_back(
        scatter_cols(element_terms(node_elem, first_values).reshape(modes, -1), node_table),
        send_node_table,
    )
    second = first + jacobi_weight * (nodal_res - node_image) / node_diag
    ends = gather_cols(extend(second, send_node_table), grad_table)
    w_block = smooth + ends[:, :owned_edges] - ends[:, owned_edges:]
    w_values = edge_values(extend(w_block, send_edge_table))
    stiff_wterm = element_terms(stiff_elem, w_values)
    mass_wterm = element_terms(mass_elem, w_values)
    basis_values = jnp.concatenate([pair_values[:modes], w_values, pair_values[modes:]], axis=0)
    w_rows = jnp.stack(
        [inner_elements(stiff_wterm, basis_values), inner_elements(mass_wterm, basis_values)]
    )
    stiff_part = inner_elements(pair_values, stiff_pair)
    mass_part = inner_elements(pair_values, mass_pair)
    full_gram = lax.psum(arrange(jnp.stack([stiff_part, mass_part]), w_rows, modes), "dom")
    total_edges = owned_edges * lax.axis_size("dom")
    return (w_block, full_gram[0] / total_edges, full_gram[1] / total_edges)


def solution(mesh):
    in_specs = (
        P(None, "dom"),
        P(None, "dom"),
        P(None, None, "dom"),
        P(None, None, "dom"),
        P(None, None, "dom"),
        P(None, "dom"),
        P(None, "dom"),
        P(None, "dom"),
        P(None, "dom"),
        P(None, "dom"),
    )
    out_specs = (P(None, "dom"), P(), P())
    return jax.shard_map(shards, mesh=mesh, in_specs=in_specs, out_specs=out_specs, check_vma=False)
```

```python
import jax
import jax.numpy as jnp
from jax import lax
from jax.sharding import PartitionSpec as P

CHEB_DEG = 3
NNODE = 384
LANES = 128


highest = lax.Precision.HIGHEST
OFFSETS = (1, -1, 4, -4, 16, -16)
interval_low = 0.3
interval_high = 1.7
jacobi_weight = 0.7


def from_behind(shard, axis, by):
    length = lax.axis_size(axis)
    return lax.ppermute(shard, axis, [(i, (i + by) % length) for i in range(length)])


def shift_pieces(pieces, offsets):
    length = lax.axis_size("dom")
    out = [None] * len(pieces)
    targets = {}
    for number, offset in enumerate(offsets):
        targets.setdefault(offset % length, []).append(number)
    for offset, numbers in targets.items():
        sizes = [pieces[number].shape[1] for number in numbers]
        moved = from_behind(jnp.concatenate([pieces[number] for number in numbers], axis=1), "dom", offset)
        start = 0
        for number, size in zip(numbers, sizes):
            out[number] = moved[:, start : start + size]
            start += size
    return out


def all_sum(value):
    length = lax.axis_size("dom")
    if length & (length - 1):
        return lax.psum(value, "dom")
    stride = 1
    while stride < length:
        value = value + lax.ppermute(value, "dom", [(i, i ^ stride) for i in range(length)])
        stride *= 2
    return value


def index_table(index, length):
    groups = -(-length // LANES)
    lo = index % LANES
    hi = index // LANES
    lo_hot = (lo[:, None] == jnp.arange(LANES, dtype=jnp.int32)[None, :]).astype(jnp.float32)
    hi_mask = (hi[None, :] == jnp.arange(groups, dtype=jnp.int32)[:, None]).astype(jnp.float32)
    return lo_hot, hi_mask, length


def gather_cols(values, table):
    lo_hot, hi_mask, length = table
    groups = hi_mask.shape[0]
    rows = values.shape[0]
    padded = jnp.pad(values, ((0, 0), (0, groups * LANES - length)))
    split = padded.reshape(rows, groups, LANES)
    picked = jnp.einsum("rab,nb->ran", split, lo_hot, precision=highest)
    return jnp.sum(picked * hi_mask[None], axis=1)


def scatter_cols(terms, table):
    lo_hot, hi_mask, length = table
    groups = hi_mask.shape[0]
    rows = terms.shape[0]
    spread = terms[:, None, :] * hi_mask[None]
    summed = jnp.einsum("ran,nb->rab", spread, lo_hot, precision=highest)
    return summed.reshape(rows, groups * LANES)[:, :length]


def extend(values, send_table):
    outgoing = gather_cols(values, send_table)
    ghosts = outgoing.shape[1] // 6
    pieces = [outgoing[:, direction * ghosts : (direction + 1) * ghosts] for direction in range(6)]
    return jnp.concatenate([values] + shift_pieces(pieces, OFFSETS), axis=1)


def give_back(extended, send_table):
    owned = send_table[2]
    ghosts = (extended.shape[1] - owned) // 6
    pieces = [extended[:, owned + d * ghosts : owned + (d + 1) * ghosts] for d in range(6)]
    backs = shift_pieces(pieces, [-offset for offset in OFFSETS])
    return extended[:, :owned] + scatter_cols(jnp.concatenate(backs, axis=1), send_table)


def element_terms(matrices, values):
    return jnp.sum(matrices[None, :, :, :] * values[:, None, :, :], axis=2)


def inner_elements(left, right):
    return jnp.einsum("cke,dke->cd", left, right, precision=highest)


def arrange(pair_part, row_part, modes):
    mode_mode = pair_part[:, :modes, :modes]
    mode_prev = pair_part[:, :modes, modes:]
    prev_mode = pair_part[:, modes:, :modes]
    prev_prev = pair_part[:, modes:, modes:]
    new_mode = jnp.swapaxes(row_part[:, :, :modes], 1, 2)
    new_prev = jnp.swapaxes(row_part[:, :, 2 * modes :], 1, 2)
    upper = jnp.concatenate([mode_mode, new_mode, mode_prev], axis=2)
    lower = jnp.concatenate([prev_mode, new_prev, prev_prev], axis=2)
    return jnp.concatenate([upper, row_part, lower], axis=1)


def shards(
    x_block,
    p_block,
    stiff_elem,
    mass_elem,
    node_elem,
    elem_edge,
    elem_node,
    send_edge,
    send_node,
    grad_pairs,
):
    modes = x_block.shape[0]
    owned_edges = x_block.shape[1]
    edofs, elements = elem_edge.shape
    ndofs = elem_node.shape[0]
    edge_length = owned_edges + 6 * send_edge.shape[1]
    node_length = NNODE + 6 * send_node.shape[1]

    edge_table = index_table(elem_edge.reshape(-1), edge_length)
    node_table = index_table(elem_node.reshape(-1), node_length)
    send_edge_table = index_table(send_edge.reshape(-1), owned_edges)
    send_node_table = index_table(send_node.reshape(-1), NNODE)
    tails = grad_pairs[0]
    heads = grad_pairs[1]
    grad_table = index_table(jnp.concatenate([heads, tails]), node_length)

    def edge_values(extended):
        return gather_cols(extended, edge_table).reshape(extended.shape[0], edofs, elements)

    def edge_sum(terms):
        return scatter_cols(terms.reshape(terms.shape[0], -1), edge_table)

    pair = jnp.concatenate([x_block, p_block], axis=0)
    pair_values = edge_values(extend(pair, send_edge_table))
    stiff_pair = element_terms(stiff_elem, pair_values)
    mass_pair = element_terms(mass_elem, pair_values)
    edge_diag_terms = jnp.einsum("jje->je", stiff_elem)[None]
    images = give_back(
        edge_sum(jnp.concatenate([stiff_pair[:modes], mass_pair[:modes], edge_diag_terms], axis=0)),
        send_edge_table,
    )
    stiff_x = images[:modes]
    mass_x = images[modes : 2 * modes]
    edge_diag = images[2 * modes]
    node_diag_terms = jnp.einsum("jje->je", node_elem).reshape(1, -1)
    node_diag = give_back(scatter_cols(node_diag_terms, node_table), send_node_table)[0]
    numerator, denominator = all_sum(
        jnp.stack([jnp.sum(x_block * stiff_x, axis=1), jnp.sum(x_block * mass_x, axis=1)])
    )
    quotient = numerator / denominator
    residual = stiff_x - quotient[:, None] * mass_x

    def stiff_image(vectors):
        values = edge_values(extend(vectors, send_edge_table))
        return give_back(edge_sum(element_terms(stiff_elem, values)), send_edge_table)

    center = 0.5 * (interval_high + interval_low)
    spread = 0.5 * (interval_high - interval_low)
    sigma = center / spread
    rho_now = 1.0 / sigma
    step_dir = residual / (center * edge_diag)
    smooth = step_dir
    for turn in range(CHEB_DEG - 1):
        rho_next = 1.0 / (2.0 * sigma - rho_now)
        remain = residual - stiff_image(smooth)
        step_dir = rho_next * rho_now * step_dir + 2.0 * rho_next / spread * remain / edge_diag
        smooth = smooth + step_dir
        rho_now = rho_next
    after = residual - stiff_image(smooth)
    gathered_res = scatter_cols(jnp.concatenate([after, -after], axis=1), grad_table)
    nodal_res = give_back(gathered_res, send_node_table)
    first = jacobi_weight * nodal_res / node_diag
    first_values = gather_cols(extend(first, send_node_table), node_table).reshape(modes, ndofs, elements)
    node_image = give_back(
        scatter_cols(element_terms(node_elem, first_values).reshape(modes, -1), node_table),
        send_node_table,
    )
    second = first + jacobi_weight * (nodal_res - node_image) / node_diag
    ends = gather_cols(extend(second, send_node_table), grad_table)
    w_block = smooth + ends[:, :owned_edges] - ends[:, owned_edges:]
    w_values = edge_values(extend(w_block, send_edge_table))
    stiff_wterm = element_terms(stiff_elem, w_values)
    mass_wterm = element_terms(mass_elem, w_values)
    basis_values = jnp.concatenate([pair_values[:modes], w_values, pair_values[modes:]], axis=0)
    w_rows = jnp.stack(
        [inner_elements(stiff_wterm, basis_values), inner_elements(mass_wterm, basis_values)]
    )
    stiff_part = inner_elements(pair_values, stiff_pair)
    mass_part = inner_elements(pair_values, mass_pair)
    full_gram = all_sum(arrange(jnp.stack([stiff_part, mass_part]), w_rows, modes))
    total_edges = owned_edges * lax.axis_size("dom")
    return (w_block, full_gram[0] / total_edges, full_gram[1] / total_edges)


def solution(mesh):
    in_specs = (
        P(None, "dom"),
        P(None, "dom"),
        P(None, None, "dom"),
        P(None, None, "dom"),
        P(None, None, "dom"),
        P(None, "dom"),
        P(None, "dom"),
        P(None, "dom"),
        P(None, "dom"),
        P(None, "dom"),
    )
    out_specs = (P(None, "dom"), P(), P())
    return jax.shard_map(shards, mesh=mesh, in_specs=in_specs, out_specs=out_specs, check_vma=False)
```

```python
import jax
import jax.numpy as jnp
from jax import lax
from jax.sharding import PartitionSpec as P

CHEB_DEG = 3
NNODE = 384
LANES = 128


highest = lax.Precision.HIGHEST
OFFSETS = (1, -1, 4, -4, 16, -16)
interval_low = 0.3
interval_high = 1.7
jacobi_weight = 0.7


def from_behind(shard, axis, by):
    length = lax.axis_size(axis)
    return lax.ppermute(shard, axis, [(i, (i + by) % length) for i in range(length)])


def shift_pieces(pieces, offsets):
    length = lax.axis_size("dom")
    out = [None] * len(pieces)
    targets = {}
    for number, offset in enumerate(offsets):
        targets.setdefault(offset % length, []).append(number)
    for offset, numbers in targets.items():
        sizes = [pieces[number].shape[1] for number in numbers]
        moved = from_behind(jnp.concatenate([pieces[number] for number in numbers], axis=1), "dom", offset)
        start = 0
        for number, size in zip(numbers, sizes):
            out[number] = moved[:, start : start + size]
            start += size
    return out


def all_sum(value):
    length = lax.axis_size("dom")
    if length & (length - 1):
        return lax.psum(value, "dom")
    stride = 1
    while stride < length:
        value = value + lax.ppermute(value, "dom", [(i, i ^ stride) for i in range(length)])
        stride *= 2
    return value


def index_table(index, length):
    groups = -(-length // LANES)
    lo = index % LANES
    hi = index // LANES
    lo_hot = (lo[:, None] == jnp.arange(LANES, dtype=jnp.int32)[None, :]).astype(jnp.bfloat16)
    hi_mask = (hi[None, :] == jnp.arange(groups, dtype=jnp.int32)[:, None]).astype(jnp.float32)
    return lo_hot, hi_mask, length


def three_parts(values):
    first = lax.reduce_precision(values, exponent_bits=8, mantissa_bits=7)
    rest = values - first
    second = lax.reduce_precision(rest, exponent_bits=8, mantissa_bits=7)
    third = rest - second
    return jnp.concatenate([first, second, third], axis=0).astype(jnp.bfloat16)


def gather_cols(values, table):
    lo_hot, hi_mask, length = table
    groups = hi_mask.shape[0]
    rows = values.shape[0]
    padded = jnp.pad(values, ((0, 0), (0, groups * LANES - length)))
    split = three_parts(padded).reshape(3 * rows, groups, LANES)
    picked = jnp.einsum("rab,nb->ran", split, lo_hot, preferred_element_type=jnp.float32)
    picked = picked.reshape(3, rows, groups, -1)
    return jnp.sum(picked * hi_mask[None, None], axis=(0, 2))


def scatter_cols(terms, table):
    lo_hot, hi_mask, length = table
    groups = hi_mask.shape[0]
    rows = terms.shape[0]
    spread = three_parts(terms[:, None, :] * hi_mask[None])
    summed = jnp.einsum("ran,nb->rab", spread, lo_hot, preferred_element_type=jnp.float32)
    summed = jnp.sum(summed.reshape(3, rows, groups, LANES), axis=0)
    return summed.reshape(rows, groups * LANES)[:, :length]


def extend_pieces(values, send_table):
    outgoing = gather_cols(values, send_table)
    ghosts = outgoing.shape[1] // 6
    return [outgoing[:, d * ghosts : (d + 1) * ghosts] for d in range(6)], list(OFFSETS)


def extend_finish(values, moved):
    return jnp.concatenate([values] + moved, axis=1)


def give_back_pieces(extended, send_table):
    owned = send_table[2]
    ghosts = (extended.shape[1] - owned) // 6
    pieces = [extended[:, owned + d * ghosts : owned + (d + 1) * ghosts] for d in range(6)]
    return pieces, [-offset for offset in OFFSETS]


def give_back_finish(extended, moved, send_table):
    owned = send_table[2]
    return extended[:, :owned] + scatter_cols(jnp.concatenate(moved, axis=1), send_table)


def exchange(*groups):
    pieces, offsets, bounds = [], [], []
    for group_pieces, group_offsets in groups:
        bounds.append((len(pieces), len(group_pieces)))
        pieces += [piece.reshape(1, -1) for piece in group_pieces]
        offsets += group_offsets
    moved = shift_pieces(pieces, offsets)
    out = []
    for (start, count), (group_pieces, _) in zip(bounds, groups):
        out.append([m.reshape(p.shape) for m, p in zip(moved[start : start + count], group_pieces)])
    return out


def extend(values, send_table):
    (moved,) = exchange(extend_pieces(values, send_table))
    return extend_finish(values, moved)


def give_back(extended, send_table):
    (moved,) = exchange(give_back_pieces(extended, send_table))
    return give_back_finish(extended, moved, send_table)


def element_terms(matrices, values):
    return jnp.sum(matrices[None, :, :, :] * values[:, None, :, :], axis=2)


def inner_elements(left, right):
    return jnp.einsum("cke,dke->cd", left, right, precision=highest)


def arrange(pair_part, row_part, modes):
    mode_mode = pair_part[:, :modes, :modes]
    mode_prev = pair_part[:, :modes, modes:]
    prev_mode = pair_part[:, modes:, :modes]
    prev_prev = pair_part[:, modes:, modes:]
    new_mode = jnp.swapaxes(row_part[:, :, :modes], 1, 2)
    new_prev = jnp.swapaxes(row_part[:, :, 2 * modes :], 1, 2)
    upper = jnp.concatenate([mode_mode, new_mode, mode_prev], axis=2)
    lower = jnp.concatenate([prev_mode, new_prev, prev_prev], axis=2)
    return jnp.concatenate([upper, row_part, lower], axis=1)


def shards(
    x_block,
    p_block,
    stiff_elem,
    mass_elem,
    node_elem,
    elem_edge,
    elem_node,
    send_edge,
    send_node,
    grad_pairs,
):
    modes = x_block.shape[0]
    owned_edges = x_block.shape[1]
    edofs, elements = elem_edge.shape
    ndofs = elem_node.shape[0]
    edge_length = owned_edges + 6 * send_edge.shape[1]
    node_length = NNODE + 6 * send_node.shape[1]

    edge_table = index_table(elem_edge.reshape(-1), edge_length)
    node_table = index_table(elem_node.reshape(-1), node_length)
    send_edge_table = index_table(send_edge.reshape(-1), owned_edges)
    send_node_table = index_table(send_node.reshape(-1), NNODE)
    tails = grad_pairs[0]
    heads = grad_pairs[1]
    grad_table = index_table(jnp.concatenate([heads, tails]), node_length)

    def edge_values(extended):
        return gather_cols(extended, edge_table).reshape(extended.shape[0], edofs, elements)

    def edge_sum(terms):
        return scatter_cols(terms.reshape(terms.shape[0], -1), edge_table)

    pair = jnp.concatenate([x_block, p_block], axis=0)
    node_diag_local = scatter_cols(jnp.einsum("jje->je", node_elem).reshape(1, -1), node_table)
    pair_moved, node_diag_moved = exchange(
        extend_pieces(pair, send_edge_table), give_back_pieces(node_diag_local, send_node_table)
    )
    pair_values = edge_values(extend_finish(pair, pair_moved))
    node_diag = give_back_finish(node_diag_local, node_diag_moved, send_node_table)[0]
    stiff_pair = element_terms(stiff_elem, pair_values)
    mass_pair = element_terms(mass_elem, pair_values)
    edge_diag_terms = jnp.einsum("jje->je", stiff_elem)[None]
    images = give_back(
        edge_sum(jnp.concatenate([stiff_pair[:modes], mass_pair[:modes], edge_diag_terms], axis=0)),
        send_edge_table,
    )
    stiff_x = images[:modes]
    mass_x = images[modes : 2 * modes]
    edge_diag = images[2 * modes]
    numerator, denominator = all_sum(
        jnp.stack([jnp.sum(x_block * stiff_x, axis=1), jnp.sum(x_block * mass_x, axis=1)])
    )
    quotient = numerator / denominator
    residual = stiff_x - quotient[:, None] * mass_x

    def stiff_image(vectors):
        values = edge_values(extend(vectors, send_edge_table))
        return give_back(edge_sum(element_terms(stiff_elem, values)), send_edge_table)

    center = 0.5 * (interval_high + interval_low)
    spread = 0.5 * (interval_high - interval_low)
    sigma = center / spread
    rho_now = 1.0 / sigma
    step_dir = residual / (center * edge_diag)
    smooth = step_dir
    for turn in range(CHEB_DEG - 1):
        rho_next = 1.0 / (2.0 * sigma - rho_now)
        remain = residual - stiff_image(smooth)
        step_dir = rho_next * rho_now * step_dir + 2.0 * rho_next / spread * remain / edge_diag
        smooth = smooth + step_dir
        rho_now = rho_next
    after = residual - stiff_image(smooth)
    gathered_res = scatter_cols(jnp.concatenate([after, -after], axis=1), grad_table)
    nodal_res = give_back(gathered_res, send_node_table)
    first = jacobi_weight * nodal_res / node_diag
    first_values = gather_cols(extend(first, send_node_table), node_table).reshape(modes, ndofs, elements)
    node_image = give_back(
        scatter_cols(element_terms(node_elem, first_values).reshape(modes, -1), node_table),
        send_node_table,
    )
    second = first + jacobi_weight * (nodal_res - node_image) / node_diag
    ends = gather_cols(extend(second, send_node_table), grad_table)
    w_block = smooth + ends[:, :owned_edges] - ends[:, owned_edges:]
    w_values = edge_values(extend(w_block, send_edge_table))
    stiff_wterm = element_terms(stiff_elem, w_values)
    mass_wterm = element_terms(mass_elem, w_values)
    basis_values = jnp.concatenate([pair_values[:modes], w_values, pair_values[modes:]], axis=0)
    w_rows = jnp.stack(
        [inner_elements(stiff_wterm, basis_values), inner_elements(mass_wterm, basis_values)]
    )
    stiff_part = inner_elements(pair_values, stiff_pair)
    mass_part = inner_elements(pair_values, mass_pair)
    full_gram = all_sum(arrange(jnp.stack([stiff_part, mass_part]), w_rows, modes))
    total_edges = owned_edges * lax.axis_size("dom")
    return (w_block, full_gram[0] / total_edges, full_gram[1] / total_edges)


def solution(mesh):
    in_specs = (
        P(None, "dom"),
        P(None, "dom"),
        P(None, None, "dom"),
        P(None, None, "dom"),
        P(None, None, "dom"),
        P(None, "dom"),
        P(None, "dom"),
        P(None, "dom"),
        P(None, "dom"),
        P(None, "dom"),
    )
    out_specs = (P(None, "dom"), P(), P())
    return jax.shard_map(shards, mesh=mesh, in_specs=in_specs, out_specs=out_specs, check_vma=False)
```

```python
import jax
import jax.numpy as jnp
from jax import lax
from jax.sharding import PartitionSpec as P

CHEB_DEG = 3
NNODE = 384
LANES = 128


highest = lax.Precision.HIGHEST
OFFSETS = (1, -1, 4, -4, 16, -16)
interval_low = 0.3
interval_high = 1.7
jacobi_weight = 0.7


def from_behind(shard, axis, by):
    length = lax.axis_size(axis)
    return lax.ppermute(shard, axis, [(i, (i + by) % length) for i in range(length)])


def shift_pieces(pieces, offsets):
    length = lax.axis_size("dom")
    out = [None] * len(pieces)
    targets = {}
    for number, offset in enumerate(offsets):
        targets.setdefault(offset % length, []).append(number)
    for offset, numbers in targets.items():
        sizes = [pieces[number].shape[1] for number in numbers]
        moved = from_behind(jnp.concatenate([pieces[number] for number in numbers], axis=1), "dom", offset)
        start = 0
        for number, size in zip(numbers, sizes):
            out[number] = moved[:, start : start + size]
            start += size
    return out


def all_sum(value):
    length = lax.axis_size("dom")
    if length & (length - 1):
        return lax.psum(value, "dom")
    stride = 1
    while stride < length:
        value = value + lax.ppermute(value, "dom", [(i, i ^ stride) for i in range(length)])
        stride *= 2
    return value


def index_table(index, length):
    groups = -(-length // LANES)
    lo = index % LANES
    hi = index // LANES
    lo_hot = (lo[:, None] == jnp.arange(LANES, dtype=jnp.int32)[None, :]).astype(jnp.float32)
    hi_mask = (hi[None, :] == jnp.arange(groups, dtype=jnp.int32)[:, None]).astype(jnp.float32)
    return lo_hot, hi_mask, length


def gather_cols(values, table):
    lo_hot, hi_mask, length = table
    groups = hi_mask.shape[0]
    rows = values.shape[0]
    padded = jnp.pad(values, ((0, 0), (0, groups * LANES - length)))
    split = padded.reshape(rows, groups, LANES)
    picked = jnp.einsum("rab,nb->ran", split, lo_hot, precision=highest)
    return jnp.sum(picked * hi_mask[None], axis=1)


def scatter_cols(terms, table):
    lo_hot, hi_mask, length = table
    groups = hi_mask.shape[0]
    rows = terms.shape[0]
    spread = terms[:, None, :] * hi_mask[None]
    summed = jnp.einsum("ran,nb->rab", spread, lo_hot, precision=highest)
    return summed.reshape(rows, groups * LANES)[:, :length]


def extend_pieces(values, send_table):
    outgoing = gather_cols(values, send_table)
    ghosts = outgoing.shape[1] // 6
    return [outgoing[:, d * ghosts : (d + 1) * ghosts] for d in range(6)], list(OFFSETS)


def extend_finish(values, moved):
    return jnp.concatenate([values] + moved, axis=1)


def give_back_pieces(extended, send_table):
    owned = send_table[2]
    ghosts = (extended.shape[1] - owned) // 6
    pieces = [extended[:, owned + d * ghosts : owned + (d + 1) * ghosts] for d in range(6)]
    return pieces, [-offset for offset in OFFSETS]


def give_back_finish(extended, moved, send_table):
    owned = send_table[2]
    return extended[:, :owned] + scatter_cols(jnp.concatenate(moved, axis=1), send_table)


def exchange(*groups):
    pieces, offsets, bounds = [], [], []
    flat = len({piece.shape[0] for group_pieces, _ in groups for piece in group_pieces}) > 1
    for group_pieces, group_offsets in groups:
        bounds.append((len(pieces), len(group_pieces)))
        pieces += [piece.reshape(1, -1) if flat else piece for piece in group_pieces]
        offsets += group_offsets
    moved = shift_pieces(pieces, offsets)
    out = []
    for (start, count), (group_pieces, _) in zip(bounds, groups):
        out.append([m.reshape(p.shape) for m, p in zip(moved[start : start + count], group_pieces)])
    return out


def extend(values, send_table):
    (moved,) = exchange(extend_pieces(values, send_table))
    return extend_finish(values, moved)


def give_back(extended, send_table):
    (moved,) = exchange(give_back_pieces(extended, send_table))
    return give_back_finish(extended, moved, send_table)


def element_terms(matrices, values):
    return jnp.sum(matrices[None, :, :, :] * values[:, None, :, :], axis=2)


def inner_elements(left, right):
    return jnp.einsum("cke,dke->cd", left, right, precision=highest)


def arrange(pair_part, row_part, modes):
    mode_mode = pair_part[:, :modes, :modes]
    mode_prev = pair_part[:, :modes, modes:]
    prev_mode = pair_part[:, modes:, :modes]
    prev_prev = pair_part[:, modes:, modes:]
    new_mode = jnp.swapaxes(row_part[:, :, :modes], 1, 2)
    new_prev = jnp.swapaxes(row_part[:, :, 2 * modes :], 1, 2)
    upper = jnp.concatenate([mode_mode, new_mode, mode_prev], axis=2)
    lower = jnp.concatenate([prev_mode, new_prev, prev_prev], axis=2)
    return jnp.concatenate([upper, row_part, lower], axis=1)


def shards(
    x_block,
    p_block,
    stiff_elem,
    mass_elem,
    node_elem,
    elem_edge,
    elem_node,
    send_edge,
    send_node,
    grad_pairs,
):
    modes = x_block.shape[0]
    owned_edges = x_block.shape[1]
    edofs, elements = elem_edge.shape
    ndofs = elem_node.shape[0]
    edge_length = owned_edges + 6 * send_edge.shape[1]
    node_length = NNODE + 6 * send_node.shape[1]

    edge_table = index_table(elem_edge.reshape(-1), edge_length)
    node_table = index_table(elem_node.reshape(-1), node_length)
    send_edge_table = index_table(send_edge.reshape(-1), owned_edges)
    send_node_table = index_table(send_node.reshape(-1), NNODE)
    tails = grad_pairs[0]
    heads = grad_pairs[1]
    grad_table = index_table(jnp.concatenate([heads, tails]), node_length)

    def edge_values(extended):
        return gather_cols(extended, edge_table).reshape(extended.shape[0], edofs, elements)

    def edge_sum(terms):
        return scatter_cols(terms.reshape(terms.shape[0], -1), edge_table)

    pair = jnp.concatenate([x_block, p_block], axis=0)
    node_diag_local = scatter_cols(jnp.einsum("jje->je", node_elem).reshape(1, -1), node_table)
    pair_moved, node_diag_moved = exchange(
        extend_pieces(pair, send_edge_table), give_back_pieces(node_diag_local, send_node_table)
    )
    pair_values = edge_values(extend_finish(pair, pair_moved))
    node_diag = give_back_finish(node_diag_local, node_diag_moved, send_node_table)[0]
    stiff_pair = element_terms(stiff_elem, pair_values)
    mass_pair = element_terms(mass_elem, pair_values)
    edge_diag_terms = jnp.einsum("jje->je", stiff_elem)[None]
    images = give_back(
        edge_sum(jnp.concatenate([stiff_pair[:modes], mass_pair[:modes], edge_diag_terms], axis=0)),
        send_edge_table,
    )
    stiff_x = images[:modes]
    mass_x = images[modes : 2 * modes]
    edge_diag = images[2 * modes]
    numerator, denominator = all_sum(
        jnp.stack([jnp.sum(x_block * stiff_x, axis=1), jnp.sum(x_block * mass_x, axis=1)])
    )
    quotient = numerator / denominator
    residual = stiff_x - quotient[:, None] * mass_x

    def stiff_image(vectors):
        values = edge_values(extend(vectors, send_edge_table))
        return give_back(edge_sum(element_terms(stiff_elem, values)), send_edge_table)

    center = 0.5 * (interval_high + interval_low)
    spread = 0.5 * (interval_high - interval_low)
    sigma = center / spread
    rho_now = 1.0 / sigma
    step_dir = residual / (center * edge_diag)
    smooth = step_dir
    for turn in range(CHEB_DEG - 1):
        rho_next = 1.0 / (2.0 * sigma - rho_now)
        remain = residual - stiff_image(smooth)
        step_dir = rho_next * rho_now * step_dir + 2.0 * rho_next / spread * remain / edge_diag
        smooth = smooth + step_dir
        rho_now = rho_next
    after = residual - stiff_image(smooth)
    gathered_res = scatter_cols(jnp.concatenate([after, -after], axis=1), grad_table)
    nodal_res = give_back(gathered_res, send_node_table)
    first = jacobi_weight * nodal_res / node_diag
    first_values = gather_cols(extend(first, send_node_table), node_table).reshape(modes, ndofs, elements)
    node_image = give_back(
        scatter_cols(element_terms(node_elem, first_values).reshape(modes, -1), node_table),
        send_node_table,
    )
    second = first + jacobi_weight * (nodal_res - node_image) / node_diag
    ends = gather_cols(extend(second, send_node_table), grad_table)
    w_block = smooth + ends[:, :owned_edges] - ends[:, owned_edges:]
    w_values = edge_values(extend(w_block, send_edge_table))
    stiff_wterm = element_terms(stiff_elem, w_values)
    mass_wterm = element_terms(mass_elem, w_values)
    basis_values = jnp.concatenate([pair_values[:modes], w_values, pair_values[modes:]], axis=0)
    w_rows = jnp.stack(
        [inner_elements(stiff_wterm, basis_values), inner_elements(mass_wterm, basis_values)]
    )
    stiff_part = inner_elements(pair_values, stiff_pair)
    mass_part = inner_elements(pair_values, mass_pair)
    full_gram = all_sum(arrange(jnp.stack([stiff_part, mass_part]), w_rows, modes))
    total_edges = owned_edges * lax.axis_size("dom")
    return (w_block, full_gram[0] / total_edges, full_gram[1] / total_edges)


def solution(mesh):
    in_specs = (
        P(None, "dom"),
        P(None, "dom"),
        P(None, None, "dom"),
        P(None, None, "dom"),
        P(None, None, "dom"),
        P(None, "dom"),
        P(None, "dom"),
        P(None, "dom"),
        P(None, "dom"),
        P(None, "dom"),
    )
    out_specs = (P(None, "dom"), P(), P())
    return jax.shard_map(shards, mesh=mesh, in_specs=in_specs, out_specs=out_specs, check_vma=False)
```

```python
import jax
import jax.numpy as jnp
from jax import lax
from jax.sharding import PartitionSpec as P

CHEB_DEG = 3
NNODE = 384
LANES = 128


highest = lax.Precision.HIGHEST
OFFSETS = (1, -1, 4, -4, 16, -16)
interval_low = 0.3
interval_high = 1.7
jacobi_weight = 0.7


def from_behind(shard, axis, by):
    length = lax.axis_size(axis)
    return lax.ppermute(shard, axis, [(i, (i + by) % length) for i in range(length)])


def shift_pieces(pieces, offsets):
    length = lax.axis_size("dom")
    out = [None] * len(pieces)
    targets = {}
    for number, offset in enumerate(offsets):
        targets.setdefault(offset % length, []).append(number)
    for offset, numbers in targets.items():
        sizes = [pieces[number].shape[1] for number in numbers]
        moved = from_behind(jnp.concatenate([pieces[number] for number in numbers], axis=1), "dom", offset)
        start = 0
        for number, size in zip(numbers, sizes):
            out[number] = moved[:, start : start + size]
            start += size
    return out


def all_sum(value):
    length = lax.axis_size("dom")
    if length & (length - 1):
        return lax.psum(value, "dom")
    stride = 1
    while stride < length:
        value = value + lax.ppermute(value, "dom", [(i, i ^ stride) for i in range(length)])
        stride *= 2
    return value


def index_table(index, length):
    groups = -(-length // LANES)
    lo = index % LANES
    hi = index // LANES
    lo_hot = (lo[:, None] == jnp.arange(LANES, dtype=jnp.int32)[None, :]).astype(jnp.bfloat16)
    hi_mask = (hi[None, :] == jnp.arange(groups, dtype=jnp.int32)[:, None]).astype(jnp.float32)
    return lo_hot, hi_mask, length


def three_parts(values, axis):
    first = lax.reduce_precision(values, exponent_bits=8, mantissa_bits=7)
    rest = values - first
    second = lax.reduce_precision(rest, exponent_bits=8, mantissa_bits=7)
    third = rest - second
    return jnp.concatenate([first, second, third], axis=axis).astype(jnp.bfloat16)


def gather_cols(values, table):
    lo_hot, hi_mask, length = table
    groups = hi_mask.shape[0]
    rows = values.shape[0]
    padded = jnp.pad(values, ((0, 0), (0, groups * LANES - length)))
    split = three_parts(padded.reshape(rows, groups, LANES), 2)
    picked = jnp.einsum(
        "rak,nk->ran", split, jnp.concatenate([lo_hot] * 3, axis=1), preferred_element_type=jnp.float32
    )
    return jnp.sum(picked * hi_mask[None], axis=1)


def scatter_cols(terms, table):
    lo_hot, hi_mask, length = table
    groups = hi_mask.shape[0]
    rows = terms.shape[0]
    spread = three_parts(terms[:, None, :] * hi_mask[None], 2)
    summed = jnp.einsum(
        "ran,nb->rab", spread, jnp.concatenate([lo_hot] * 3, axis=0), preferred_element_type=jnp.float32
    )
    return summed.reshape(rows, groups * LANES)[:, :length]


def extend_pieces(values, send_table):
    outgoing = gather_cols(values, send_table)
    ghosts = outgoing.shape[1] // 6
    return [outgoing[:, d * ghosts : (d + 1) * ghosts] for d in range(6)], list(OFFSETS)


def extend_finish(values, moved):
    return jnp.concatenate([values] + moved, axis=1)


def give_back_pieces(extended, send_table):
    owned = send_table[2]
    ghosts = (extended.shape[1] - owned) // 6
    pieces = [extended[:, owned + d * ghosts : owned + (d + 1) * ghosts] for d in range(6)]
    return pieces, [-offset for offset in OFFSETS]


def give_back_finish(extended, moved, send_table):
    owned = send_table[2]
    return extended[:, :owned] + scatter_cols(jnp.concatenate(moved, axis=1), send_table)


def exchange(*groups):
    pieces, offsets, bounds = [], [], []
    flat = len({piece.shape[0] for group_pieces, _ in groups for piece in group_pieces}) > 1
    for group_pieces, group_offsets in groups:
        bounds.append((len(pieces), len(group_pieces)))
        pieces += [piece.reshape(1, -1) if flat else piece for piece in group_pieces]
        offsets += group_offsets
    moved = shift_pieces(pieces, offsets)
    out = []
    for (start, count), (group_pieces, _) in zip(bounds, groups):
        out.append([m.reshape(p.shape) for m, p in zip(moved[start : start + count], group_pieces)])
    return out


def extend(values, send_table):
    (moved,) = exchange(extend_pieces(values, send_table))
    return extend_finish(values, moved)


def give_back(extended, send_table):
    (moved,) = exchange(give_back_pieces(extended, send_table))
    return give_back_finish(extended, moved, send_table)


def element_terms(matrices, values):
    return jnp.sum(matrices[None, :, :, :] * values[:, None, :, :], axis=2)


def inner_elements(left, right):
    return jnp.einsum("cke,dke->cd", left, right, precision=highest)


def arrange(pair_part, row_part, modes):
    mode_mode = pair_part[:, :modes, :modes]
    mode_prev = pair_part[:, :modes, modes:]
    prev_mode = pair_part[:, modes:, :modes]
    prev_prev = pair_part[:, modes:, modes:]
    new_mode = jnp.swapaxes(row_part[:, :, :modes], 1, 2)
    new_prev = jnp.swapaxes(row_part[:, :, 2 * modes :], 1, 2)
    upper = jnp.concatenate([mode_mode, new_mode, mode_prev], axis=2)
    lower = jnp.concatenate([prev_mode, new_prev, prev_prev], axis=2)
    return jnp.concatenate([upper, row_part, lower], axis=1)


def shards(
    x_block,
    p_block,
    stiff_elem,
    mass_elem,
    node_elem,
    elem_edge,
    elem_node,
    send_edge,
    send_node,
    grad_pairs,
):
    modes = x_block.shape[0]
    owned_edges = x_block.shape[1]
    edofs, elements = elem_edge.shape
    ndofs = elem_node.shape[0]
    edge_length = owned_edges + 6 * send_edge.shape[1]
    node_length = NNODE + 6 * send_node.shape[1]

    edge_table = index_table(elem_edge.reshape(-1), edge_length)
    node_table = index_table(elem_node.reshape(-1), node_length)
    send_edge_table = index_table(send_edge.reshape(-1), owned_edges)
    send_node_table = index_table(send_node.reshape(-1), NNODE)
    tails = grad_pairs[0]
    heads = grad_pairs[1]
    grad_table = index_table(jnp.concatenate([heads, tails]), node_length)

    def edge_values(extended):
        return gather_cols(extended, edge_table).reshape(extended.shape[0], edofs, elements)

    def edge_sum(terms):
        return scatter_cols(terms.reshape(terms.shape[0], -1), edge_table)

    pair = jnp.concatenate([x_block, p_block], axis=0)
    node_diag_local = scatter_cols(jnp.einsum("jje->je", node_elem).reshape(1, -1), node_table)
    pair_moved, node_diag_moved = exchange(
        extend_pieces(pair, send_edge_table), give_back_pieces(node_diag_local, send_node_table)
    )
    pair_values = edge_values(extend_finish(pair, pair_moved))
    node_diag = give_back_finish(node_diag_local, node_diag_moved, send_node_table)[0]
    stiff_pair = element_terms(stiff_elem, pair_values)
    mass_pair = element_terms(mass_elem, pair_values)
    edge_diag_terms = jnp.einsum("jje->je", stiff_elem)[None]
    images = give_back(
        edge_sum(jnp.concatenate([stiff_pair[:modes], mass_pair[:modes], edge_diag_terms], axis=0)),
        send_edge_table,
    )
    stiff_x = images[:modes]
    mass_x = images[modes : 2 * modes]
    edge_diag = images[2 * modes]
    numerator, denominator = all_sum(
        jnp.stack([jnp.sum(x_block * stiff_x, axis=1), jnp.sum(x_block * mass_x, axis=1)])
    )
    quotient = numerator / denominator
    residual = stiff_x - quotient[:, None] * mass_x

    def stiff_image(vectors):
        values = edge_values(extend(vectors, send_edge_table))
        return give_back(edge_sum(element_terms(stiff_elem, values)), send_edge_table)

    center = 0.5 * (interval_high + interval_low)
    spread = 0.5 * (interval_high - interval_low)
    sigma = center / spread
    rho_now = 1.0 / sigma
    step_dir = residual / (center * edge_diag)
    smooth = step_dir
    for turn in range(CHEB_DEG - 1):
        rho_next = 1.0 / (2.0 * sigma - rho_now)
        remain = residual - stiff_image(smooth)
        step_dir = rho_next * rho_now * step_dir + 2.0 * rho_next / spread * remain / edge_diag
        smooth = smooth + step_dir
        rho_now = rho_next
    after = residual - stiff_image(smooth)
    gathered_res = scatter_cols(jnp.concatenate([after, -after], axis=1), grad_table)
    nodal_res = give_back(gathered_res, send_node_table)
    first = jacobi_weight * nodal_res / node_diag
    first_values = gather_cols(extend(first, send_node_table), node_table).reshape(modes, ndofs, elements)
    node_image = give_back(
        scatter_cols(element_terms(node_elem, first_values).reshape(modes, -1), node_table),
        send_node_table,
    )
    second = first + jacobi_weight * (nodal_res - node_image) / node_diag
    ends = gather_cols(extend(second, send_node_table), grad_table)
    w_block = smooth + ends[:, :owned_edges] - ends[:, owned_edges:]
    w_values = edge_values(extend(w_block, send_edge_table))
    stiff_wterm = element_terms(stiff_elem, w_values)
    mass_wterm = element_terms(mass_elem, w_values)
    basis_values = jnp.concatenate([pair_values[:modes], w_values, pair_values[modes:]], axis=0)
    w_rows = jnp.stack(
        [inner_elements(stiff_wterm, basis_values), inner_elements(mass_wterm, basis_values)]
    )
    stiff_part = inner_elements(pair_values, stiff_pair)
    mass_part = inner_elements(pair_values, mass_pair)
    full_gram = all_sum(arrange(jnp.stack([stiff_part, mass_part]), w_rows, modes))
    total_edges = owned_edges * lax.axis_size("dom")
    return (w_block, full_gram[0] / total_edges, full_gram[1] / total_edges)


def solution(mesh):
    in_specs = (
        P(None, "dom"),
        P(None, "dom"),
        P(None, None, "dom"),
        P(None, None, "dom"),
        P(None, None, "dom"),
        P(None, "dom"),
        P(None, "dom"),
        P(None, "dom"),
        P(None, "dom"),
        P(None, "dom"),
    )
    out_specs = (P(None, "dom"), P(), P())
    return jax.shard_map(shards, mesh=mesh, in_specs=in_specs, out_specs=out_specs, check_vma=False)
```

```python
import jax
import jax.numpy as jnp
from jax import lax
from jax.sharding import PartitionSpec as P

CHEB_DEG = 3
NNODE = 384
LANES = 128


highest = lax.Precision.HIGHEST
OFFSETS = (1, -1, 4, -4, 16, -16)
interval_low = 0.3
interval_high = 1.7
jacobi_weight = 0.7


def from_behind(shard, axis, by):
    length = lax.axis_size(axis)
    return lax.ppermute(shard, axis, [(i, (i + by) % length) for i in range(length)])


def shift_pieces(pieces, offsets):
    length = lax.axis_size("dom")
    out = [None] * len(pieces)
    targets = {}
    for number, offset in enumerate(offsets):
        targets.setdefault(offset % length, []).append(number)
    for offset, numbers in targets.items():
        sizes = [pieces[number].shape[1] for number in numbers]
        moved = from_behind(jnp.concatenate([pieces[number] for number in numbers], axis=1), "dom", offset)
        start = 0
        for number, size in zip(numbers, sizes):
            out[number] = moved[:, start : start + size]
            start += size
    return out


def all_sum(value):
    length = lax.axis_size("dom")
    if length & (length - 1):
        return lax.psum(value, "dom")
    stride = 1
    while stride < length:
        value = value + lax.ppermute(value, "dom", [(i, i ^ stride) for i in range(length)])
        stride *= 2
    return value


def index_table(index, length):
    groups = -(-length // LANES)
    lo = index % LANES
    hi = index // LANES
    lo_hot = (lo[:, None] == jnp.arange(LANES, dtype=jnp.int32)[None, :]).astype(jnp.float32)
    hi_mask = (hi[None, :] == jnp.arange(groups, dtype=jnp.int32)[:, None]).astype(jnp.float32)
    return lo_hot, hi_mask, length


def gather_cols(values, table):
    lo_hot, hi_mask, length = table
    groups = hi_mask.shape[0]
    rows = values.shape[0]
    padded = jnp.pad(values, ((0, 0), (0, groups * LANES - length)))
    split = padded.reshape(rows, groups, LANES)
    picked = jnp.einsum("rab,nb->ran", split, lo_hot, precision=highest)
    return jnp.sum(picked * hi_mask[None], axis=1)


def scatter_cols(terms, table):
    lo_hot, hi_mask, length = table
    groups = hi_mask.shape[0]
    rows = terms.shape[0]
    spread = terms[:, None, :] * hi_mask[None]
    summed = jnp.einsum("ran,nb->rab", spread, lo_hot, precision=highest)
    return summed.reshape(rows, groups * LANES)[:, :length]


def extend_pieces(values, send_table):
    outgoing = gather_cols(values, send_table)
    ghosts = outgoing.shape[1] // 6
    return [outgoing[:, d * ghosts : (d + 1) * ghosts] for d in range(6)], list(OFFSETS)


def extend_finish(values, moved):
    return jnp.concatenate([values] + moved, axis=1)


def give_back_pieces(extended, send_table):
    owned = send_table[2]
    ghosts = (extended.shape[1] - owned) // 6
    pieces = [extended[:, owned + d * ghosts : owned + (d + 1) * ghosts] for d in range(6)]
    return pieces, [-offset for offset in OFFSETS]


def give_back_finish(extended, moved, send_table):
    owned = send_table[2]
    return extended[:, :owned] + scatter_cols(jnp.concatenate(moved, axis=1), send_table)


def exchange(*groups):
    pieces, offsets, bounds = [], [], []
    flat = len({piece.shape[0] for group_pieces, _ in groups for piece in group_pieces}) > 1
    for group_pieces, group_offsets in groups:
        bounds.append((len(pieces), len(group_pieces)))
        pieces += [piece.reshape(1, -1) if flat else piece for piece in group_pieces]
        offsets += group_offsets
    moved = shift_pieces(pieces, offsets)
    out = []
    for (start, count), (group_pieces, _) in zip(bounds, groups):
        out.append([m.reshape(p.shape) for m, p in zip(moved[start : start + count], group_pieces)])
    return out


def extend(values, send_table):
    (moved,) = exchange(extend_pieces(values, send_table))
    return extend_finish(values, moved)


def give_back(extended, send_table):
    (moved,) = exchange(give_back_pieces(extended, send_table))
    return give_back_finish(extended, moved, send_table)


def element_terms(matrices, values):
    return jnp.sum(matrices[None, :, :, :] * values[:, None, :, :], axis=2)


def inner_elements(left, right):
    return jnp.einsum("cke,dke->cd", left, right, precision=highest)


def arrange(pair_part, row_part, modes):
    mode_mode = pair_part[:, :modes, :modes]
    mode_prev = pair_part[:, :modes, modes:]
    prev_mode = pair_part[:, modes:, :modes]
    prev_prev = pair_part[:, modes:, modes:]
    new_mode = jnp.swapaxes(row_part[:, :, :modes], 1, 2)
    new_prev = jnp.swapaxes(row_part[:, :, 2 * modes :], 1, 2)
    upper = jnp.concatenate([mode_mode, new_mode, mode_prev], axis=2)
    lower = jnp.concatenate([prev_mode, new_prev, prev_prev], axis=2)
    return jnp.concatenate([upper, row_part, lower], axis=1)


def shards(
    x_block,
    p_block,
    stiff_elem,
    mass_elem,
    node_elem,
    elem_edge,
    elem_node,
    send_edge,
    send_node,
    grad_pairs,
):
    modes = x_block.shape[0]
    owned_edges = x_block.shape[1]
    edofs, elements = elem_edge.shape
    ndofs = elem_node.shape[0]
    edge_length = owned_edges + 6 * send_edge.shape[1]
    node_length = NNODE + 6 * send_node.shape[1]

    edge_table = index_table(elem_edge.reshape(-1), edge_length)
    node_table = index_table(elem_node.reshape(-1), node_length)
    send_edge_table = index_table(send_edge.reshape(-1), owned_edges)
    send_node_table = index_table(send_node.reshape(-1), NNODE)
    tails = grad_pairs[0]
    heads = grad_pairs[1]
    grad_table = index_table(jnp.concatenate([heads, tails]), node_length)

    def edge_values(extended):
        return gather_cols(extended, edge_table).reshape(extended.shape[0], edofs, elements)

    def edge_sum(terms):
        return scatter_cols(terms.reshape(terms.shape[0], -1), edge_table)

    pair = jnp.concatenate([x_block, p_block], axis=0)
    node_diag_local = scatter_cols(jnp.einsum("jje->je", node_elem).reshape(1, -1), node_table)
    pair_moved, node_diag_moved = exchange(
        extend_pieces(pair, send_edge_table), give_back_pieces(node_diag_local, send_node_table)
    )
    pair_values = edge_values(extend_finish(pair, pair_moved))
    node_diag = give_back_finish(node_diag_local, node_diag_moved, send_node_table)[0]
    stiff_pair = element_terms(stiff_elem, pair_values)
    mass_pair = element_terms(mass_elem, pair_values)
    edge_diag_terms = jnp.einsum("jje->je", stiff_elem)[None]
    images = give_back(
        edge_sum(jnp.concatenate([stiff_pair[:modes], mass_pair[:modes], edge_diag_terms], axis=0)),
        send_edge_table,
    )
    stiff_x = images[:modes]
    mass_x = images[modes : 2 * modes]
    edge_diag = images[2 * modes]
    stiff_part = inner_elements(pair_values, stiff_pair)
    mass_part = inner_elements(pair_values, mass_pair)
    numerator, denominator = all_sum(
        jnp.stack([jnp.diagonal(stiff_part)[:modes], jnp.diagonal(mass_part)[:modes]])
    )
    quotient = numerator / denominator
    residual = stiff_x - quotient[:, None] * mass_x

    def stiff_image(vectors):
        values = edge_values(extend(vectors, send_edge_table))
        return give_back(edge_sum(element_terms(stiff_elem, values)), send_edge_table)

    center = 0.5 * (interval_high + interval_low)
    spread = 0.5 * (interval_high - interval_low)
    sigma = center / spread
    rho_now = 1.0 / sigma
    step_dir = residual / (center * edge_diag)
    smooth = step_dir
    for turn in range(CHEB_DEG - 1):
        rho_next = 1.0 / (2.0 * sigma - rho_now)
        remain = residual - stiff_image(smooth)
        step_dir = rho_next * rho_now * step_dir + 2.0 * rho_next / spread * remain / edge_diag
        smooth = smooth + step_dir
        rho_now = rho_next
    after = residual - stiff_image(smooth)
    gathered_res = scatter_cols(jnp.concatenate([after, -after], axis=1), grad_table)
    nodal_res = give_back(gathered_res, send_node_table)
    first = jacobi_weight * nodal_res / node_diag
    first_values = gather_cols(extend(first, send_node_table), node_table).reshape(modes, ndofs, elements)
    node_image = give_back(
        scatter_cols(element_terms(node_elem, first_values).reshape(modes, -1), node_table),
        send_node_table,
    )
    second = first + jacobi_weight * (nodal_res - node_image) / node_diag
    ends = gather_cols(extend(second, send_node_table), grad_table)
    w_block = smooth + ends[:, :owned_edges] - ends[:, owned_edges:]
    w_values = edge_values(extend(w_block, send_edge_table))
    stiff_wterm = element_terms(stiff_elem, w_values)
    mass_wterm = element_terms(mass_elem, w_values)
    basis_values = jnp.concatenate([pair_values[:modes], w_values, pair_values[modes:]], axis=0)
    w_rows = jnp.stack(
        [inner_elements(stiff_wterm, basis_values), inner_elements(mass_wterm, basis_values)]
    )
    full_gram = all_sum(arrange(jnp.stack([stiff_part, mass_part]), w_rows, modes))
    total_edges = owned_edges * lax.axis_size("dom")
    return (w_block, full_gram[0] / total_edges, full_gram[1] / total_edges)


def solution(mesh):
    in_specs = (
        P(None, "dom"),
        P(None, "dom"),
        P(None, None, "dom"),
        P(None, None, "dom"),
        P(None, None, "dom"),
        P(None, "dom"),
        P(None, "dom"),
        P(None, "dom"),
        P(None, "dom"),
        P(None, "dom"),
    )
    out_specs = (P(None, "dom"), P(), P())
    return jax.shard_map(shards, mesh=mesh, in_specs=in_specs, out_specs=out_specs, check_vma=False)
```

```python
import jax
import jax.numpy as jnp
from jax import lax
from jax.sharding import PartitionSpec as P

CHEB_DEG = 3
NNODE = 384
LANES = 128


highest = lax.Precision.HIGHEST
OFFSETS = (1, -1, 4, -4, 16, -16)
interval_low = 0.3
interval_high = 1.7
jacobi_weight = 0.7


def from_behind(shard, axis, by):
    length = lax.axis_size(axis)
    return lax.ppermute(shard, axis, [(i, (i + by) % length) for i in range(length)])


def shift_pieces(pieces, offsets):
    length = lax.axis_size("dom")
    out = [None] * len(pieces)
    targets = {}
    for number, offset in enumerate(offsets):
        targets.setdefault(offset % length, []).append(number)
    for offset, numbers in targets.items():
        sizes = [pieces[number].shape[1] for number in numbers]
        moved = from_behind(jnp.concatenate([pieces[number] for number in numbers], axis=1), "dom", offset)
        start = 0
        for number, size in zip(numbers, sizes):
            out[number] = moved[:, start : start + size]
            start += size
    return out


def all_sum(value):
    length = lax.axis_size("dom")
    if length & (length - 1):
        return lax.psum(value, "dom")
    me = lax.axis_index("dom")
    shift = 0
    while (1 << shift) < length:
        bits = 2 if (4 << shift) <= length else 1
        size = 1 << bits
        got = [value] + [
            lax.ppermute(value, "dom", [(i, i ^ (t << shift)) for i in range(length)])
            for t in range(1, size)
        ]
        digit = (me >> shift) & (size - 1)
        ordered = jnp.take(jnp.stack(got), jnp.arange(size) ^ digit, axis=0)
        while ordered.shape[0] > 1:
            ordered = ordered[0::2] + ordered[1::2]
        value = ordered[0]
        shift += bits
    return value


def index_table(index, length):
    groups = -(-length // LANES)
    lo = index % LANES
    hi = index // LANES
    lo_hot = (lo[:, None] == jnp.arange(LANES, dtype=jnp.int32)[None, :]).astype(jnp.float32)
    hi_mask = (hi[None, :] == jnp.arange(groups, dtype=jnp.int32)[:, None]).astype(jnp.float32)
    return lo_hot, hi_mask, length


def gather_cols(values, table):
    lo_hot, hi_mask, length = table
    groups = hi_mask.shape[0]
    rows = values.shape[0]
    padded = jnp.pad(values, ((0, 0), (0, groups * LANES - length)))
    split = padded.reshape(rows, groups, LANES)
    picked = jnp.einsum("rab,nb->ran", split, lo_hot, precision=highest)
    return jnp.sum(picked * hi_mask[None], axis=1)


def scatter_cols(terms, table):
    lo_hot, hi_mask, length = table
    groups = hi_mask.shape[0]
    rows = terms.shape[0]
    spread = terms[:, None, :] * hi_mask[None]
    summed = jnp.einsum("ran,nb->rab", spread, lo_hot, precision=highest)
    return summed.reshape(rows, groups * LANES)[:, :length]


def extend_pieces(values, send_table):
    outgoing = gather_cols(values, send_table)
    ghosts = outgoing.shape[1] // 6
    return [outgoing[:, d * ghosts : (d + 1) * ghosts] for d in range(6)], list(OFFSETS)


def extend_finish(values, moved):
    return jnp.concatenate([values] + moved, axis=1)


def give_back_pieces(extended, send_table):
    owned = send_table[2]
    ghosts = (extended.shape[1] - owned) // 6
    pieces = [extended[:, owned + d * ghosts : owned + (d + 1) * ghosts] for d in range(6)]
    return pieces, [-offset for offset in OFFSETS]


def give_back_finish(extended, moved, send_table):
    owned = send_table[2]
    return extended[:, :owned] + scatter_cols(jnp.concatenate(moved, axis=1), send_table)


def exchange(*groups):
    pieces, offsets, bounds = [], [], []
    flat = len({piece.shape[0] for group_pieces, _ in groups for piece in group_pieces}) > 1
    for group_pieces, group_offsets in groups:
        bounds.append((len(pieces), len(group_pieces)))
        pieces += [piece.reshape(1, -1) if flat else piece for piece in group_pieces]
        offsets += group_offsets
    moved = shift_pieces(pieces, offsets)
    out = []
    for (start, count), (group_pieces, _) in zip(bounds, groups):
        out.append([m.reshape(p.shape) for m, p in zip(moved[start : start + count], group_pieces)])
    return out


def extend(values, send_table):
    (moved,) = exchange(extend_pieces(values, send_table))
    return extend_finish(values, moved)


def give_back(extended, send_table):
    (moved,) = exchange(give_back_pieces(extended, send_table))
    return give_back_finish(extended, moved, send_table)


def element_terms(matrices, values):
    return jnp.sum(matrices[None, :, :, :] * values[:, None, :, :], axis=2)


def inner_elements(left, right):
    return jnp.einsum("cke,dke->cd", left, right, precision=highest)


def arrange(pair_part, row_part, modes):
    mode_mode = pair_part[:, :modes, :modes]
    mode_prev = pair_part[:, :modes, modes:]
    prev_mode = pair_part[:, modes:, :modes]
    prev_prev = pair_part[:, modes:, modes:]
    new_mode = jnp.swapaxes(row_part[:, :, :modes], 1, 2)
    new_prev = jnp.swapaxes(row_part[:, :, 2 * modes :], 1, 2)
    upper = jnp.concatenate([mode_mode, new_mode, mode_prev], axis=2)
    lower = jnp.concatenate([prev_mode, new_prev, prev_prev], axis=2)
    return jnp.concatenate([upper, row_part, lower], axis=1)


def shards(
    x_block,
    p_block,
    stiff_elem,
    mass_elem,
    node_elem,
    elem_edge,
    elem_node,
    send_edge,
    send_node,
    grad_pairs,
):
    modes = x_block.shape[0]
    owned_edges = x_block.shape[1]
    edofs, elements = elem_edge.shape
    ndofs = elem_node.shape[0]
    edge_length = owned_edges + 6 * send_edge.shape[1]
    node_length = NNODE + 6 * send_node.shape[1]

    edge_table = index_table(elem_edge.reshape(-1), edge_length)
    node_table = index_table(elem_node.reshape(-1), node_length)
    send_edge_table = index_table(send_edge.reshape(-1), owned_edges)
    send_node_table = index_table(send_node.reshape(-1), NNODE)
    tails = grad_pairs[0]
    heads = grad_pairs[1]
    grad_table = index_table(jnp.concatenate([heads, tails]), node_length)

    def edge_values(extended):
        return gather_cols(extended, edge_table).reshape(extended.shape[0], edofs, elements)

    def edge_sum(terms):
        return scatter_cols(terms.reshape(terms.shape[0], -1), edge_table)

    pair = jnp.concatenate([x_block, p_block], axis=0)
    node_diag_local = scatter_cols(jnp.einsum("jje->je", node_elem).reshape(1, -1), node_table)
    pair_moved, node_diag_moved = exchange(
        extend_pieces(pair, send_edge_table), give_back_pieces(node_diag_local, send_node_table)
    )
    pair_values = edge_values(extend_finish(pair, pair_moved))
    node_diag = give_back_finish(node_diag_local, node_diag_moved, send_node_table)[0]
    stiff_pair = element_terms(stiff_elem, pair_values)
    mass_pair = element_terms(mass_elem, pair_values)
    edge_diag_terms = jnp.einsum("jje->je", stiff_elem)[None]
    images = give_back(
        edge_sum(jnp.concatenate([stiff_pair[:modes], mass_pair[:modes], edge_diag_terms], axis=0)),
        send_edge_table,
    )
    stiff_x = images[:modes]
    mass_x = images[modes : 2 * modes]
    edge_diag = images[2 * modes]
    images_ext = extend(images, send_edge_table)
    stiff_part = inner_elements(pair_values, stiff_pair)
    mass_part = inner_elements(pair_values, mass_pair)
    numerator, denominator = all_sum(
        jnp.stack([jnp.diagonal(stiff_part)[:modes], jnp.diagonal(mass_part)[:modes]])
    )
    quotient = numerator / denominator
    residual = stiff_x - quotient[:, None] * mass_x

    def stiff_image(vectors, extended=None):
        if extended is None:
            extended = extend(vectors, send_edge_table)
        values = edge_values(extended)
        return give_back(edge_sum(element_terms(stiff_elem, values)), send_edge_table)

    center = 0.5 * (interval_high + interval_low)
    spread = 0.5 * (interval_high - interval_low)
    sigma = center / spread
    rho_now = 1.0 / sigma
    step_dir = residual / (center * edge_diag)
    smooth = step_dir
    residual_ext = images_ext[:modes] - quotient[:, None] * images_ext[modes : 2 * modes]
    smooth_ext = residual_ext / (center * images_ext[2 * modes])
    for turn in range(CHEB_DEG - 1):
        rho_next = 1.0 / (2.0 * sigma - rho_now)
        remain = residual - stiff_image(smooth, smooth_ext if turn == 0 else None)
        step_dir = rho_next * rho_now * step_dir + 2.0 * rho_next / spread * remain / edge_diag
        smooth = smooth + step_dir
        rho_now = rho_next
    after = residual - stiff_image(smooth)
    gathered_res = scatter_cols(jnp.concatenate([after, -after], axis=1), grad_table)
    nodal_res = give_back(gathered_res, send_node_table)
    first = jacobi_weight * nodal_res / node_diag
    first_values = gather_cols(extend(first, send_node_table), node_table).reshape(modes, ndofs, elements)
    node_image = give_back(
        scatter_cols(element_terms(node_elem, first_values).reshape(modes, -1), node_table),
        send_node_table,
    )
    second = first + jacobi_weight * (nodal_res - node_image) / node_diag
    ends = gather_cols(extend(second, send_node_table), grad_table)
    w_block = smooth + ends[:, :owned_edges] - ends[:, owned_edges:]
    w_values = edge_values(extend(w_block, send_edge_table))
    stiff_wterm = element_terms(stiff_elem, w_values)
    mass_wterm = element_terms(mass_elem, w_values)
    basis_values = jnp.concatenate([pair_values[:modes], w_values, pair_values[modes:]], axis=0)
    w_rows = jnp.stack(
        [inner_elements(stiff_wterm, basis_values), inner_elements(mass_wterm, basis_values)]
    )
    full_gram = all_sum(arrange(jnp.stack([stiff_part, mass_part]), w_rows, modes))
    total_edges = owned_edges * lax.axis_size("dom")
    return (w_block, full_gram[0] / total_edges, full_gram[1] / total_edges)


def solution(mesh):
    in_specs = (
        P(None, "dom"),
        P(None, "dom"),
        P(None, None, "dom"),
        P(None, None, "dom"),
        P(None, None, "dom"),
        P(None, "dom"),
        P(None, "dom"),
        P(None, "dom"),
        P(None, "dom"),
        P(None, "dom"),
    )
    out_specs = (P(None, "dom"), P(), P())
    return jax.shard_map(shards, mesh=mesh, in_specs=in_specs, out_specs=out_specs, check_vma=False)
```

```python
import jax
import jax.numpy as jnp
from jax import lax
from jax.sharding import PartitionSpec as P

CHEB_DEG = 3
NNODE = 384
LANES = 128


highest = lax.Precision.HIGHEST
OFFSETS = (1, -1, 4, -4, 16, -16)
interval_low = 0.3
interval_high = 1.7
jacobi_weight = 0.7


def from_behind(shard, axis, by):
    length = lax.axis_size(axis)
    return lax.ppermute(shard, axis, [(i, (i + by) % length) for i in range(length)])


def shift_pieces(pieces, offsets):
    length = lax.axis_size("dom")
    out = [None] * len(pieces)
    targets = {}
    for number, offset in enumerate(offsets):
        targets.setdefault(offset % length, []).append(number)
    for offset, numbers in targets.items():
        sizes = [pieces[number].shape[1] for number in numbers]
        moved = from_behind(jnp.concatenate([pieces[number] for number in numbers], axis=1), "dom", offset)
        start = 0
        for number, size in zip(numbers, sizes):
            out[number] = moved[:, start : start + size]
            start += size
    return out


def all_sum(value):
    length = lax.axis_size("dom")
    if length & (length - 1):
        return lax.psum(value, "dom")
    me = lax.axis_index("dom")
    shift = 0
    while (1 << shift) < length:
        bits = 2 if (4 << shift) <= length else 1
        size = 1 << bits
        got = [value] + [
            lax.ppermute(value, "dom", [(i, i ^ (t << shift)) for i in range(length)])
            for t in range(1, size)
        ]
        digit = (me >> shift) & (size - 1)
        ordered = jnp.take(jnp.stack(got), jnp.arange(size) ^ digit, axis=0)
        while ordered.shape[0] > 1:
            ordered = ordered[0::2] + ordered[1::2]
        value = ordered[0]
        shift += bits
    return value


def index_table(index, length):
    groups = -(-length // LANES)
    lo = index % LANES
    hi = index // LANES
    lo_hot = (lo[:, None] == jnp.arange(LANES, dtype=jnp.int32)[None, :]).astype(jnp.float32)
    hi_mask = (hi[None, :] == jnp.arange(groups, dtype=jnp.int32)[:, None]).astype(jnp.float32)
    return lo_hot, hi_mask, length


def gather_cols(values, table):
    lo_hot, hi_mask, length = table
    groups = hi_mask.shape[0]
    rows = values.shape[0]
    padded = jnp.pad(values, ((0, 0), (0, groups * LANES - length)))
    split = padded.reshape(rows, groups, LANES)
    picked = jnp.einsum("rab,nb->ran", split, lo_hot, precision=highest)
    return jnp.sum(picked * hi_mask[None], axis=1)


def gather_split(owned, ghosts, table):
    lo_hot, hi_mask, length = table
    rows, width = owned.shape
    if width % LANES:
        return gather_cols(jnp.concatenate([owned, ghosts], axis=1), table)
    split = width // LANES
    groups = hi_mask.shape[0]
    near = jnp.einsum("rab,nb->ran", owned.reshape(rows, split, LANES), lo_hot, precision=highest)
    far = jnp.pad(ghosts, ((0, 0), (0, (groups - split) * LANES - ghosts.shape[1])))
    far = jnp.einsum("rab,nb->ran", far.reshape(rows, groups - split, LANES), lo_hot, precision=highest)
    return jnp.sum(near * hi_mask[None, :split], axis=1) + jnp.sum(far * hi_mask[None, split:], axis=1)


def scatter_split(terms, table, width):
    lo_hot, hi_mask, length = table
    rows = terms.shape[0]
    groups = hi_mask.shape[0]
    if width % LANES:
        summed = scatter_cols(terms, table)
        return summed[:, :width], summed[:, width:]
    split = width // LANES
    spread = terms[:, None, :] * hi_mask[None]
    far = jnp.einsum("ran,nb->rab", spread[:, split:], lo_hot, precision=highest)
    near = jnp.einsum("ran,nb->rab", spread[:, :split], lo_hot, precision=highest)
    far = far.reshape(rows, (groups - split) * LANES)[:, : length - width]
    return near.reshape(rows, width), far


def scatter_cols(terms, table):
    lo_hot, hi_mask, length = table
    groups = hi_mask.shape[0]
    rows = terms.shape[0]
    spread = terms[:, None, :] * hi_mask[None]
    summed = jnp.einsum("ran,nb->rab", spread, lo_hot, precision=highest)
    return summed.reshape(rows, groups * LANES)[:, :length]


def extend_pieces(values, send_table):
    outgoing = gather_cols(values, send_table)
    ghosts = outgoing.shape[1] // 6
    return [outgoing[:, d * ghosts : (d + 1) * ghosts] for d in range(6)], list(OFFSETS)


def extend_finish(values, moved):
    return jnp.concatenate([values] + moved, axis=1)


def give_back_pieces(extended, send_table):
    owned = send_table[2]
    ghosts = (extended.shape[1] - owned) // 6
    pieces = [extended[:, owned + d * ghosts : owned + (d + 1) * ghosts] for d in range(6)]
    return pieces, [-offset for offset in OFFSETS]


def give_back_finish(extended, moved, send_table):
    owned = send_table[2]
    return extended[:, :owned] + scatter_cols(jnp.concatenate(moved, axis=1), send_table)


def exchange(*groups):
    pieces, offsets, bounds = [], [], []
    flat = len({piece.shape[0] for group_pieces, _ in groups for piece in group_pieces}) > 1
    for group_pieces, group_offsets in groups:
        bounds.append((len(pieces), len(group_pieces)))
        pieces += [piece.reshape(1, -1) if flat else piece for piece in group_pieces]
        offsets += group_offsets
    moved = shift_pieces(pieces, offsets)
    out = []
    for (start, count), (group_pieces, _) in zip(bounds, groups):
        out.append([m.reshape(p.shape) for m, p in zip(moved[start : start + count], group_pieces)])
    return out


def extend(values, send_table):
    (moved,) = exchange(extend_pieces(values, send_table))
    return extend_finish(values, moved)


def extend_gather(values, send_table, table):
    (moved,) = exchange(extend_pieces(values, send_table))
    return gather_split(values, jnp.concatenate(moved, axis=1), table)


def sum_give_back(terms, table, send_table):
    owned = send_table[2]
    near, far = scatter_split(terms, table, owned)
    ghosts = far.shape[1] // 6
    pieces = [far[:, d * ghosts : (d + 1) * ghosts] for d in range(6)]
    (moved,) = exchange((pieces, [-offset for offset in OFFSETS]))
    return near + scatter_cols(jnp.concatenate(moved, axis=1), send_table)


def give_back(extended, send_table):
    (moved,) = exchange(give_back_pieces(extended, send_table))
    return give_back_finish(extended, moved, send_table)


def element_terms(matrices, values):
    return jnp.sum(matrices[None, :, :, :] * values[:, None, :, :], axis=2)


def inner_elements(left, right):
    return jnp.einsum("cke,dke->cd", left, right, precision=highest)


def arrange(pair_part, row_part, modes):
    mode_mode = pair_part[:, :modes, :modes]
    mode_prev = pair_part[:, :modes, modes:]
    prev_mode = pair_part[:, modes:, :modes]
    prev_prev = pair_part[:, modes:, modes:]
    new_mode = jnp.swapaxes(row_part[:, :, :modes], 1, 2)
    new_prev = jnp.swapaxes(row_part[:, :, 2 * modes :], 1, 2)
    upper = jnp.concatenate([mode_mode, new_mode, mode_prev], axis=2)
    lower = jnp.concatenate([prev_mode, new_prev, prev_prev], axis=2)
    return jnp.concatenate([upper, row_part, lower], axis=1)


def shards(
    x_block,
    p_block,
    stiff_elem,
    mass_elem,
    node_elem,
    elem_edge,
    elem_node,
    send_edge,
    send_node,
    grad_pairs,
):
    modes = x_block.shape[0]
    owned_edges = x_block.shape[1]
    edofs, elements = elem_edge.shape
    ndofs = elem_node.shape[0]
    edge_length = owned_edges + 6 * send_edge.shape[1]
    node_length = NNODE + 6 * send_node.shape[1]

    edge_table = index_table(elem_edge.reshape(-1), edge_length)
    node_table = index_table(elem_node.reshape(-1), node_length)
    send_edge_table = index_table(send_edge.reshape(-1), owned_edges)
    send_node_table = index_table(send_node.reshape(-1), NNODE)
    tails = grad_pairs[0]
    heads = grad_pairs[1]
    grad_table = index_table(jnp.concatenate([heads, tails]), node_length)

    def edge_values(extended):
        return gather_cols(extended, edge_table).reshape(extended.shape[0], edofs, elements)

    def edge_sum(terms):
        return scatter_cols(terms.reshape(terms.shape[0], -1), edge_table)

    pair = jnp.concatenate([x_block, p_block], axis=0)
    node_diag_local = scatter_cols(jnp.einsum("jje->je", node_elem).reshape(1, -1), node_table)
    pair_moved, node_diag_moved = exchange(
        extend_pieces(pair, send_edge_table), give_back_pieces(node_diag_local, send_node_table)
    )
    pair_values = edge_values(extend_finish(pair, pair_moved))
    node_diag = give_back_finish(node_diag_local, node_diag_moved, send_node_table)[0]
    stiff_pair = element_terms(stiff_elem, pair_values)
    mass_pair = element_terms(mass_elem, pair_values)
    edge_diag_terms = jnp.einsum("jje->je", stiff_elem)[None]
    images = sum_give_back(
        jnp.concatenate([stiff_pair[:modes], mass_pair[:modes], edge_diag_terms], axis=0).reshape(
            2 * modes + 1, -1
        ),
        edge_table,
        send_edge_table,
    )
    stiff_x = images[:modes]
    mass_x = images[modes : 2 * modes]
    edge_diag = images[2 * modes]
    stiff_part = inner_elements(pair_values, stiff_pair)
    mass_part = inner_elements(pair_values, mass_pair)
    numerator, denominator = all_sum(
        jnp.stack([jnp.diagonal(stiff_part)[:modes], jnp.diagonal(mass_part)[:modes]])
    )
    quotient = numerator / denominator
    residual = stiff_x - quotient[:, None] * mass_x

    def stiff_image(vectors):
        values = extend_gather(vectors, send_edge_table, edge_table).reshape(-1, edofs, elements)
        terms = element_terms(stiff_elem, values)
        return sum_give_back(terms.reshape(terms.shape[0], -1), edge_table, send_edge_table)

    center = 0.5 * (interval_high + interval_low)
    spread = 0.5 * (interval_high - interval_low)
    sigma = center / spread
    rho_now = 1.0 / sigma
    step_dir = residual / (center * edge_diag)
    smooth = step_dir
    for turn in range(CHEB_DEG - 1):
        rho_next = 1.0 / (2.0 * sigma - rho_now)
        remain = residual - stiff_image(smooth)
        step_dir = rho_next * rho_now * step_dir + 2.0 * rho_next / spread * remain / edge_diag
        smooth = smooth + step_dir
        rho_now = rho_next
    after = residual - stiff_image(smooth)
    nodal_res = sum_give_back(jnp.concatenate([after, -after], axis=1), grad_table, send_node_table)
    first = jacobi_weight * nodal_res / node_diag
    first_values = extend_gather(first, send_node_table, node_table).reshape(modes, ndofs, elements)
    node_image = sum_give_back(
        element_terms(node_elem, first_values).reshape(modes, -1), node_table, send_node_table
    )
    second = first + jacobi_weight * (nodal_res - node_image) / node_diag
    ends = extend_gather(second, send_node_table, grad_table)
    w_block = smooth + ends[:, :owned_edges] - ends[:, owned_edges:]
    w_values = extend_gather(w_block, send_edge_table, edge_table).reshape(modes, edofs, elements)
    stiff_wterm = element_terms(stiff_elem, w_values)
    mass_wterm = element_terms(mass_elem, w_values)
    basis_values = jnp.concatenate([pair_values[:modes], w_values, pair_values[modes:]], axis=0)
    w_rows = jnp.stack(
        [inner_elements(stiff_wterm, basis_values), inner_elements(mass_wterm, basis_values)]
    )
    full_gram = all_sum(arrange(jnp.stack([stiff_part, mass_part]), w_rows, modes))
    total_edges = owned_edges * lax.axis_size("dom")
    return (w_block, full_gram[0] / total_edges, full_gram[1] / total_edges)


def solution(mesh):
    in_specs = (
        P(None, "dom"),
        P(None, "dom"),
        P(None, None, "dom"),
        P(None, None, "dom"),
        P(None, None, "dom"),
        P(None, "dom"),
        P(None, "dom"),
        P(None, "dom"),
        P(None, "dom"),
        P(None, "dom"),
    )
    out_specs = (P(None, "dom"), P(), P())
    return jax.shard_map(shards, mesh=mesh, in_specs=in_specs, out_specs=out_specs, check_vma=False)
```

```python
import jax
import jax.numpy as jnp
from jax import lax
from jax.sharding import PartitionSpec as P

CHEB_DEG = 3
NNODE = 384
LANES = 128


highest = lax.Precision.HIGHEST
OFFSETS = (1, -1, 4, -4, 16, -16)
interval_low = 0.3
interval_high = 1.7
jacobi_weight = 0.7


def from_behind(shard, axis, by):
    length = lax.axis_size(axis)
    return lax.ppermute(shard, axis, [(i, (i + by) % length) for i in range(length)])


def shift_pieces(pieces, offsets):
    length = lax.axis_size("dom")
    out = [None] * len(pieces)
    targets = {}
    for number, offset in enumerate(offsets):
        targets.setdefault(offset % length, []).append(number)
    for offset, numbers in targets.items():
        sizes = [pieces[number].shape[1] for number in numbers]
        moved = from_behind(jnp.concatenate([pieces[number] for number in numbers], axis=1), "dom", offset)
        start = 0
        for number, size in zip(numbers, sizes):
            out[number] = moved[:, start : start + size]
            start += size
    return out


def all_sum(value):
    length = lax.axis_size("dom")
    if length & (length - 1):
        return lax.psum(value, "dom")
    me = lax.axis_index("dom")
    shift = 0
    while (1 << shift) < length:
        bits = 2 if (4 << shift) <= length else 1
        size = 1 << bits
        got = [value] + [
            lax.ppermute(value, "dom", [(i, i ^ (t << shift)) for i in range(length)])
            for t in range(1, size)
        ]
        digit = (me >> shift) & (size - 1)
        ordered = []
        for member in range(size):
            pick = got[0]
            for t in range(1, size):
                pick = jnp.where((member ^ digit) == t, got[t], pick)
            ordered.append(pick)
        while len(ordered) > 1:
            ordered = [ordered[k] + ordered[k + 1] for k in range(0, len(ordered), 2)]
        value = ordered[0]
        shift += bits
    return value


def index_table(index, length):
    groups = -(-length // LANES)
    lo = index % LANES
    hi = index // LANES
    lo_hot = (lo[:, None] == jnp.arange(LANES, dtype=jnp.int32)[None, :]).astype(jnp.float32)
    hi_mask = (hi[None, :] == jnp.arange(groups, dtype=jnp.int32)[:, None]).astype(jnp.float32)
    return lo_hot, hi_mask, length


def gather_cols(values, table):
    lo_hot, hi_mask, length = table
    groups = hi_mask.shape[0]
    rows = values.shape[0]
    padded = jnp.pad(values, ((0, 0), (0, groups * LANES - length)))
    split = padded.reshape(rows, groups, LANES)
    picked = jnp.einsum("rab,nb->ran", split, lo_hot, precision=highest)
    return jnp.sum(picked * hi_mask[None], axis=1)


def scatter_cols(terms, table):
    lo_hot, hi_mask, length = table
    groups = hi_mask.shape[0]
    rows = terms.shape[0]
    spread = terms[:, None, :] * hi_mask[None]
    summed = jnp.einsum("ran,nb->rab", spread, lo_hot, precision=highest)
    return summed.reshape(rows, groups * LANES)[:, :length]


def extend_pieces(values, send_table):
    outgoing = gather_cols(values, send_table)
    ghosts = outgoing.shape[1] // 6
    return [outgoing[:, d * ghosts : (d + 1) * ghosts] for d in range(6)], list(OFFSETS)


def extend_finish(values, moved):
    return jnp.concatenate([values] + moved, axis=1)


def give_back_pieces(extended, send_table):
    owned = send_table[2]
    ghosts = (extended.shape[1] - owned) // 6
    pieces = [extended[:, owned + d * ghosts : owned + (d + 1) * ghosts] for d in range(6)]
    return pieces, [-offset for offset in OFFSETS]


def give_back_finish(extended, moved, send_table):
    owned = send_table[2]
    return extended[:, :owned] + scatter_cols(jnp.concatenate(moved, axis=1), send_table)


def exchange(*groups):
    pieces, offsets, bounds = [], [], []
    flat = len({piece.shape[0] for group_pieces, _ in groups for piece in group_pieces}) > 1
    for group_pieces, group_offsets in groups:
        bounds.append((len(pieces), len(group_pieces)))
        pieces += [piece.reshape(1, -1) if flat else piece for piece in group_pieces]
        offsets += group_offsets
    moved = shift_pieces(pieces, offsets)
    out = []
    for (start, count), (group_pieces, _) in zip(bounds, groups):
        out.append([m.reshape(p.shape) for m, p in zip(moved[start : start + count], group_pieces)])
    return out


def extend(values, send_table):
    (moved,) = exchange(extend_pieces(values, send_table))
    return extend_finish(values, moved)


def give_back(extended, send_table):
    (moved,) = exchange(give_back_pieces(extended, send_table))
    return give_back_finish(extended, moved, send_table)


def element_terms(matrices, values):
    return jnp.sum(matrices[None, :, :, :] * values[:, None, :, :], axis=2)


def inner_elements(left, right):
    return jnp.einsum("cke,dke->cd", left, right, precision=highest)


def arrange(pair_part, row_part, modes):
    mode_mode = pair_part[:, :modes, :modes]
    mode_prev = pair_part[:, :modes, modes:]
    prev_mode = pair_part[:, modes:, :modes]
    prev_prev = pair_part[:, modes:, modes:]
    new_mode = jnp.swapaxes(row_part[:, :, :modes], 1, 2)
    new_prev = jnp.swapaxes(row_part[:, :, 2 * modes :], 1, 2)
    upper = jnp.concatenate([mode_mode, new_mode, mode_prev], axis=2)
    lower = jnp.concatenate([prev_mode, new_prev, prev_prev], axis=2)
    return jnp.concatenate([upper, row_part, lower], axis=1)


def shards(
    x_block,
    p_block,
    stiff_elem,
    mass_elem,
    node_elem,
    elem_edge,
    elem_node,
    send_edge,
    send_node,
    grad_pairs,
):
    modes = x_block.shape[0]
    owned_edges = x_block.shape[1]
    edofs, elements = elem_edge.shape
    ndofs = elem_node.shape[0]
    edge_length = owned_edges + 6 * send_edge.shape[1]
    node_length = NNODE + 6 * send_node.shape[1]

    edge_table = index_table(elem_edge.reshape(-1), edge_length)
    node_table = index_table(elem_node.reshape(-1), node_length)
    send_edge_table = index_table(send_edge.reshape(-1), owned_edges)
    send_node_table = index_table(send_node.reshape(-1), NNODE)
    tails = grad_pairs[0]
    heads = grad_pairs[1]
    grad_table = index_table(jnp.concatenate([heads, tails]), node_length)

    def edge_values(extended):
        return gather_cols(extended, edge_table).reshape(extended.shape[0], edofs, elements)

    def edge_sum(terms):
        return scatter_cols(terms.reshape(terms.shape[0], -1), edge_table)

    pair = jnp.concatenate([x_block, p_block], axis=0)
    node_diag_local = scatter_cols(jnp.einsum("jje->je", node_elem).reshape(1, -1), node_table)
    pair_moved, node_diag_moved = exchange(
        extend_pieces(pair, send_edge_table), give_back_pieces(node_diag_local, send_node_table)
    )
    pair_values = edge_values(extend_finish(pair, pair_moved))
    node_diag = give_back_finish(node_diag_local, node_diag_moved, send_node_table)[0]
    stiff_pair = element_terms(stiff_elem, pair_values)
    mass_pair = element_terms(mass_elem, pair_values)
    edge_diag_terms = jnp.einsum("jje->je", stiff_elem)[None]
    images = give_back(
        edge_sum(jnp.concatenate([stiff_pair[:modes], mass_pair[:modes], edge_diag_terms], axis=0)),
        send_edge_table,
    )
    stiff_x = images[:modes]
    mass_x = images[modes : 2 * modes]
    edge_diag = images[2 * modes]
    stiff_part = inner_elements(pair_values, stiff_pair)
    mass_part = inner_elements(pair_values, mass_pair)
    numerator, denominator = all_sum(
        jnp.stack([jnp.diagonal(stiff_part)[:modes], jnp.diagonal(mass_part)[:modes]])
    )
    quotient = numerator / denominator
    residual = stiff_x - quotient[:, None] * mass_x

    def stiff_image(vectors):
        values = edge_values(extend(vectors, send_edge_table))
        return give_back(edge_sum(element_terms(stiff_elem, values)), send_edge_table)

    center = 0.5 * (interval_high + interval_low)
    spread = 0.5 * (interval_high - interval_low)
    sigma = center / spread
    rho_now = 1.0 / sigma
    step_dir = residual / (center * edge_diag)
    smooth = step_dir
    for turn in range(CHEB_DEG - 1):
        rho_next = 1.0 / (2.0 * sigma - rho_now)
        remain = residual - stiff_image(smooth)
        step_dir = rho_next * rho_now * step_dir + 2.0 * rho_next / spread * remain / edge_diag
        smooth = smooth + step_dir
        rho_now = rho_next
    after = residual - stiff_image(smooth)
    gathered_res = scatter_cols(jnp.concatenate([after, -after], axis=1), grad_table)
    nodal_res = give_back(gathered_res, send_node_table)
    first = jacobi_weight * nodal_res / node_diag
    first_values = gather_cols(extend(first, send_node_table), node_table).reshape(modes, ndofs, elements)
    node_image = give_back(
        scatter_cols(element_terms(node_elem, first_values).reshape(modes, -1), node_table),
        send_node_table,
    )
    second = first + jacobi_weight * (nodal_res - node_image) / node_diag
    ends = gather_cols(extend(second, send_node_table), grad_table)
    w_block = smooth + ends[:, :owned_edges] - ends[:, owned_edges:]
    w_values = edge_values(extend(w_block, send_edge_table))
    stiff_wterm = element_terms(stiff_elem, w_values)
    mass_wterm = element_terms(mass_elem, w_values)
    basis_values = jnp.concatenate([pair_values[:modes], w_values, pair_values[modes:]], axis=0)
    w_rows = jnp.stack(
        [inner_elements(stiff_wterm, basis_values), inner_elements(mass_wterm, basis_values)]
    )
    full_gram = all_sum(arrange(jnp.stack([stiff_part, mass_part]), w_rows, modes))
    total_edges = owned_edges * lax.axis_size("dom")
    return (w_block, full_gram[0] / total_edges, full_gram[1] / total_edges)


def solution(mesh):
    in_specs = (
        P(None, "dom"),
        P(None, "dom"),
        P(None, None, "dom"),
        P(None, None, "dom"),
        P(None, None, "dom"),
        P(None, "dom"),
        P(None, "dom"),
        P(None, "dom"),
        P(None, "dom"),
        P(None, "dom"),
    )
    out_specs = (P(None, "dom"), P(), P())
    return jax.shard_map(shards, mesh=mesh, in_specs=in_specs, out_specs=out_specs, check_vma=False)
```

```python
import jax
import jax.numpy as jnp
from jax import lax
from jax.sharding import PartitionSpec as P

CHEB_DEG = 3
NNODE = 384
LANES = 128


highest = lax.Precision.HIGHEST
OFFSETS = (1, -1, 4, -4, 16, -16)
interval_low = 0.3
interval_high = 1.7
jacobi_weight = 0.7


def from_behind(shard, axis, by):
    length = lax.axis_size(axis)
    return lax.ppermute(shard, axis, [(i, (i + by) % length) for i in range(length)])


def shift_pieces(pieces, offsets):
    length = lax.axis_size("dom")
    out = [None] * len(pieces)
    targets = {}
    for number, offset in enumerate(offsets):
        targets.setdefault(offset % length, []).append(number)
    for offset, numbers in targets.items():
        sizes = [pieces[number].shape[1] for number in numbers]
        moved = from_behind(jnp.concatenate([pieces[number] for number in numbers], axis=1), "dom", offset)
        start = 0
        for number, size in zip(numbers, sizes):
            out[number] = moved[:, start : start + size]
            start += size
    return out


def all_sum(value):
    length = lax.axis_size("dom")
    if length & (length - 1):
        return lax.psum(value, "dom")
    me = lax.axis_index("dom")
    shift = 0
    while (1 << shift) < length:
        bits = 2 if (4 << shift) <= length else 1
        size = 1 << bits
        got = [value] + [
            lax.ppermute(value, "dom", [(i, i ^ (t << shift)) for i in range(length)])
            for t in range(1, size)
        ]
        digit = (me >> shift) & (size - 1)
        ordered = []
        for member in range(size):
            pick = got[0]
            for t in range(1, size):
                pick = jnp.where((member ^ digit) == t, got[t], pick)
            ordered.append(pick)
        while len(ordered) > 1:
            ordered = [ordered[k] + ordered[k + 1] for k in range(0, len(ordered), 2)]
        value = ordered[0]
        shift += bits
    return value


def index_table(index, length):
    groups = -(-length // LANES)
    lo = index % LANES
    hi = index // LANES
    lo_hot = (lo[:, None] == jnp.arange(LANES, dtype=jnp.int32)[None, :]).astype(jnp.float32)
    hi_mask = (hi[None, :] == jnp.arange(groups, dtype=jnp.int32)[:, None]).astype(jnp.float32)
    return lo_hot, hi_mask, length


def gather_cols(values, table):
    lo_hot, hi_mask, length = table
    groups = hi_mask.shape[0]
    rows = values.shape[0]
    padded = jnp.pad(values, ((0, 0), (0, groups * LANES - length)))
    split = padded.reshape(rows, groups, LANES)
    picked = jnp.einsum("rab,nb->ran", split, lo_hot, precision=lax.Precision.HIGH)
    return jnp.sum(picked * hi_mask[None], axis=1)


def scatter_cols(terms, table):
    lo_hot, hi_mask, length = table
    groups = hi_mask.shape[0]
    rows = terms.shape[0]
    spread = terms[:, None, :] * hi_mask[None]
    summed = jnp.einsum("ran,nb->rab", spread, lo_hot, precision=lax.Precision.HIGH)
    return summed.reshape(rows, groups * LANES)[:, :length]


def extend_pieces(values, send_table):
    outgoing = gather_cols(values, send_table)
    ghosts = outgoing.shape[1] // 6
    return [outgoing[:, d * ghosts : (d + 1) * ghosts] for d in range(6)], list(OFFSETS)


def extend_finish(values, moved):
    return jnp.concatenate([values] + moved, axis=1)


def give_back_pieces(extended, send_table):
    owned = send_table[2]
    ghosts = (extended.shape[1] - owned) // 6
    pieces = [extended[:, owned + d * ghosts : owned + (d + 1) * ghosts] for d in range(6)]
    return pieces, [-offset for offset in OFFSETS]


def give_back_finish(extended, moved, send_table):
    owned = send_table[2]
    return extended[:, :owned] + scatter_cols(jnp.concatenate(moved, axis=1), send_table)


def exchange(*groups):
    pieces, offsets, bounds = [], [], []
    flat = len({piece.shape[0] for group_pieces, _ in groups for piece in group_pieces}) > 1
    for group_pieces, group_offsets in groups:
        bounds.append((len(pieces), len(group_pieces)))
        pieces += [piece.reshape(1, -1) if flat else piece for piece in group_pieces]
        offsets += group_offsets
    moved = shift_pieces(pieces, offsets)
    out = []
    for (start, count), (group_pieces, _) in zip(bounds, groups):
        out.append([m.reshape(p.shape) for m, p in zip(moved[start : start + count], group_pieces)])
    return out


def extend(values, send_table):
    (moved,) = exchange(extend_pieces(values, send_table))
    return extend_finish(values, moved)


def give_back(extended, send_table):
    (moved,) = exchange(give_back_pieces(extended, send_table))
    return give_back_finish(extended, moved, send_table)


def element_terms(matrices, values):
    return jnp.sum(matrices[None, :, :, :] * values[:, None, :, :], axis=2)


def inner_elements(left, right):
    return jnp.einsum("cke,dke->cd", left, right, precision=highest)


def arrange(pair_part, row_part, modes):
    mode_mode = pair_part[:, :modes, :modes]
    mode_prev = pair_part[:, :modes, modes:]
    prev_mode = pair_part[:, modes:, :modes]
    prev_prev = pair_part[:, modes:, modes:]
    new_mode = jnp.swapaxes(row_part[:, :, :modes], 1, 2)
    new_prev = jnp.swapaxes(row_part[:, :, 2 * modes :], 1, 2)
    upper = jnp.concatenate([mode_mode, new_mode, mode_prev], axis=2)
    lower = jnp.concatenate([prev_mode, new_prev, prev_prev], axis=2)
    return jnp.concatenate([upper, row_part, lower], axis=1)


def shards(
    x_block,
    p_block,
    stiff_elem,
    mass_elem,
    node_elem,
    elem_edge,
    elem_node,
    send_edge,
    send_node,
    grad_pairs,
):
    modes = x_block.shape[0]
    owned_edges = x_block.shape[1]
    edofs, elements = elem_edge.shape
    ndofs = elem_node.shape[0]
    edge_length = owned_edges + 6 * send_edge.shape[1]
    node_length = NNODE + 6 * send_node.shape[1]

    edge_table = index_table(elem_edge.reshape(-1), edge_length)
    node_table = index_table(elem_node.reshape(-1), node_length)
    send_edge_table = index_table(send_edge.reshape(-1), owned_edges)
    send_node_table = index_table(send_node.reshape(-1), NNODE)
    tails = grad_pairs[0]
    heads = grad_pairs[1]
    grad_table = index_table(jnp.concatenate([heads, tails]), node_length)

    def edge_values(extended):
        return gather_cols(extended, edge_table).reshape(extended.shape[0], edofs, elements)

    def edge_sum(terms):
        return scatter_cols(terms.reshape(terms.shape[0], -1), edge_table)

    pair = jnp.concatenate([x_block, p_block], axis=0)
    node_diag_local = scatter_cols(jnp.einsum("jje->je", node_elem).reshape(1, -1), node_table)
    pair_moved, node_diag_moved = exchange(
        extend_pieces(pair, send_edge_table), give_back_pieces(node_diag_local, send_node_table)
    )
    pair_values = edge_values(extend_finish(pair, pair_moved))
    node_diag = give_back_finish(node_diag_local, node_diag_moved, send_node_table)[0]
    stiff_pair = element_terms(stiff_elem, pair_values)
    mass_pair = element_terms(mass_elem, pair_values)
    edge_diag_terms = jnp.einsum("jje->je", stiff_elem)[None]
    images = give_back(
        edge_sum(jnp.concatenate([stiff_pair[:modes], mass_pair[:modes], edge_diag_terms], axis=0)),
        send_edge_table,
    )
    stiff_x = images[:modes]
    mass_x = images[modes : 2 * modes]
    edge_diag = images[2 * modes]
    stiff_part = inner_elements(pair_values, stiff_pair)
    mass_part = inner_elements(pair_values, mass_pair)
    numerator, denominator = all_sum(
        jnp.stack([jnp.diagonal(stiff_part)[:modes], jnp.diagonal(mass_part)[:modes]])
    )
    quotient = numerator / denominator
    residual = stiff_x - quotient[:, None] * mass_x

    def stiff_image(vectors):
        values = edge_values(extend(vectors, send_edge_table))
        return give_back(edge_sum(element_terms(stiff_elem, values)), send_edge_table)

    center = 0.5 * (interval_high + interval_low)
    spread = 0.5 * (interval_high - interval_low)
    sigma = center / spread
    rho_now = 1.0 / sigma
    step_dir = residual / (center * edge_diag)
    smooth = step_dir
    for turn in range(CHEB_DEG - 1):
        rho_next = 1.0 / (2.0 * sigma - rho_now)
        remain = residual - stiff_image(smooth)
        step_dir = rho_next * rho_now * step_dir + 2.0 * rho_next / spread * remain / edge_diag
        smooth = smooth + step_dir
        rho_now = rho_next
    after = residual - stiff_image(smooth)
    gathered_res = scatter_cols(jnp.concatenate([after, -after], axis=1), grad_table)
    nodal_res = give_back(gathered_res, send_node_table)
    first = jacobi_weight * nodal_res / node_diag
    first_values = gather_cols(extend(first, send_node_table), node_table).reshape(modes, ndofs, elements)
    node_image = give_back(
        scatter_cols(element_terms(node_elem, first_values).reshape(modes, -1), node_table),
        send_node_table,
    )
    second = first + jacobi_weight * (nodal_res - node_image) / node_diag
    ends = gather_cols(extend(second, send_node_table), grad_table)
    w_block = smooth + ends[:, :owned_edges] - ends[:, owned_edges:]
    w_values = edge_values(extend(w_block, send_edge_table))
    stiff_wterm = element_terms(stiff_elem, w_values)
    mass_wterm = element_terms(mass_elem, w_values)
    basis_values = jnp.concatenate([pair_values[:modes], w_values, pair_values[modes:]], axis=0)
    w_rows = jnp.stack(
        [inner_elements(stiff_wterm, basis_values), inner_elements(mass_wterm, basis_values)]
    )
    full_gram = all_sum(arrange(jnp.stack([stiff_part, mass_part]), w_rows, modes))
    total_edges = owned_edges * lax.axis_size("dom")
    return (w_block, full_gram[0] / total_edges, full_gram[1] / total_edges)


def solution(mesh):
    in_specs = (
        P(None, "dom"),
        P(None, "dom"),
        P(None, None, "dom"),
        P(None, None, "dom"),
        P(None, None, "dom"),
        P(None, "dom"),
        P(None, "dom"),
        P(None, "dom"),
        P(None, "dom"),
        P(None, "dom"),
    )
    out_specs = (P(None, "dom"), P(), P())
    return jax.shard_map(shards, mesh=mesh, in_specs=in_specs, out_specs=out_specs, check_vma=False)
```

```python
import jax
import jax.numpy as jnp
from jax import lax
from jax.sharding import PartitionSpec as P

CHEB_DEG = 3
NNODE = 384
LANES = 128


highest = lax.Precision.HIGHEST
OFFSETS = (1, -1, 4, -4, 16, -16)
interval_low = 0.3
interval_high = 1.7
jacobi_weight = 0.7


def from_behind(shard, axis, by):
    length = lax.axis_size(axis)
    return lax.ppermute(shard, axis, [(i, (i + by) % length) for i in range(length)])


def shift_pieces(pieces, offsets):
    length = lax.axis_size("dom")
    out = [None] * len(pieces)
    targets = {}
    for number, offset in enumerate(offsets):
        targets.setdefault(offset % length, []).append(number)
    for offset, numbers in targets.items():
        sizes = [pieces[number].shape[1] for number in numbers]
        moved = from_behind(jnp.concatenate([pieces[number] for number in numbers], axis=1), "dom", offset)
        start = 0
        for number, size in zip(numbers, sizes):
            out[number] = moved[:, start : start + size]
            start += size
    return out


def all_sum(value):
    length = lax.axis_size("dom")
    if length & (length - 1):
        return lax.psum(value, "dom")
    me = lax.axis_index("dom")
    shift = 0
    while (1 << shift) < length:
        bits = 2 if (4 << shift) <= length else 1
        size = 1 << bits
        got = [value] + [
            lax.ppermute(value, "dom", [(i, i ^ (t << shift)) for i in range(length)])
            for t in range(1, size)
        ]
        digit = (me >> shift) & (size - 1)
        ordered = []
        for member in range(size):
            pick = got[0]
            for t in range(1, size):
                pick = jnp.where((member ^ digit) == t, got[t], pick)
            ordered.append(pick)
        while len(ordered) > 1:
            ordered = [ordered[k] + ordered[k + 1] for k in range(0, len(ordered), 2)]
        value = ordered[0]
        shift += bits
    return value


def index_table(index, length):
    groups = -(-length // LANES)
    lo = index % LANES
    hi = index // LANES
    lo_hot = (lo[:, None] == jnp.arange(LANES, dtype=jnp.int32)[None, :]).astype(jnp.float32)
    hi_mask = (hi[None, :] == jnp.arange(groups, dtype=jnp.int32)[:, None]).astype(jnp.float32)
    return lo_hot, hi_mask, length


def gather_cols(values, table):
    lo_hot, hi_mask, length = table
    groups = hi_mask.shape[0]
    rows = values.shape[0]
    padded = jnp.pad(values, ((0, 0), (0, groups * LANES - length)))
    split = padded.reshape(rows, groups, LANES)
    picked = jnp.einsum("rab,nb->ran", split, lo_hot, precision=lax.Precision.HIGH)
    return jnp.sum(picked * hi_mask[None], axis=1)


def scatter_cols(terms, table):
    lo_hot, hi_mask, length = table
    groups = hi_mask.shape[0]
    rows = terms.shape[0]
    spread = terms[:, None, :] * hi_mask[None]
    summed = jnp.einsum("ran,nb->rab", spread, lo_hot, precision=highest)
    return summed.reshape(rows, groups * LANES)[:, :length]


def extend_pieces(values, send_table):
    outgoing = gather_cols(values, send_table)
    ghosts = outgoing.shape[1] // 6
    return [outgoing[:, d * ghosts : (d + 1) * ghosts] for d in range(6)], list(OFFSETS)


def extend_finish(values, moved):
    return jnp.concatenate([values] + moved, axis=1)


def give_back_pieces(extended, send_table):
    owned = send_table[2]
    ghosts = (extended.shape[1] - owned) // 6
    pieces = [extended[:, owned + d * ghosts : owned + (d + 1) * ghosts] for d in range(6)]
    return pieces, [-offset for offset in OFFSETS]


def give_back_finish(extended, moved, send_table):
    owned = send_table[2]
    return extended[:, :owned] + scatter_cols(jnp.concatenate(moved, axis=1), send_table)


def exchange(*groups):
    pieces, offsets, bounds = [], [], []
    flat = len({piece.shape[0] for group_pieces, _ in groups for piece in group_pieces}) > 1
    for group_pieces, group_offsets in groups:
        bounds.append((len(pieces), len(group_pieces)))
        pieces += [piece.reshape(1, -1) if flat else piece for piece in group_pieces]
        offsets += group_offsets
    moved = shift_pieces(pieces, offsets)
    out = []
    for (start, count), (group_pieces, _) in zip(bounds, groups):
        out.append([m.reshape(p.shape) for m, p in zip(moved[start : start + count], group_pieces)])
    return out


def extend(values, send_table):
    (moved,) = exchange(extend_pieces(values, send_table))
    return extend_finish(values, moved)


def give_back(extended, send_table):
    (moved,) = exchange(give_back_pieces(extended, send_table))
    return give_back_finish(extended, moved, send_table)


def element_terms(matrices, values):
    return jnp.sum(matrices[None, :, :, :] * values[:, None, :, :], axis=2)


def inner_elements(left, right):
    return jnp.einsum("cke,dke->cd", left, right, precision=highest)


def arrange(pair_part, row_part, modes):
    mode_mode = pair_part[:, :modes, :modes]
    mode_prev = pair_part[:, :modes, modes:]
    prev_mode = pair_part[:, modes:, :modes]
    prev_prev = pair_part[:, modes:, modes:]
    new_mode = jnp.swapaxes(row_part[:, :, :modes], 1, 2)
    new_prev = jnp.swapaxes(row_part[:, :, 2 * modes :], 1, 2)
    upper = jnp.concatenate([mode_mode, new_mode, mode_prev], axis=2)
    lower = jnp.concatenate([prev_mode, new_prev, prev_prev], axis=2)
    return jnp.concatenate([upper, row_part, lower], axis=1)


def shards(
    x_block,
    p_block,
    stiff_elem,
    mass_elem,
    node_elem,
    elem_edge,
    elem_node,
    send_edge,
    send_node,
    grad_pairs,
):
    modes = x_block.shape[0]
    owned_edges = x_block.shape[1]
    edofs, elements = elem_edge.shape
    ndofs = elem_node.shape[0]
    edge_length = owned_edges + 6 * send_edge.shape[1]
    node_length = NNODE + 6 * send_node.shape[1]

    edge_table = index_table(elem_edge.reshape(-1), edge_length)
    node_table = index_table(elem_node.reshape(-1), node_length)
    send_edge_table = index_table(send_edge.reshape(-1), owned_edges)
    send_node_table = index_table(send_node.reshape(-1), NNODE)
    tails = grad_pairs[0]
    heads = grad_pairs[1]
    grad_table = index_table(jnp.concatenate([heads, tails]), node_length)

    def edge_values(extended):
        return gather_cols(extended, edge_table).reshape(extended.shape[0], edofs, elements)

    def edge_sum(terms):
        return scatter_cols(terms.reshape(terms.shape[0], -1), edge_table)

    pair = jnp.concatenate([x_block, p_block], axis=0)
    node_diag_local = scatter_cols(jnp.einsum("jje->je", node_elem).reshape(1, -1), node_table)
    pair_moved, node_diag_moved = exchange(
        extend_pieces(pair, send_edge_table), give_back_pieces(node_diag_local, send_node_table)
    )
    pair_values = edge_values(extend_finish(pair, pair_moved))
    node_diag = give_back_finish(node_diag_local, node_diag_moved, send_node_table)[0]
    stiff_pair = element_terms(stiff_elem, pair_values)
    mass_pair = element_terms(mass_elem, pair_values)
    edge_diag_terms = jnp.einsum("jje->je", stiff_elem)[None]
    images = give_back(
        edge_sum(jnp.concatenate([stiff_pair[:modes], mass_pair[:modes], edge_diag_terms], axis=0)),
        send_edge_table,
    )
    stiff_x = images[:modes]
    mass_x = images[modes : 2 * modes]
    edge_diag = images[2 * modes]
    stiff_part = inner_elements(pair_values, stiff_pair)
    mass_part = inner_elements(pair_values, mass_pair)
    numerator, denominator = all_sum(
        jnp.stack([jnp.diagonal(stiff_part)[:modes], jnp.diagonal(mass_part)[:modes]])
    )
    quotient = numerator / denominator
    residual = stiff_x - quotient[:, None] * mass_x

    def stiff_image(vectors):
        values = edge_values(extend(vectors, send_edge_table))
        return give_back(edge_sum(element_terms(stiff_elem, values)), send_edge_table)

    center = 0.5 * (interval_high + interval_low)
    spread = 0.5 * (interval_high - interval_low)
    sigma = center / spread
    rho_now = 1.0 / sigma
    step_dir = residual / (center * edge_diag)
    smooth = step_dir
    for turn in range(CHEB_DEG - 1):
        rho_next = 1.0 / (2.0 * sigma - rho_now)
        remain = residual - stiff_image(smooth)
        step_dir = rho_next * rho_now * step_dir + 2.0 * rho_next / spread * remain / edge_diag
        smooth = smooth + step_dir
        rho_now = rho_next
    after = residual - stiff_image(smooth)
    gathered_res = scatter_cols(jnp.concatenate([after, -after], axis=1), grad_table)
    nodal_res = give_back(gathered_res, send_node_table)
    first = jacobi_weight * nodal_res / node_diag
    first_values = gather_cols(extend(first, send_node_table), node_table).reshape(modes, ndofs, elements)
    node_image = give_back(
        scatter_cols(element_terms(node_elem, first_values).reshape(modes, -1), node_table),
        send_node_table,
    )
    second = first + jacobi_weight * (nodal_res - node_image) / node_diag
    ends = gather_cols(extend(second, send_node_table), grad_table)
    w_block = smooth + ends[:, :owned_edges] - ends[:, owned_edges:]
    w_values = edge_values(extend(w_block, send_edge_table))
    stiff_wterm = element_terms(stiff_elem, w_values)
    mass_wterm = element_terms(mass_elem, w_values)
    basis_values = jnp.concatenate([pair_values[:modes], w_values, pair_values[modes:]], axis=0)
    w_rows = jnp.stack(
        [inner_elements(stiff_wterm, basis_values), inner_elements(mass_wterm, basis_values)]
    )
    full_gram = all_sum(arrange(jnp.stack([stiff_part, mass_part]), w_rows, modes))
    total_edges = owned_edges * lax.axis_size("dom")
    return (w_block, full_gram[0] / total_edges, full_gram[1] / total_edges)


def solution(mesh):
    in_specs = (
        P(None, "dom"),
        P(None, "dom"),
        P(None, None, "dom"),
        P(None, None, "dom"),
        P(None, None, "dom"),
        P(None, "dom"),
        P(None, "dom"),
        P(None, "dom"),
        P(None, "dom"),
        P(None, "dom"),
    )
    out_specs = (P(None, "dom"), P(), P())
    return jax.shard_map(shards, mesh=mesh, in_specs=in_specs, out_specs=out_specs, check_vma=False)
```

```python
import jax
import jax.numpy as jnp
from jax import lax
from jax.sharding import PartitionSpec as P

CHEB_DEG = 3
NNODE = 384
LANES = 128


highest = lax.Precision.HIGHEST
OFFSETS = (1, -1, 4, -4, 16, -16)
interval_low = 0.3
interval_high = 1.7
jacobi_weight = 0.7


def from_behind(shard, axis, by):
    length = lax.axis_size(axis)
    return lax.ppermute(shard, axis, [(i, (i + by) % length) for i in range(length)])


def shift_pieces(pieces, offsets):
    length = lax.axis_size("dom")
    out = [None] * len(pieces)
    targets = {}
    for number, offset in enumerate(offsets):
        targets.setdefault(offset % length, []).append(number)
    for offset, numbers in targets.items():
        sizes = [pieces[number].shape[1] for number in numbers]
        moved = from_behind(jnp.concatenate([pieces[number] for number in numbers], axis=1), "dom", offset)
        start = 0
        for number, size in zip(numbers, sizes):
            out[number] = moved[:, start : start + size]
            start += size
    return out


def all_sum(value):
    length = lax.axis_size("dom")
    if length & (length - 1):
        return lax.psum(value, "dom")
    me = lax.axis_index("dom")
    shift = 0
    while (1 << shift) < length:
        bits = 2 if (4 << shift) <= length else 1
        size = 1 << bits
        got = [value] + [
            lax.ppermute(value, "dom", [(i, i ^ (t << shift)) for i in range(length)])
            for t in range(1, size)
        ]
        digit = (me >> shift) & (size - 1)
        ordered = []
        for member in range(size):
            pick = got[0]
            for t in range(1, size):
                pick = jnp.where((member ^ digit) == t, got[t], pick)
            ordered.append(pick)
        while len(ordered) > 1:
            ordered = [ordered[k] + ordered[k + 1] for k in range(0, len(ordered), 2)]
        value = ordered[0]
        shift += bits
    return value


def index_table(index, length):
    groups = -(-length // LANES)
    lo = index % LANES
    hi = index // LANES
    lo_hot = (lo[:, None] == jnp.arange(LANES, dtype=jnp.int32)[None, :]).astype(jnp.float32)
    hi_mask = (hi[None, :] == jnp.arange(groups, dtype=jnp.int32)[:, None]).astype(jnp.float32)
    return lo_hot, hi_mask, length


def gather_cols(values, table, precision=lax.Precision.HIGH):
    lo_hot, hi_mask, length = table
    groups = hi_mask.shape[0]
    rows = values.shape[0]
    padded = jnp.pad(values, ((0, 0), (0, groups * LANES - length)))
    split = padded.reshape(rows, groups, LANES)
    picked = jnp.einsum("rab,nb->ran", split, lo_hot, precision=precision)
    return jnp.sum(picked * hi_mask[None], axis=1)


def scatter_cols(terms, table):
    lo_hot, hi_mask, length = table
    groups = hi_mask.shape[0]
    rows = terms.shape[0]
    spread = terms[:, None, :] * hi_mask[None]
    summed = jnp.einsum("ran,nb->rab", spread, lo_hot, precision=lax.Precision.HIGH)
    return summed.reshape(rows, groups * LANES)[:, :length]


def extend_pieces(values, send_table):
    outgoing = gather_cols(values, send_table)
    ghosts = outgoing.shape[1] // 6
    return [outgoing[:, d * ghosts : (d + 1) * ghosts] for d in range(6)], list(OFFSETS)


def extend_finish(values, moved):
    return jnp.concatenate([values] + moved, axis=1)


def give_back_pieces(extended, send_table):
    owned = send_table[2]
    ghosts = (extended.shape[1] - owned) // 6
    pieces = [extended[:, owned + d * ghosts : owned + (d + 1) * ghosts] for d in range(6)]
    return pieces, [-offset for offset in OFFSETS]


def give_back_finish(extended, moved, send_table):
    owned = send_table[2]
    return extended[:, :owned] + scatter_cols(jnp.concatenate(moved, axis=1), send_table)


def exchange(*groups):
    pieces, offsets, bounds = [], [], []
    flat = len({piece.shape[0] for group_pieces, _ in groups for piece in group_pieces}) > 1
    for group_pieces, group_offsets in groups:
        bounds.append((len(pieces), len(group_pieces)))
        pieces += [piece.reshape(1, -1) if flat else piece for piece in group_pieces]
        offsets += group_offsets
    moved = shift_pieces(pieces, offsets)
    out = []
    for (start, count), (group_pieces, _) in zip(bounds, groups):
        out.append([m.reshape(p.shape) for m, p in zip(moved[start : start + count], group_pieces)])
    return out


def extend(values, send_table):
    (moved,) = exchange(extend_pieces(values, send_table))
    return extend_finish(values, moved)


def give_back(extended, send_table):
    (moved,) = exchange(give_back_pieces(extended, send_table))
    return give_back_finish(extended, moved, send_table)


def element_terms(matrices, values):
    return jnp.sum(matrices[None, :, :, :] * values[:, None, :, :], axis=2)


def inner_elements(left, right):
    return jnp.einsum("cke,dke->cd", left, right, precision=highest)


def arrange(pair_part, row_part, modes):
    mode_mode = pair_part[:, :modes, :modes]
    mode_prev = pair_part[:, :modes, modes:]
    prev_mode = pair_part[:, modes:, :modes]
    prev_prev = pair_part[:, modes:, modes:]
    new_mode = jnp.swapaxes(row_part[:, :, :modes], 1, 2)
    new_prev = jnp.swapaxes(row_part[:, :, 2 * modes :], 1, 2)
    upper = jnp.concatenate([mode_mode, new_mode, mode_prev], axis=2)
    lower = jnp.concatenate([prev_mode, new_prev, prev_prev], axis=2)
    return jnp.concatenate([upper, row_part, lower], axis=1)


def shards(
    x_block,
    p_block,
    stiff_elem,
    mass_elem,
    node_elem,
    elem_edge,
    elem_node,
    send_edge,
    send_node,
    grad_pairs,
):
    modes = x_block.shape[0]
    owned_edges = x_block.shape[1]
    edofs, elements = elem_edge.shape
    ndofs = elem_node.shape[0]
    edge_length = owned_edges + 6 * send_edge.shape[1]
    node_length = NNODE + 6 * send_node.shape[1]

    edge_table = index_table(elem_edge.reshape(-1), edge_length)
    node_table = index_table(elem_node.reshape(-1), node_length)
    send_edge_table = index_table(send_edge.reshape(-1), owned_edges)
    send_node_table = index_table(send_node.reshape(-1), NNODE)
    tails = grad_pairs[0]
    heads = grad_pairs[1]
    grad_table = index_table(jnp.concatenate([heads, tails]), node_length)

    def edge_values(extended):
        return gather_cols(extended, edge_table).reshape(extended.shape[0], edofs, elements)

    def edge_sum(terms):
        return scatter_cols(terms.reshape(terms.shape[0], -1), edge_table)

    pair = jnp.concatenate([x_block, p_block], axis=0)
    node_diag_local = scatter_cols(jnp.einsum("jje->je", node_elem).reshape(1, -1), node_table)
    pair_moved, node_diag_moved = exchange(
        extend_pieces(pair, send_edge_table), give_back_pieces(node_diag_local, send_node_table)
    )
    pair_values = gather_cols(extend_finish(pair, pair_moved), edge_table, highest).reshape(
        2 * modes, edofs, elements
    )
    node_diag = give_back_finish(node_diag_local, node_diag_moved, send_node_table)[0]
    stiff_pair = element_terms(stiff_elem, pair_values)
    mass_pair = element_terms(mass_elem, pair_values)
    edge_diag_terms = jnp.einsum("jje->je", stiff_elem)[None]
    images = give_back(
        edge_sum(jnp.concatenate([stiff_pair[:modes], mass_pair[:modes], edge_diag_terms], axis=0)),
        send_edge_table,
    )
    stiff_x = images[:modes]
    mass_x = images[modes : 2 * modes]
    edge_diag = images[2 * modes]
    stiff_part = inner_elements(pair_values, stiff_pair)
    mass_part = inner_elements(pair_values, mass_pair)
    numerator, denominator = all_sum(
        jnp.stack([jnp.diagonal(stiff_part)[:modes], jnp.diagonal(mass_part)[:modes]])
    )
    quotient = numerator / denominator
    residual = stiff_x - quotient[:, None] * mass_x

    def stiff_image(vectors):
        values = edge_values(extend(vectors, send_edge_table))
        return give_back(edge_sum(element_terms(stiff_elem, values)), send_edge_table)

    center = 0.5 * (interval_high + interval_low)
    spread = 0.5 * (interval_high - interval_low)
    sigma = center / spread
    rho_now = 1.0 / sigma
    step_dir = residual / (center * edge_diag)
    smooth = step_dir
    for turn in range(CHEB_DEG - 1):
        rho_next = 1.0 / (2.0 * sigma - rho_now)
        remain = residual - stiff_image(smooth)
        step_dir = rho_next * rho_now * step_dir + 2.0 * rho_next / spread * remain / edge_diag
        smooth = smooth + step_dir
        rho_now = rho_next
    after = residual - stiff_image(smooth)
    gathered_res = scatter_cols(jnp.concatenate([after, -after], axis=1), grad_table)
    nodal_res = give_back(gathered_res, send_node_table)
    first = jacobi_weight * nodal_res / node_diag
    first_values = gather_cols(extend(first, send_node_table), node_table).reshape(modes, ndofs, elements)
    node_image = give_back(
        scatter_cols(element_terms(node_elem, first_values).reshape(modes, -1), node_table),
        send_node_table,
    )
    second = first + jacobi_weight * (nodal_res - node_image) / node_diag
    ends = gather_cols(extend(second, send_node_table), grad_table)
    w_block = smooth + ends[:, :owned_edges] - ends[:, owned_edges:]
    w_values = edge_values(extend(w_block, send_edge_table))
    stiff_wterm = element_terms(stiff_elem, w_values)
    mass_wterm = element_terms(mass_elem, w_values)
    basis_values = jnp.concatenate([pair_values[:modes], w_values, pair_values[modes:]], axis=0)
    w_rows = jnp.stack(
        [inner_elements(stiff_wterm, basis_values), inner_elements(mass_wterm, basis_values)]
    )
    full_gram = all_sum(arrange(jnp.stack([stiff_part, mass_part]), w_rows, modes))
    total_edges = owned_edges * lax.axis_size("dom")
    return (w_block, full_gram[0] / total_edges, full_gram[1] / total_edges)


def solution(mesh):
    in_specs = (
        P(None, "dom"),
        P(None, "dom"),
        P(None, None, "dom"),
        P(None, None, "dom"),
        P(None, None, "dom"),
        P(None, "dom"),
        P(None, "dom"),
        P(None, "dom"),
        P(None, "dom"),
        P(None, "dom"),
    )
    out_specs = (P(None, "dom"), P(), P())
    return jax.shard_map(shards, mesh=mesh, in_specs=in_specs, out_specs=out_specs, check_vma=False)
```

```python
import jax
import jax.numpy as jnp
from jax import lax
from jax.sharding import PartitionSpec as P

CHEB_DEG = 3
NNODE = 384
LANES = 128


highest = lax.Precision.HIGHEST
OFFSETS = (1, -1, 4, -4, 16, -16)
interval_low = 0.3
interval_high = 1.7
jacobi_weight = 0.7


def from_behind(shard, axis, by):
    length = lax.axis_size(axis)
    return lax.ppermute(shard, axis, [(i, (i + by) % length) for i in range(length)])


def shift_pieces(pieces, offsets):
    length = lax.axis_size("dom")
    out = [None] * len(pieces)
    targets = {}
    for number, offset in enumerate(offsets):
        targets.setdefault(offset % length, []).append(number)
    for offset, numbers in targets.items():
        sizes = [pieces[number].shape[1] for number in numbers]
        moved = from_behind(jnp.concatenate([pieces[number] for number in numbers], axis=1), "dom", offset)
        start = 0
        for number, size in zip(numbers, sizes):
            out[number] = moved[:, start : start + size]
            start += size
    return out


def all_sum(value):
    length = lax.axis_size("dom")
    if length & (length - 1):
        return lax.psum(value, "dom")
    me = lax.axis_index("dom")
    shift = 0
    while (1 << shift) < length:
        bits = 2 if (4 << shift) <= length else 1
        size = 1 << bits
        got = [value] + [
            lax.ppermute(value, "dom", [(i, i ^ (t << shift)) for i in range(length)])
            for t in range(1, size)
        ]
        digit = (me >> shift) & (size - 1)
        ordered = []
        for member in range(size):
            pick = got[0]
            for t in range(1, size):
                pick = jnp.where((member ^ digit) == t, got[t], pick)
            ordered.append(pick)
        while len(ordered) > 1:
            ordered = [ordered[k] + ordered[k + 1] for k in range(0, len(ordered), 2)]
        value = ordered[0]
        shift += bits
    return value


def index_table(index, length):
    groups = -(-length // LANES)
    lo = index % LANES
    hi = index // LANES
    lo_hot = (lo[:, None] == jnp.arange(LANES, dtype=jnp.int32)[None, :]).astype(jnp.float32)
    hi_mask = (hi[None, :] == jnp.arange(groups, dtype=jnp.int32)[:, None]).astype(jnp.float32)
    lo_hot_t = (jnp.arange(LANES, dtype=jnp.int32)[:, None] == lo[None, :]).astype(jnp.float32)
    return lo_hot, hi_mask, length, lo_hot_t


def gather_cols(values, table, precision=lax.Precision.HIGH):
    lo_hot, hi_mask, length, lo_hot_t = table
    groups = hi_mask.shape[0]
    rows = values.shape[0]
    padded = jnp.pad(values, ((0, 0), (0, groups * LANES - length)))
    split = padded.reshape(rows, groups, LANES)
    picked = jnp.einsum("rab,bn->ran", split, lo_hot_t, precision=precision)
    return jnp.sum(picked * hi_mask[None], axis=1)


def scatter_cols(terms, table):
    lo_hot, hi_mask, length, lo_hot_t = table
    groups = hi_mask.shape[0]
    rows = terms.shape[0]
    spread = terms[:, None, :] * hi_mask[None]
    summed = jnp.einsum("ran,nb->rab", spread, lo_hot, precision=lax.Precision.HIGH)
    return summed.reshape(rows, groups * LANES)[:, :length]


def extend_pieces(values, send_table):
    outgoing = gather_cols(values, send_table)
    ghosts = outgoing.shape[1] // 6
    return [outgoing[:, d * ghosts : (d + 1) * ghosts] for d in range(6)], list(OFFSETS)


def extend_finish(values, moved):
    return jnp.concatenate([values] + moved, axis=1)


def give_back_pieces(extended, send_table):
    owned = send_table[2]
    ghosts = (extended.shape[1] - owned) // 6
    pieces = [extended[:, owned + d * ghosts : owned + (d + 1) * ghosts] for d in range(6)]
    return pieces, [-offset for offset in OFFSETS]


def give_back_finish(extended, moved, send_table):
    owned = send_table[2]
    return extended[:, :owned] + scatter_cols(jnp.concatenate(moved, axis=1), send_table)


def exchange(*groups):
    pieces, offsets, bounds = [], [], []
    flat = len({piece.shape[0] for group_pieces, _ in groups for piece in group_pieces}) > 1
    for group_pieces, group_offsets in groups:
        bounds.append((len(pieces), len(group_pieces)))
        pieces += [piece.reshape(1, -1) if flat else piece for piece in group_pieces]
        offsets += group_offsets
    moved = shift_pieces(pieces, offsets)
    out = []
    for (start, count), (group_pieces, _) in zip(bounds, groups):
        out.append([m.reshape(p.shape) for m, p in zip(moved[start : start + count], group_pieces)])
    return out


def extend(values, send_table):
    (moved,) = exchange(extend_pieces(values, send_table))
    return extend_finish(values, moved)


def give_back(extended, send_table):
    (moved,) = exchange(give_back_pieces(extended, send_table))
    return give_back_finish(extended, moved, send_table)


def element_terms(matrices, values):
    return jnp.sum(matrices[None, :, :, :] * values[:, None, :, :], axis=2)


def inner_elements(left, right):
    return jnp.einsum("cke,dke->cd", left, right, precision=highest)


def arrange(pair_part, row_part, modes):
    mode_mode = pair_part[:, :modes, :modes]
    mode_prev = pair_part[:, :modes, modes:]
    prev_mode = pair_part[:, modes:, :modes]
    prev_prev = pair_part[:, modes:, modes:]
    new_mode = jnp.swapaxes(row_part[:, :, :modes], 1, 2)
    new_prev = jnp.swapaxes(row_part[:, :, 2 * modes :], 1, 2)
    upper = jnp.concatenate([mode_mode, new_mode, mode_prev], axis=2)
    lower = jnp.concatenate([prev_mode, new_prev, prev_prev], axis=2)
    return jnp.concatenate([upper, row_part, lower], axis=1)


def shards(
    x_block,
    p_block,
    stiff_elem,
    mass_elem,
    node_elem,
    elem_edge,
    elem_node,
    send_edge,
    send_node,
    grad_pairs,
):
    modes = x_block.shape[0]
    owned_edges = x_block.shape[1]
    edofs, elements = elem_edge.shape
    ndofs = elem_node.shape[0]
    edge_length = owned_edges + 6 * send_edge.shape[1]
    node_length = NNODE + 6 * send_node.shape[1]

    edge_table = index_table(elem_edge.reshape(-1), edge_length)
    node_table = index_table(elem_node.reshape(-1), node_length)
    send_edge_table = index_table(send_edge.reshape(-1), owned_edges)
    send_node_table = index_table(send_node.reshape(-1), NNODE)
    tails = grad_pairs[0]
    heads = grad_pairs[1]
    grad_table = index_table(jnp.concatenate([heads, tails]), node_length)

    def edge_values(extended):
        return gather_cols(extended, edge_table).reshape(extended.shape[0], edofs, elements)

    def edge_sum(terms):
        return scatter_cols(terms.reshape(terms.shape[0], -1), edge_table)

    pair = jnp.concatenate([x_block, p_block], axis=0)
    node_diag_local = scatter_cols(jnp.einsum("jje->je", node_elem).reshape(1, -1), node_table)
    pair_moved, node_diag_moved = exchange(
        extend_pieces(pair, send_edge_table), give_back_pieces(node_diag_local, send_node_table)
    )
    pair_values = gather_cols(extend_finish(pair, pair_moved), edge_table, highest).reshape(
        2 * modes, edofs, elements
    )
    node_diag = give_back_finish(node_diag_local, node_diag_moved, send_node_table)[0]
    stiff_pair = element_terms(stiff_elem, pair_values)
    mass_pair = element_terms(mass_elem, pair_values)
    edge_diag_terms = jnp.einsum("jje->je", stiff_elem)[None]
    images = give_back(
        edge_sum(jnp.concatenate([stiff_pair[:modes], mass_pair[:modes], edge_diag_terms], axis=0)),
        send_edge_table,
    )
    stiff_x = images[:modes]
    mass_x = images[modes : 2 * modes]
    edge_diag = images[2 * modes]
    stiff_part = inner_elements(pair_values, stiff_pair)
    mass_part = inner_elements(pair_values, mass_pair)
    numerator, denominator = all_sum(
        jnp.stack([jnp.diagonal(stiff_part)[:modes], jnp.diagonal(mass_part)[:modes]])
    )
    quotient = numerator / denominator
    residual = stiff_x - quotient[:, None] * mass_x

    def stiff_image(vectors):
        values = edge_values(extend(vectors, send_edge_table))
        return give_back(edge_sum(element_terms(stiff_elem, values)), send_edge_table)

    center = 0.5 * (interval_high + interval_low)
    spread = 0.5 * (interval_high - interval_low)
    sigma = center / spread
    rho_now = 1.0 / sigma
    step_dir = residual / (center * edge_diag)
    smooth = step_dir
    for turn in range(CHEB_DEG - 1):
        rho_next = 1.0 / (2.0 * sigma - rho_now)
        remain = residual - stiff_image(smooth)
        step_dir = rho_next * rho_now * step_dir + 2.0 * rho_next / spread * remain / edge_diag
        smooth = smooth + step_dir
        rho_now = rho_next
    after = residual - stiff_image(smooth)
    gathered_res = scatter_cols(jnp.concatenate([after, -after], axis=1), grad_table)
    nodal_res = give_back(gathered_res, send_node_table)
    first = jacobi_weight * nodal_res / node_diag
    first_values = gather_cols(extend(first, send_node_table), node_table).reshape(modes, ndofs, elements)
    node_image = give_back(
        scatter_cols(element_terms(node_elem, first_values).reshape(modes, -1), node_table),
        send_node_table,
    )
    second = first + jacobi_weight * (nodal_res - node_image) / node_diag
    ends = gather_cols(extend(second, send_node_table), grad_table)
    w_block = smooth + ends[:, :owned_edges] - ends[:, owned_edges:]
    w_values = edge_values(extend(w_block, send_edge_table))
    stiff_wterm = element_terms(stiff_elem, w_values)
    mass_wterm = element_terms(mass_elem, w_values)
    basis_values = jnp.concatenate([pair_values[:modes], w_values, pair_values[modes:]], axis=0)
    w_rows = jnp.stack(
        [inner_elements(stiff_wterm, basis_values), inner_elements(mass_wterm, basis_values)]
    )
    full_gram = all_sum(arrange(jnp.stack([stiff_part, mass_part]), w_rows, modes))
    total_edges = owned_edges * lax.axis_size("dom")
    return (w_block, full_gram[0] / total_edges, full_gram[1] / total_edges)


def solution(mesh):
    in_specs = (
        P(None, "dom"),
        P(None, "dom"),
        P(None, None, "dom"),
        P(None, None, "dom"),
        P(None, None, "dom"),
        P(None, "dom"),
        P(None, "dom"),
        P(None, "dom"),
        P(None, "dom"),
        P(None, "dom"),
    )
    out_specs = (P(None, "dom"), P(), P())
    return jax.shard_map(shards, mesh=mesh, in_specs=in_specs, out_specs=out_specs, check_vma=False)
```

```python
import jax
import jax.numpy as jnp
from jax import lax
from jax.sharding import PartitionSpec as P

CHEB_DEG = 3
NNODE = 384
LANES = 128


highest = lax.Precision.HIGHEST
OFFSETS = (1, -1, 4, -4, 16, -16)
interval_low = 0.3
interval_high = 1.7
jacobi_weight = 0.7


def from_behind(shard, axis, by):
    length = lax.axis_size(axis)
    return lax.ppermute(shard, axis, [(i, (i + by) % length) for i in range(length)])


def shift_pieces(pieces, offsets):
    length = lax.axis_size("dom")
    out = [None] * len(pieces)
    targets = {}
    for number, offset in enumerate(offsets):
        targets.setdefault(offset % length, []).append(number)
    for offset, numbers in targets.items():
        sizes = [pieces[number].shape[1] for number in numbers]
        moved = from_behind(jnp.concatenate([pieces[number] for number in numbers], axis=1), "dom", offset)
        start = 0
        for number, size in zip(numbers, sizes):
            out[number] = moved[:, start : start + size]
            start += size
    return out


def all_sum(value):
    length = lax.axis_size("dom")
    if length & (length - 1):
        return lax.psum(value, "dom")
    me = lax.axis_index("dom")
    shift = 0
    while (1 << shift) < length:
        bits = 2 if (4 << shift) <= length else 1
        size = 1 << bits
        got = [value] + [
            lax.ppermute(value, "dom", [(i, i ^ (t << shift)) for i in range(length)])
            for t in range(1, size)
        ]
        digit = (me >> shift) & (size - 1)
        ordered = []
        for member in range(size):
            pick = got[0]
            for t in range(1, size):
                pick = jnp.where((member ^ digit) == t, got[t], pick)
            ordered.append(pick)
        while len(ordered) > 1:
            ordered = [ordered[k] + ordered[k + 1] for k in range(0, len(ordered), 2)]
        value = ordered[0]
        shift += bits
    return value


def index_table(index, length):
    groups = -(-length // LANES)
    lo = index % LANES
    hi = index // LANES
    lo_hot = (lo[:, None] == jnp.arange(LANES, dtype=jnp.int32)[None, :]).astype(jnp.float32)
    hi_mask = (hi[None, :] == jnp.arange(groups, dtype=jnp.int32)[:, None]).astype(jnp.float32)
    lo_hot_t = (jnp.arange(LANES, dtype=jnp.int32)[:, None] == lo[None, :]).astype(jnp.float32)
    return lo_hot, hi_mask, length, lo_hot_t


def gather_cols(values, table, precision=highest):
    lo_hot, hi_mask, length, lo_hot_t = table
    groups = hi_mask.shape[0]
    rows = values.shape[0]
    padded = jnp.pad(values, ((0, 0), (0, groups * LANES - length)))
    split = padded.reshape(rows, groups, LANES)
    picked = jnp.einsum("rab,bn->ran", split, lo_hot_t, precision=precision)
    return jnp.sum(picked * hi_mask[None], axis=1)


def scatter_cols(terms, table):
    lo_hot, hi_mask, length, lo_hot_t = table
    groups = hi_mask.shape[0]
    rows = terms.shape[0]
    spread = terms[:, None, :] * hi_mask[None]
    summed = jnp.einsum("ran,nb->rab", spread, lo_hot, precision=highest)
    return summed.reshape(rows, groups * LANES)[:, :length]


def extend_pieces(values, send_table):
    outgoing = gather_cols(values, send_table)
    ghosts = outgoing.shape[1] // 6
    return [outgoing[:, d * ghosts : (d + 1) * ghosts] for d in range(6)], list(OFFSETS)


def extend_finish(values, moved):
    return jnp.concatenate([values] + moved, axis=1)


def give_back_pieces(extended, send_table):
    owned = send_table[2]
    ghosts = (extended.shape[1] - owned) // 6
    pieces = [extended[:, owned + d * ghosts : owned + (d + 1) * ghosts] for d in range(6)]
    return pieces, [-offset for offset in OFFSETS]


def give_back_finish(extended, moved, send_table):
    owned = send_table[2]
    return extended[:, :owned] + scatter_cols(jnp.concatenate(moved, axis=1), send_table)


def exchange(*groups):
    pieces, offsets, bounds = [], [], []
    flat = len({piece.shape[0] for group_pieces, _ in groups for piece in group_pieces}) > 1
    for group_pieces, group_offsets in groups:
        bounds.append((len(pieces), len(group_pieces)))
        pieces += [piece.reshape(1, -1) if flat else piece for piece in group_pieces]
        offsets += group_offsets
    moved = shift_pieces(pieces, offsets)
    out = []
    for (start, count), (group_pieces, _) in zip(bounds, groups):
        out.append([m.reshape(p.shape) for m, p in zip(moved[start : start + count], group_pieces)])
    return out


def extend(values, send_table):
    (moved,) = exchange(extend_pieces(values, send_table))
    return extend_finish(values, moved)


def give_back(extended, send_table):
    (moved,) = exchange(give_back_pieces(extended, send_table))
    return give_back_finish(extended, moved, send_table)


def element_terms(matrices, values):
    return jnp.sum(matrices[None, :, :, :] * values[:, None, :, :], axis=2)


def inner_elements(left, right):
    return jnp.einsum("cke,dke->cd", left, right, precision=highest)


def arrange(pair_part, row_part, modes):
    mode_mode = pair_part[:, :modes, :modes]
    mode_prev = pair_part[:, :modes, modes:]
    prev_mode = pair_part[:, modes:, :modes]
    prev_prev = pair_part[:, modes:, modes:]
    new_mode = jnp.swapaxes(row_part[:, :, :modes], 1, 2)
    new_prev = jnp.swapaxes(row_part[:, :, 2 * modes :], 1, 2)
    upper = jnp.concatenate([mode_mode, new_mode, mode_prev], axis=2)
    lower = jnp.concatenate([prev_mode, new_prev, prev_prev], axis=2)
    return jnp.concatenate([upper, row_part, lower], axis=1)


def shards(
    x_block,
    p_block,
    stiff_elem,
    mass_elem,
    node_elem,
    elem_edge,
    elem_node,
    send_edge,
    send_node,
    grad_pairs,
):
    modes = x_block.shape[0]
    owned_edges = x_block.shape[1]
    edofs, elements = elem_edge.shape
    ndofs = elem_node.shape[0]
    edge_length = owned_edges + 6 * send_edge.shape[1]
    node_length = NNODE + 6 * send_node.shape[1]

    edge_table = index_table(elem_edge.reshape(-1), edge_length)
    node_table = index_table(elem_node.reshape(-1), node_length)
    send_edge_table = index_table(send_edge.reshape(-1), owned_edges)
    send_node_table = index_table(send_node.reshape(-1), NNODE)
    tails = grad_pairs[0]
    heads = grad_pairs[1]
    grad_table = index_table(jnp.concatenate([heads, tails]), node_length)

    def edge_values(extended):
        return gather_cols(extended, edge_table).reshape(extended.shape[0], edofs, elements)

    def edge_sum(terms):
        return scatter_cols(terms.reshape(terms.shape[0], -1), edge_table)

    pair = jnp.concatenate([x_block, p_block], axis=0)
    node_diag_local = scatter_cols(jnp.einsum("jje->je", node_elem).reshape(1, -1), node_table)
    pair_moved, node_diag_moved = exchange(
        extend_pieces(pair, send_edge_table), give_back_pieces(node_diag_local, send_node_table)
    )
    pair_values = edge_values(extend_finish(pair, pair_moved))
    node_diag = give_back_finish(node_diag_local, node_diag_moved, send_node_table)[0]
    stiff_pair = element_terms(stiff_elem, pair_values)
    mass_pair = element_terms(mass_elem, pair_values)
    edge_diag_terms = jnp.einsum("jje->je", stiff_elem)[None]
    images = give_back(
        edge_sum(jnp.concatenate([stiff_pair[:modes], mass_pair[:modes], edge_diag_terms], axis=0)),
        send_edge_table,
    )
    stiff_x = images[:modes]
    mass_x = images[modes : 2 * modes]
    edge_diag = images[2 * modes]
    stiff_part = inner_elements(pair_values, stiff_pair)
    mass_part = inner_elements(pair_values, mass_pair)
    numerator, denominator = all_sum(
        jnp.stack([jnp.diagonal(stiff_part)[:modes], jnp.diagonal(mass_part)[:modes]])
    )
    quotient = numerator / denominator
    residual = stiff_x - quotient[:, None] * mass_x

    def stiff_image(vectors):
        values = edge_values(extend(vectors, send_edge_table))
        return give_back(edge_sum(element_terms(stiff_elem, values)), send_edge_table)

    center = 0.5 * (interval_high + interval_low)
    spread = 0.5 * (interval_high - interval_low)
    sigma = center / spread
    rho_now = 1.0 / sigma
    step_dir = residual / (center * edge_diag)
    smooth = step_dir
    for turn in range(CHEB_DEG - 1):
        rho_next = 1.0 / (2.0 * sigma - rho_now)
        remain = residual - stiff_image(smooth)
        step_dir = rho_next * rho_now * step_dir + 2.0 * rho_next / spread * remain / edge_diag
        smooth = smooth + step_dir
        rho_now = rho_next
    after = residual - stiff_image(smooth)
    gathered_res = scatter_cols(jnp.concatenate([after, -after], axis=1), grad_table)
    nodal_res = give_back(gathered_res, send_node_table)
    first = jacobi_weight * nodal_res / node_diag
    first_values = gather_cols(extend(first, send_node_table), node_table).reshape(modes, ndofs, elements)
    node_image = give_back(
        scatter_cols(element_terms(node_elem, first_values).reshape(modes, -1), node_table),
        send_node_table,
    )
    second = first + jacobi_weight * (nodal_res - node_image) / node_diag
    ends = gather_cols(extend(second, send_node_table), grad_table)
    w_block = smooth + ends[:, :owned_edges] - ends[:, owned_edges:]
    w_values = edge_values(extend(w_block, send_edge_table))
    stiff_wterm = element_terms(stiff_elem, w_values)
    mass_wterm = element_terms(mass_elem, w_values)
    basis_values = jnp.concatenate([pair_values[:modes], w_values, pair_values[modes:]], axis=0)
    w_rows = jnp.stack(
        [inner_elements(stiff_wterm, basis_values), inner_elements(mass_wterm, basis_values)]
    )
    full_gram = all_sum(arrange(jnp.stack([stiff_part, mass_part]), w_rows, modes))
    total_edges = owned_edges * lax.axis_size("dom")
    return (w_block, full_gram[0] / total_edges, full_gram[1] / total_edges)


def solution(mesh):
    in_specs = (
        P(None, "dom"),
        P(None, "dom"),
        P(None, None, "dom"),
        P(None, None, "dom"),
        P(None, None, "dom"),
        P(None, "dom"),
        P(None, "dom"),
        P(None, "dom"),
        P(None, "dom"),
        P(None, "dom"),
    )
    out_specs = (P(None, "dom"), P(), P())
    return jax.shard_map(shards, mesh=mesh, in_specs=in_specs, out_specs=out_specs, check_vma=False)
```

```python
import jax
import jax.numpy as jnp
from jax import lax
from jax.sharding import PartitionSpec as P

CHEB_DEG = 3
NNODE = 384
LANES = 128


highest = lax.Precision.HIGHEST
OFFSETS = (1, -1, 4, -4, 16, -16)
interval_low = 0.3
interval_high = 1.7
jacobi_weight = 0.7


def from_behind(shard, axis, by):
    length = lax.axis_size(axis)
    return lax.ppermute(shard, axis, [(i, (i + by) % length) for i in range(length)])


def shift_pieces(pieces, offsets):
    length = lax.axis_size("dom")
    out = [None] * len(pieces)
    targets = {}
    for number, offset in enumerate(offsets):
        targets.setdefault(offset % length, []).append(number)
    for offset, numbers in targets.items():
        sizes = [pieces[number].shape[1] for number in numbers]
        moved = from_behind(jnp.concatenate([pieces[number] for number in numbers], axis=1), "dom", offset)
        start = 0
        for number, size in zip(numbers, sizes):
            out[number] = moved[:, start : start + size]
            start += size
    return out


def all_sum(value):
    length = lax.axis_size("dom")
    if length & (length - 1):
        return lax.psum(value, "dom")
    me = lax.axis_index("dom")
    shift = 0
    while (1 << shift) < length:
        bits = 2 if (4 << shift) <= length else 1
        size = 1 << bits
        got = [value] + [
            lax.ppermute(value, "dom", [(i, i ^ (t << shift)) for i in range(length)])
            for t in range(1, size)
        ]
        digit = (me >> shift) & (size - 1)
        ordered = []
        for member in range(size):
            pick = got[0]
            for t in range(1, size):
                pick = jnp.where((member ^ digit) == t, got[t], pick)
            ordered.append(pick)
        while len(ordered) > 1:
            ordered = [ordered[k] + ordered[k + 1] for k in range(0, len(ordered), 2)]
        value = ordered[0]
        shift += bits
    return value


def index_table(index, length):
    groups = -(-length // LANES)
    lo = index % LANES
    hi = index // LANES
    lo_hot = (lo[:, None] == jnp.arange(LANES, dtype=jnp.int32)[None, :]).astype(jnp.float32)
    hi_mask = (hi[None, :] == jnp.arange(groups, dtype=jnp.int32)[:, None]).astype(jnp.float32)
    lo_hot_t = (jnp.arange(LANES, dtype=jnp.int32)[:, None] == lo[None, :]).astype(jnp.float32)
    return lo_hot, hi_mask, length, lo_hot_t


def gather_cols(values, table, precision=lax.Precision.HIGH):
    lo_hot, hi_mask, length, lo_hot_t = table
    groups = hi_mask.shape[0]
    rows = values.shape[0]
    padded = jnp.pad(values, ((0, 0), (0, groups * LANES - length)))
    split = padded.reshape(rows, groups, LANES)
    picked = jnp.einsum("rab,bn->ran", split, lo_hot_t, precision=precision)
    return jnp.sum(picked * hi_mask[None], axis=1)


def scatter_cols(terms, table):
    lo_hot, hi_mask, length, lo_hot_t = table
    groups = hi_mask.shape[0]
    rows = terms.shape[0]
    spread = terms[:, None, :] * hi_mask[None]
    summed = jnp.einsum("ran,nb->rab", spread, lo_hot, precision=lax.Precision.HIGH)
    return summed.reshape(rows, groups * LANES)[:, :length]


def extend_pieces(values, send_table):
    outgoing = gather_cols(values, send_table)
    ghosts = outgoing.shape[1] // 6
    return [outgoing[:, d * ghosts : (d + 1) * ghosts] for d in range(6)], list(OFFSETS)


def extend_finish(values, moved):
    return jnp.concatenate([values] + moved, axis=1)


def give_back_pieces(extended, send_table):
    owned = send_table[2]
    ghosts = (extended.shape[1] - owned) // 6
    pieces = [extended[:, owned + d * ghosts : owned + (d + 1) * ghosts] for d in range(6)]
    return pieces, [-offset for offset in OFFSETS]


def give_back_finish(extended, moved, send_table):
    owned = send_table[2]
    return extended[:, :owned] + scatter_cols(jnp.concatenate(moved, axis=1), send_table)


def exchange(*groups):
    pieces, offsets, bounds = [], [], []
    rows = max(piece.shape[0] for group_pieces, _ in groups for piece in group_pieces)
    for group_pieces, group_offsets in groups:
        bounds.append((len(pieces), len(group_pieces)))
        pieces += [jnp.pad(piece, ((0, rows - piece.shape[0]), (0, 0))) for piece in group_pieces]
        offsets += group_offsets
    moved = shift_pieces(pieces, offsets)
    out = []
    for (start, count), (group_pieces, _) in zip(bounds, groups):
        out.append([m[: p.shape[0]] for m, p in zip(moved[start : start + count], group_pieces)])
    return out


def extend(values, send_table):
    (moved,) = exchange(extend_pieces(values, send_table))
    return extend_finish(values, moved)


def give_back(extended, send_table):
    (moved,) = exchange(give_back_pieces(extended, send_table))
    return give_back_finish(extended, moved, send_table)


def element_terms(matrices, values):
    return jnp.sum(matrices[None, :, :, :] * values[:, None, :, :], axis=2)


def inner_elements(left, right):
    return jnp.einsum("cke,dke->cd", left, right, precision=highest)


def arrange(pair_part, row_part, modes):
    mode_mode = pair_part[:, :modes, :modes]
    mode_prev = pair_part[:, :modes, modes:]
    prev_mode = pair_part[:, modes:, :modes]
    prev_prev = pair_part[:, modes:, modes:]
    new_mode = jnp.swapaxes(row_part[:, :, :modes], 1, 2)
    new_prev = jnp.swapaxes(row_part[:, :, 2 * modes :], 1, 2)
    upper = jnp.concatenate([mode_mode, new_mode, mode_prev], axis=2)
    lower = jnp.concatenate([prev_mode, new_prev, prev_prev], axis=2)
    return jnp.concatenate([upper, row_part, lower], axis=1)


def shards(
    x_block,
    p_block,
    stiff_elem,
    mass_elem,
    node_elem,
    elem_edge,
    elem_node,
    send_edge,
    send_node,
    grad_pairs,
):
    modes = x_block.shape[0]
    owned_edges = x_block.shape[1]
    edofs, elements = elem_edge.shape
    ndofs = elem_node.shape[0]
    edge_length = owned_edges + 6 * send_edge.shape[1]
    node_length = NNODE + 6 * send_node.shape[1]

    edge_table = index_table(elem_edge.reshape(-1), edge_length)
    node_table = index_table(elem_node.reshape(-1), node_length)
    send_edge_table = index_table(send_edge.reshape(-1), owned_edges)
    send_node_table = index_table(send_node.reshape(-1), NNODE)
    tails = grad_pairs[0]
    heads = grad_pairs[1]
    grad_table = index_table(jnp.concatenate([heads, tails]), node_length)

    def edge_values(extended):
        return gather_cols(extended, edge_table).reshape(extended.shape[0], edofs, elements)

    def edge_sum(terms):
        return scatter_cols(terms.reshape(terms.shape[0], -1), edge_table)

    pair = jnp.concatenate([x_block, p_block], axis=0)
    node_diag_local = scatter_cols(jnp.einsum("jje->je", node_elem).reshape(1, -1), node_table)
    pair_moved, node_diag_moved = exchange(
        extend_pieces(pair, send_edge_table), give_back_pieces(node_diag_local, send_node_table)
    )
    pair_values = gather_cols(extend_finish(pair, pair_moved), edge_table, highest).reshape(
        2 * modes, edofs, elements
    )
    node_diag = give_back_finish(node_diag_local, node_diag_moved, send_node_table)[0]
    stiff_pair = element_terms(stiff_elem, pair_values)
    mass_pair = element_terms(mass_elem, pair_values)
    edge_diag_terms = jnp.einsum("jje->je", stiff_elem)[None]
    images = give_back(
        edge_sum(jnp.concatenate([stiff_pair[:modes], mass_pair[:modes], edge_diag_terms], axis=0)),
        send_edge_table,
    )
    stiff_x = images[:modes]
    mass_x = images[modes : 2 * modes]
    edge_diag = images[2 * modes]
    stiff_part = inner_elements(pair_values, stiff_pair)
    mass_part = inner_elements(pair_values, mass_pair)
    numerator, denominator = all_sum(
        jnp.stack([jnp.diagonal(stiff_part)[:modes], jnp.diagonal(mass_part)[:modes]])
    )
    quotient = numerator / denominator
    residual = stiff_x - quotient[:, None] * mass_x

    def stiff_image(vectors):
        values = edge_values(extend(vectors, send_edge_table))
        return give_back(edge_sum(element_terms(stiff_elem, values)), send_edge_table)

    center = 0.5 * (interval_high + interval_low)
    spread = 0.5 * (interval_high - interval_low)
    sigma = center / spread
    rho_now = 1.0 / sigma
    step_dir = residual / (center * edge_diag)
    smooth = step_dir
    for turn in range(CHEB_DEG - 1):
        rho_next = 1.0 / (2.0 * sigma - rho_now)
        remain = residual - stiff_image(smooth)
        step_dir = rho_next * rho_now * step_dir + 2.0 * rho_next / spread * remain / edge_diag
        smooth = smooth + step_dir
        rho_now = rho_next
    after = residual - stiff_image(smooth)
    gathered_res = scatter_cols(jnp.concatenate([after, -after], axis=1), grad_table)
    nodal_res = give_back(gathered_res, send_node_table)
    first = jacobi_weight * nodal_res / node_diag
    first_values = gather_cols(extend(first, send_node_table), node_table).reshape(modes, ndofs, elements)
    node_image = give_back(
        scatter_cols(element_terms(node_elem, first_values).reshape(modes, -1), node_table),
        send_node_table,
    )
    second = first + jacobi_weight * (nodal_res - node_image) / node_diag
    ends = gather_cols(extend(second, send_node_table), grad_table)
    w_block = smooth + ends[:, :owned_edges] - ends[:, owned_edges:]
    w_values = edge_values(extend(w_block, send_edge_table))
    stiff_wterm = element_terms(stiff_elem, w_values)
    mass_wterm = element_terms(mass_elem, w_values)
    basis_values = jnp.concatenate([pair_values[:modes], w_values, pair_values[modes:]], axis=0)
    w_rows = jnp.stack(
        [inner_elements(stiff_wterm, basis_values), inner_elements(mass_wterm, basis_values)]
    )
    full_gram = all_sum(arrange(jnp.stack([stiff_part, mass_part]), w_rows, modes))
    total_edges = owned_edges * lax.axis_size("dom")
    return (w_block, full_gram[0] / total_edges, full_gram[1] / total_edges)


def solution(mesh):
    in_specs = (
        P(None, "dom"),
        P(None, "dom"),
        P(None, None, "dom"),
        P(None, None, "dom"),
        P(None, None, "dom"),
        P(None, "dom"),
        P(None, "dom"),
        P(None, "dom"),
        P(None, "dom"),
        P(None, "dom"),
    )
    out_specs = (P(None, "dom"), P(), P())
    return jax.shard_map(shards, mesh=mesh, in_specs=in_specs, out_specs=out_specs, check_vma=False)
```

```python
import jax
import jax.numpy as jnp
from jax import lax
from jax.sharding import PartitionSpec as P

CHEB_DEG = 3
NNODE = 384
LANES = 128


highest = lax.Precision.HIGHEST
OFFSETS = (1, -1, 4, -4, 16, -16)
interval_low = 0.3
interval_high = 1.7
jacobi_weight = 0.7


def from_behind(shard, axis, by):
    length = lax.axis_size(axis)
    return lax.ppermute(shard, axis, [(i, (i + by) % length) for i in range(length)])


def shift_pieces(pieces, offsets):
    length = lax.axis_size("dom")
    out = [None] * len(pieces)
    targets = {}
    for number, offset in enumerate(offsets):
        targets.setdefault(offset % length, []).append(number)
    for offset, numbers in targets.items():
        sizes = [pieces[number].shape[1] for number in numbers]
        moved = from_behind(jnp.concatenate([pieces[number] for number in numbers], axis=1), "dom", offset)
        start = 0
        for number, size in zip(numbers, sizes):
            out[number] = moved[:, start : start + size]
            start += size
    return out


def all_sum(value):
    length = lax.axis_size("dom")
    if length & (length - 1):
        return lax.psum(value, "dom")
    me = lax.axis_index("dom")
    shift = 0
    while (1 << shift) < length:
        bits = 2 if (4 << shift) <= length else 1
        size = 1 << bits
        got = [value] + [
            lax.ppermute(value, "dom", [(i, i ^ (t << shift)) for i in range(length)])
            for t in range(1, size)
        ]
        digit = (me >> shift) & (size - 1)
        ordered = []
        for member in range(size):
            pick = got[0]
            for t in range(1, size):
                pick = jnp.where((member ^ digit) == t, got[t], pick)
            ordered.append(pick)
        while len(ordered) > 1:
            ordered = [ordered[k] + ordered[k + 1] for k in range(0, len(ordered), 2)]
        value = ordered[0]
        shift += bits
    return value


def index_table(index, length):
    groups = -(-length // LANES)
    lo = index % LANES
    hi = index // LANES
    lo_hot = (lo[:, None] == jnp.arange(LANES, dtype=jnp.int32)[None, :]).astype(jnp.float32)
    hi_mask = (hi[None, :] == jnp.arange(groups, dtype=jnp.int32)[:, None]).astype(jnp.float32)
    lo_hot_t = (jnp.arange(LANES, dtype=jnp.int32)[:, None] == lo[None, :]).astype(jnp.float32)
    return lo_hot, hi_mask, length, lo_hot_t


def gather_cols(values, table, precision=lax.Precision.HIGH):
    lo_hot, hi_mask, length, lo_hot_t = table
    groups = hi_mask.shape[0]
    rows = values.shape[0]
    padded = jnp.pad(values, ((0, 0), (0, groups * LANES - length)))
    split = padded.reshape(rows, groups, LANES)
    picked = jnp.einsum("rab,bn->ran", split, lo_hot_t, precision=precision)
    return jnp.sum(picked * hi_mask[None], axis=1)


def scatter_cols(terms, table):
    lo_hot, hi_mask, length, lo_hot_t = table
    groups = hi_mask.shape[0]
    rows = terms.shape[0]
    spread = terms[:, None, :] * hi_mask[None]
    summed = jnp.einsum("ran,nb->rab", spread, lo_hot, precision=lax.Precision.HIGH)
    return summed.reshape(rows, groups * LANES)[:, :length]


def extend_pieces(values, send_table):
    outgoing = gather_cols(values, send_table)
    ghosts = outgoing.shape[1] // 6
    return [outgoing[:, d * ghosts : (d + 1) * ghosts] for d in range(6)], list(OFFSETS)


def extend_finish(values, moved):
    return jnp.concatenate([values] + moved, axis=1)


def give_back_pieces(extended, send_table):
    owned = send_table[2]
    ghosts = (extended.shape[1] - owned) // 6
    pieces = [extended[:, owned + d * ghosts : owned + (d + 1) * ghosts] for d in range(6)]
    return pieces, [-offset for offset in OFFSETS]


def give_back_finish(extended, moved, send_table):
    owned = send_table[2]
    return extended[:, :owned] + scatter_cols(jnp.concatenate(moved, axis=1), send_table)


def exchange(*groups):
    pieces, offsets, bounds = [], [], []
    rows = max(piece.shape[0] for group_pieces, _ in groups for piece in group_pieces)
    for group_pieces, group_offsets in groups:
        bounds.append((len(pieces), len(group_pieces)))
        pieces += [jnp.pad(piece, ((0, rows - piece.shape[0]), (0, 0))) for piece in group_pieces]
        offsets += group_offsets
    moved = shift_pieces(pieces, offsets)
    out = []
    for (start, count), (group_pieces, _) in zip(bounds, groups):
        out.append([m[: p.shape[0]] for m, p in zip(moved[start : start + count], group_pieces)])
    return out


def extend(values, send_table):
    (moved,) = exchange(extend_pieces(values, send_table))
    return extend_finish(values, moved)


def give_back(extended, send_table):
    (moved,) = exchange(give_back_pieces(extended, send_table))
    return give_back_finish(extended, moved, send_table)


def element_terms(matrices, values):
    return jnp.sum(matrices[None, :, :, :] * values[:, None, :, :], axis=2)


def inner_elements(left, right):
    return jnp.einsum("cke,dke->cd", left, right, precision=highest)


def arrange(pair_part, row_part, modes):
    mode_mode = pair_part[:, :modes, :modes]
    mode_prev = pair_part[:, :modes, modes:]
    prev_mode = pair_part[:, modes:, :modes]
    prev_prev = pair_part[:, modes:, modes:]
    new_mode = jnp.swapaxes(row_part[:, :, :modes], 1, 2)
    new_prev = jnp.swapaxes(row_part[:, :, 2 * modes :], 1, 2)
    upper = jnp.concatenate([mode_mode, new_mode, mode_prev], axis=2)
    lower = jnp.concatenate([prev_mode, new_prev, prev_prev], axis=2)
    return jnp.concatenate([upper, row_part, lower], axis=1)


def shards(
    x_block,
    p_block,
    stiff_elem,
    mass_elem,
    node_elem,
    elem_edge,
    elem_node,
    send_edge,
    send_node,
    grad_pairs,
):
    modes = x_block.shape[0]
    owned_edges = x_block.shape[1]
    edofs, elements = elem_edge.shape
    ndofs = elem_node.shape[0]
    edge_length = owned_edges + 6 * send_edge.shape[1]
    node_length = NNODE + 6 * send_node.shape[1]

    edge_table = index_table(elem_edge.reshape(-1), edge_length)
    node_table = index_table(elem_node.reshape(-1), node_length)
    send_edge_table = index_table(send_edge.reshape(-1), owned_edges)
    send_node_table = index_table(send_node.reshape(-1), NNODE)
    tails = grad_pairs[0]
    heads = grad_pairs[1]
    grad_table = index_table(jnp.concatenate([heads, tails]), node_length)

    def edge_values(extended):
        return gather_cols(extended, edge_table).reshape(extended.shape[0], edofs, elements)

    def edge_sum(terms):
        return scatter_cols(terms.reshape(terms.shape[0], -1), edge_table)

    pair = jnp.concatenate([x_block, p_block], axis=0)
    node_diag_local = scatter_cols(jnp.einsum("jje->je", node_elem).reshape(1, -1), node_table)
    x_out, edge_offsets = extend_pieces(x_block, send_edge_table)
    p_out, _ = extend_pieces(p_block, send_edge_table)
    pair_out = [jnp.concatenate([a, b], axis=0) for a, b in zip(x_out, p_out)]
    pair_moved, node_diag_moved = exchange(
        (pair_out, edge_offsets), give_back_pieces(node_diag_local, send_node_table)
    )
    pair_values = gather_cols(extend_finish(pair, pair_moved), edge_table, highest).reshape(
        2 * modes, edofs, elements
    )
    node_diag = give_back_finish(node_diag_local, node_diag_moved, send_node_table)[0]
    stiff_pair = element_terms(stiff_elem, pair_values)
    mass_pair = element_terms(mass_elem, pair_values)
    edge_diag_terms = jnp.einsum("jje->je", stiff_elem)[None]
    images = give_back(
        edge_sum(jnp.concatenate([stiff_pair[:modes], mass_pair[:modes], edge_diag_terms], axis=0)),
        send_edge_table,
    )
    stiff_x = images[:modes]
    mass_x = images[modes : 2 * modes]
    edge_diag = images[2 * modes]
    stiff_part = inner_elements(pair_values, stiff_pair)
    mass_part = inner_elements(pair_values, mass_pair)
    numerator, denominator = all_sum(
        jnp.stack([jnp.diagonal(stiff_part)[:modes], jnp.diagonal(mass_part)[:modes]])
    )
    quotient = numerator / denominator
    residual = stiff_x - quotient[:, None] * mass_x

    def stiff_image(vectors):
        values = edge_values(extend(vectors, send_edge_table))
        return give_back(edge_sum(element_terms(stiff_elem, values)), send_edge_table)

    center = 0.5 * (interval_high + interval_low)
    spread = 0.5 * (interval_high - interval_low)
    sigma = center / spread
    rho_now = 1.0 / sigma
    step_dir = residual / (center * edge_diag)
    smooth = step_dir
    for turn in range(CHEB_DEG - 1):
        rho_next = 1.0 / (2.0 * sigma - rho_now)
        remain = residual - stiff_image(smooth)
        step_dir = rho_next * rho_now * step_dir + 2.0 * rho_next / spread * remain / edge_diag
        smooth = smooth + step_dir
        rho_now = rho_next
    after = residual - stiff_image(smooth)
    gathered_res = scatter_cols(jnp.concatenate([after, -after], axis=1), grad_table)
    nodal_res = give_back(gathered_res, send_node_table)
    first = jacobi_weight * nodal_res / node_diag
    first_values = gather_cols(extend(first, send_node_table), node_table).reshape(modes, ndofs, elements)
    node_image = give_back(
        scatter_cols(element_terms(node_elem, first_values).reshape(modes, -1), node_table),
        send_node_table,
    )
    second = first + jacobi_weight * (nodal_res - node_image) / node_diag
    ends = gather_cols(extend(second, send_node_table), grad_table)
    w_block = smooth + ends[:, :owned_edges] - ends[:, owned_edges:]
    w_values = edge_values(extend(w_block, send_edge_table))
    stiff_wterm = element_terms(stiff_elem, w_values)
    mass_wterm = element_terms(mass_elem, w_values)
    basis_values = jnp.concatenate([pair_values[:modes], w_values, pair_values[modes:]], axis=0)
    w_rows = jnp.stack(
        [inner_elements(stiff_wterm, basis_values), inner_elements(mass_wterm, basis_values)]
    )
    full_gram = all_sum(arrange(jnp.stack([stiff_part, mass_part]), w_rows, modes))
    total_edges = owned_edges * lax.axis_size("dom")
    return (w_block, full_gram[0] / total_edges, full_gram[1] / total_edges)


def solution(mesh):
    in_specs = (
        P(None, "dom"),
        P(None, "dom"),
        P(None, None, "dom"),
        P(None, None, "dom"),
        P(None, None, "dom"),
        P(None, "dom"),
        P(None, "dom"),
        P(None, "dom"),
        P(None, "dom"),
        P(None, "dom"),
    )
    out_specs = (P(None, "dom"), P(), P())
    return jax.shard_map(shards, mesh=mesh, in_specs=in_specs, out_specs=out_specs, check_vma=False)
```

```python
import jax
import jax.numpy as jnp
from jax import lax
from jax.sharding import PartitionSpec as P

CHEB_DEG = 3
NNODE = 384
LANES = 128


highest = lax.Precision.HIGHEST
OFFSETS = (1, -1, 4, -4, 16, -16)
interval_low = 0.3
interval_high = 1.7
jacobi_weight = 0.7


def from_behind(shard, axis, by):
    length = lax.axis_size(axis)
    return lax.ppermute(shard, axis, [(i, (i + by) % length) for i in range(length)])


def shift_pieces(pieces, offsets):
    length = lax.axis_size("dom")
    out = [None] * len(pieces)
    targets = {}
    for number, offset in enumerate(offsets):
        targets.setdefault(offset % length, []).append(number)
    for offset, numbers in targets.items():
        sizes = [pieces[number].shape[1] for number in numbers]
        moved = from_behind(jnp.concatenate([pieces[number] for number in numbers], axis=1), "dom", offset)
        start = 0
        for number, size in zip(numbers, sizes):
            out[number] = moved[:, start : start + size]
            start += size
    return out


def all_sum(value):
    length = lax.axis_size("dom")
    if length & (length - 1):
        return lax.psum(value, "dom")
    me = lax.axis_index("dom")
    shift = 0
    while (1 << shift) < length:
        bits = 2 if (4 << shift) <= length else 1
        size = 1 << bits
        got = [value] + [
            lax.ppermute(value, "dom", [(i, i ^ (t << shift)) for i in range(length)])
            for t in range(1, size)
        ]
        digit = (me >> shift) & (size - 1)
        ordered = []
        for member in range(size):
            pick = got[0]
            for t in range(1, size):
                pick = jnp.where((member ^ digit) == t, got[t], pick)
            ordered.append(pick)
        while len(ordered) > 1:
            ordered = [ordered[k] + ordered[k + 1] for k in range(0, len(ordered), 2)]
        value = ordered[0]
        shift += bits
    return value


def index_table(index, length):
    groups = -(-length // LANES)
    lo = index % LANES
    hi = index // LANES
    lo_hot = (lo[:, None] == jnp.arange(LANES, dtype=jnp.int32)[None, :]).astype(jnp.float32)
    hi_mask = (hi[None, :] == jnp.arange(groups, dtype=jnp.int32)[:, None]).astype(jnp.float32)
    lo_hot_t = (jnp.arange(LANES, dtype=jnp.int32)[:, None] == lo[None, :]).astype(jnp.float32)
    return lo_hot, hi_mask, length, lo_hot_t


def gather_cols(values, table, precision=lax.Precision.HIGH):
    lo_hot, hi_mask, length, lo_hot_t = table
    groups = hi_mask.shape[0]
    rows = values.shape[0]
    padded = jnp.pad(values, ((0, 0), (0, groups * LANES - length)))
    split = padded.reshape(rows, groups, LANES)
    picked = jnp.einsum("rab,bn->ran", split, lo_hot_t, precision=precision)
    return jnp.sum(picked * hi_mask[None], axis=1)


def gather_split(owned, ghosts, table):
    lo_hot, hi_mask, length, lo_hot_t = table
    rows, width = owned.shape
    if width % LANES:
        return gather_cols(jnp.concatenate([owned, ghosts], axis=1), table)
    split = width // LANES
    groups = hi_mask.shape[0]
    high = lax.Precision.HIGH
    near = jnp.einsum("rab,bn->ran", owned.reshape(rows, split, LANES), lo_hot_t, precision=high)
    far = jnp.pad(ghosts, ((0, 0), (0, (groups - split) * LANES - ghosts.shape[1])))
    far = jnp.einsum("rab,bn->ran", far.reshape(rows, groups - split, LANES), lo_hot_t, precision=high)
    return jnp.sum(near * hi_mask[None, :split], axis=1) + jnp.sum(far * hi_mask[None, split:], axis=1)


def scatter_cols(terms, table):
    lo_hot, hi_mask, length, lo_hot_t = table
    groups = hi_mask.shape[0]
    rows = terms.shape[0]
    spread = terms[:, None, :] * hi_mask[None]
    summed = jnp.einsum("ran,nb->rab", spread, lo_hot, precision=lax.Precision.HIGH)
    return summed.reshape(rows, groups * LANES)[:, :length]


def extend_pieces(values, send_table):
    outgoing = gather_cols(values, send_table)
    ghosts = outgoing.shape[1] // 6
    return [outgoing[:, d * ghosts : (d + 1) * ghosts] for d in range(6)], list(OFFSETS)


def extend_finish(values, moved):
    return jnp.concatenate([values] + moved, axis=1)


def give_back_pieces(extended, send_table):
    owned = send_table[2]
    ghosts = (extended.shape[1] - owned) // 6
    pieces = [extended[:, owned + d * ghosts : owned + (d + 1) * ghosts] for d in range(6)]
    return pieces, [-offset for offset in OFFSETS]


def give_back_finish(extended, moved, send_table):
    owned = send_table[2]
    return extended[:, :owned] + scatter_cols(jnp.concatenate(moved, axis=1), send_table)


def exchange(*groups):
    pieces, offsets, bounds = [], [], []
    rows = max(piece.shape[0] for group_pieces, _ in groups for piece in group_pieces)
    for group_pieces, group_offsets in groups:
        bounds.append((len(pieces), len(group_pieces)))
        pieces += [jnp.pad(piece, ((0, rows - piece.shape[0]), (0, 0))) for piece in group_pieces]
        offsets += group_offsets
    moved = shift_pieces(pieces, offsets)
    out = []
    for (start, count), (group_pieces, _) in zip(bounds, groups):
        out.append([m[: p.shape[0]] for m, p in zip(moved[start : start + count], group_pieces)])
    return out


def extend(values, send_table):
    (moved,) = exchange(extend_pieces(values, send_table))
    return extend_finish(values, moved)


def give_back(extended, send_table):
    (moved,) = exchange(give_back_pieces(extended, send_table))
    return give_back_finish(extended, moved, send_table)


def element_terms(matrices, values):
    return jnp.sum(matrices[None, :, :, :] * values[:, None, :, :], axis=2)


def inner_elements(left, right):
    return jnp.einsum("cke,dke->cd", left, right, precision=highest)


def arrange(pair_part, row_part, modes):
    mode_mode = pair_part[:, :modes, :modes]
    mode_prev = pair_part[:, :modes, modes:]
    prev_mode = pair_part[:, modes:, :modes]
    prev_prev = pair_part[:, modes:, modes:]
    new_mode = jnp.swapaxes(row_part[:, :, :modes], 1, 2)
    new_prev = jnp.swapaxes(row_part[:, :, 2 * modes :], 1, 2)
    upper = jnp.concatenate([mode_mode, new_mode, mode_prev], axis=2)
    lower = jnp.concatenate([prev_mode, new_prev, prev_prev], axis=2)
    return jnp.concatenate([upper, row_part, lower], axis=1)


def shards(
    x_block,
    p_block,
    stiff_elem,
    mass_elem,
    node_elem,
    elem_edge,
    elem_node,
    send_edge,
    send_node,
    grad_pairs,
):
    modes = x_block.shape[0]
    owned_edges = x_block.shape[1]
    edofs, elements = elem_edge.shape
    ndofs = elem_node.shape[0]
    edge_length = owned_edges + 6 * send_edge.shape[1]
    node_length = NNODE + 6 * send_node.shape[1]

    edge_table = index_table(elem_edge.reshape(-1), edge_length)
    node_table = index_table(elem_node.reshape(-1), node_length)
    send_edge_table = index_table(send_edge.reshape(-1), owned_edges)
    send_node_table = index_table(send_node.reshape(-1), NNODE)
    tails = grad_pairs[0]
    heads = grad_pairs[1]
    grad_table = index_table(jnp.concatenate([heads, tails]), node_length)

    def edge_values(extended):
        return gather_cols(extended, edge_table).reshape(extended.shape[0], edofs, elements)

    def edge_sum(terms):
        return scatter_cols(terms.reshape(terms.shape[0], -1), edge_table)

    pair = jnp.concatenate([x_block, p_block], axis=0)
    node_diag_local = scatter_cols(jnp.einsum("jje->je", node_elem).reshape(1, -1), node_table)
    pair_moved, node_diag_moved = exchange(
        extend_pieces(pair, send_edge_table), give_back_pieces(node_diag_local, send_node_table)
    )
    pair_values = gather_cols(extend_finish(pair, pair_moved), edge_table, highest).reshape(
        2 * modes, edofs, elements
    )
    node_diag = give_back_finish(node_diag_local, node_diag_moved, send_node_table)[0]
    stiff_pair = element_terms(stiff_elem, pair_values)
    mass_pair = element_terms(mass_elem, pair_values)
    edge_diag_terms = jnp.einsum("jje->je", stiff_elem)[None]
    images = give_back(
        edge_sum(jnp.concatenate([stiff_pair[:modes], mass_pair[:modes], edge_diag_terms], axis=0)),
        send_edge_table,
    )
    stiff_x = images[:modes]
    mass_x = images[modes : 2 * modes]
    edge_diag = images[2 * modes]
    stiff_part = inner_elements(pair_values, stiff_pair)
    mass_part = inner_elements(pair_values, mass_pair)
    numerator, denominator = all_sum(
        jnp.stack([jnp.diagonal(stiff_part)[:modes], jnp.diagonal(mass_part)[:modes]])
    )
    quotient = numerator / denominator
    residual = stiff_x - quotient[:, None] * mass_x

    def stiff_image(vectors):
        values = edge_values(extend(vectors, send_edge_table))
        return give_back(edge_sum(element_terms(stiff_elem, values)), send_edge_table)

    center = 0.5 * (interval_high + interval_low)
    spread = 0.5 * (interval_high - interval_low)
    sigma = center / spread
    rho_now = 1.0 / sigma
    step_dir = residual / (center * edge_diag)
    smooth = step_dir
    for turn in range(CHEB_DEG - 1):
        rho_next = 1.0 / (2.0 * sigma - rho_now)
        remain = residual - stiff_image(smooth)
        step_dir = rho_next * rho_now * step_dir + 2.0 * rho_next / spread * remain / edge_diag
        smooth = smooth + step_dir
        rho_now = rho_next
    after = residual - stiff_image(smooth)
    gathered_res = scatter_cols(jnp.concatenate([after, -after], axis=1), grad_table)
    nodal_res = give_back(gathered_res, send_node_table)
    first = jacobi_weight * nodal_res / node_diag
    first_values = gather_cols(extend(first, send_node_table), node_table).reshape(modes, ndofs, elements)
    node_image = give_back(
        scatter_cols(element_terms(node_elem, first_values).reshape(modes, -1), node_table),
        send_node_table,
    )
    second = first + jacobi_weight * (nodal_res - node_image) / node_diag
    ends = gather_cols(extend(second, send_node_table), grad_table)
    w_block = smooth + ends[:, :owned_edges] - ends[:, owned_edges:]
    (w_moved,) = exchange(extend_pieces(w_block, send_edge_table))
    w_values = gather_split(w_block, jnp.concatenate(w_moved, axis=1), edge_table).reshape(
        modes, edofs, elements
    )
    stiff_wterm = element_terms(stiff_elem, w_values)
    mass_wterm = element_terms(mass_elem, w_values)
    basis_values = jnp.concatenate([pair_values[:modes], w_values, pair_values[modes:]], axis=0)
    w_rows = jnp.stack(
        [inner_elements(stiff_wterm, basis_values), inner_elements(mass_wterm, basis_values)]
    )
    full_gram = all_sum(arrange(jnp.stack([stiff_part, mass_part]), w_rows, modes))
    total_edges = owned_edges * lax.axis_size("dom")
    return (w_block, full_gram[0] / total_edges, full_gram[1] / total_edges)


def solution(mesh):
    in_specs = (
        P(None, "dom"),
        P(None, "dom"),
        P(None, None, "dom"),
        P(None, None, "dom"),
        P(None, None, "dom"),
        P(None, "dom"),
        P(None, "dom"),
        P(None, "dom"),
        P(None, "dom"),
        P(None, "dom"),
    )
    out_specs = (P(None, "dom"), P(), P())
    return jax.shard_map(shards, mesh=mesh, in_specs=in_specs, out_specs=out_specs, check_vma=False)
```

```python
import jax
import jax.numpy as jnp
from jax import lax
from jax.sharding import PartitionSpec as P

CHEB_DEG = 3
NNODE = 384
LANES = 128


highest = lax.Precision.HIGHEST
OFFSETS = (1, -1, 4, -4, 16, -16)
interval_low = 0.3
interval_high = 1.7
jacobi_weight = 0.7


def from_behind(shard, axis, by):
    length = lax.axis_size(axis)
    return lax.ppermute(shard, axis, [(i, (i + by) % length) for i in range(length)])


def shift_pieces(pieces, offsets):
    length = lax.axis_size("dom")
    out = [None] * len(pieces)
    targets = {}
    for number, offset in enumerate(offsets):
        targets.setdefault(offset % length, []).append(number)
    for offset, numbers in targets.items():
        sizes = [pieces[number].shape[1] for number in numbers]
        moved = from_behind(jnp.concatenate([pieces[number] for number in numbers], axis=1), "dom", offset)
        start = 0
        for number, size in zip(numbers, sizes):
            out[number] = moved[:, start : start + size]
            start += size
    return out


def all_sum(value):
    length = lax.axis_size("dom")
    if length & (length - 1):
        return lax.psum(value, "dom")
    me = lax.axis_index("dom")
    shift = 0
    while (1 << shift) < length:
        bits = 2 if (4 << shift) <= length else 1
        size = 1 << bits
        got = [value] + [
            lax.ppermute(value, "dom", [(i, i ^ (t << shift)) for i in range(length)])
            for t in range(1, size)
        ]
        digit = (me >> shift) & (size - 1)
        ordered = []
        for member in range(size):
            pick = got[0]
            for t in range(1, size):
                pick = jnp.where((member ^ digit) == t, got[t], pick)
            ordered.append(pick)
        while len(ordered) > 1:
            ordered = [ordered[k] + ordered[k + 1] for k in range(0, len(ordered), 2)]
        value = ordered[0]
        shift += bits
    return value


def index_table(index, length):
    groups = -(-length // LANES)
    lo = index % LANES
    hi = index // LANES
    lo_hot = (lo[:, None] == jnp.arange(LANES, dtype=jnp.int32)[None, :]).astype(jnp.float32)
    hi_mask = (hi[None, :] == jnp.arange(groups, dtype=jnp.int32)[:, None]).astype(jnp.float32)
    lo_hot_t = (jnp.arange(LANES, dtype=jnp.int32)[:, None] == lo[None, :]).astype(jnp.float32)
    return lo_hot, hi_mask, length, lo_hot_t


def gather_cols(values, table, precision=lax.Precision.HIGH):
    lo_hot, hi_mask, length, lo_hot_t = table
    groups = hi_mask.shape[0]
    rows = values.shape[0]
    padded = jnp.pad(values, ((0, 0), (0, groups * LANES - length)))
    split = padded.reshape(rows, groups, LANES)
    picked = jnp.einsum("rab,bn->ran", split, lo_hot_t, precision=precision)
    return jnp.sum(picked * hi_mask[None], axis=1)


def scatter_cols(terms, table):
    lo_hot, hi_mask, length, lo_hot_t = table
    groups = hi_mask.shape[0]
    rows = terms.shape[0]
    spread = terms[:, None, :] * hi_mask[None]
    summed = jnp.einsum("ran,nb->rab", spread, lo_hot, precision=lax.Precision.HIGH)
    return summed.reshape(rows, groups * LANES)[:, :length]


def extend_pieces(values, send_table):
    outgoing = gather_cols(values, send_table)
    ghosts = outgoing.shape[1] // 6
    return [outgoing[:, d * ghosts : (d + 1) * ghosts] for d in range(6)], list(OFFSETS)


def extend_finish(values, moved):
    return jnp.concatenate([values] + moved, axis=1)


def give_back_pieces(extended, send_table):
    owned = send_table[2]
    ghosts = (extended.shape[1] - owned) // 6
    pieces = [extended[:, owned + d * ghosts : owned + (d + 1) * ghosts] for d in range(6)]
    return pieces, [-offset for offset in OFFSETS]


def give_back_finish(extended, moved, send_table):
    owned = send_table[2]
    return extended[:, :owned] + scatter_cols(jnp.concatenate(moved, axis=1), send_table)


def exchange(*groups):
    pieces, offsets, bounds = [], [], []
    rows = max(piece.shape[0] for group_pieces, _ in groups for piece in group_pieces)
    for group_pieces, group_offsets in groups:
        bounds.append((len(pieces), len(group_pieces)))
        pieces += [jnp.pad(piece, ((0, rows - piece.shape[0]), (0, 0))) for piece in group_pieces]
        offsets += group_offsets
    moved = shift_pieces(pieces, offsets)
    out = []
    for (start, count), (group_pieces, _) in zip(bounds, groups):
        out.append([m[: p.shape[0]] for m, p in zip(moved[start : start + count], group_pieces)])
    return out


def extend(values, send_table):
    (moved,) = exchange(extend_pieces(values, send_table))
    return extend_finish(values, moved)


def give_back(extended, send_table):
    (moved,) = exchange(give_back_pieces(extended, send_table))
    return give_back_finish(extended, moved, send_table)


def element_terms(matrices, values):
    return jnp.sum(matrices[None, :, :, :] * values[:, None, :, :], axis=2)


def inner_elements(left, right):
    return jnp.einsum("cke,dke->cd", left, right, precision=highest)


def arrange(pair_part, row_part, modes):
    mode_mode = pair_part[:, :modes, :modes]
    mode_prev = pair_part[:, :modes, modes:]
    prev_mode = pair_part[:, modes:, :modes]
    prev_prev = pair_part[:, modes:, modes:]
    new_mode = jnp.swapaxes(row_part[:, :, :modes], 1, 2)
    new_prev = jnp.swapaxes(row_part[:, :, 2 * modes :], 1, 2)
    upper = jnp.concatenate([mode_mode, new_mode, mode_prev], axis=2)
    lower = jnp.concatenate([prev_mode, new_prev, prev_prev], axis=2)
    return jnp.concatenate([upper, row_part, lower], axis=1)


def shards(
    x_block,
    p_block,
    stiff_elem,
    mass_elem,
    node_elem,
    elem_edge,
    elem_node,
    send_edge,
    send_node,
    grad_pairs,
):
    modes = x_block.shape[0]
    owned_edges = x_block.shape[1]
    edofs, elements = elem_edge.shape
    ndofs = elem_node.shape[0]
    edge_length = owned_edges + 6 * send_edge.shape[1]
    node_length = NNODE + 6 * send_node.shape[1]

    edge_table = index_table(elem_edge.reshape(-1), edge_length)
    node_table = index_table(elem_node.reshape(-1), node_length)
    send_edge_table = index_table(send_edge.reshape(-1), owned_edges)
    send_node_table = index_table(send_node.reshape(-1), NNODE)
    tails = grad_pairs[0]
    heads = grad_pairs[1]
    grad_table = index_table(jnp.concatenate([heads, tails]), node_length)

    def edge_values(extended):
        return gather_cols(extended, edge_table).reshape(extended.shape[0], edofs, elements)

    def edge_sum(terms):
        return scatter_cols(terms.reshape(terms.shape[0], -1), edge_table)

    pair = jnp.concatenate([x_block, p_block], axis=0)
    node_diag_local = scatter_cols(jnp.einsum("jje->je", node_elem).reshape(1, -1), node_table)
    pair_moved, node_diag_moved = exchange(
        extend_pieces(pair, send_edge_table), give_back_pieces(node_diag_local, send_node_table)
    )
    pair_values = gather_cols(extend_finish(pair, pair_moved), edge_table, highest).reshape(
        2 * modes, edofs, elements
    )
    node_diag = give_back_finish(node_diag_local, node_diag_moved, send_node_table)[0]
    stiff_pair = element_terms(stiff_elem, pair_values)
    mass_pair = element_terms(mass_elem, pair_values)
    edge_diag_terms = jnp.einsum("jje->je", stiff_elem)[None]
    images = give_back(
        edge_sum(jnp.concatenate([stiff_pair[:modes], mass_pair[:modes], edge_diag_terms], axis=0)),
        send_edge_table,
    )
    stiff_x = images[:modes]
    mass_x = images[modes : 2 * modes]
    edge_diag = images[2 * modes]
    stiff_part = inner_elements(pair_values, stiff_pair)
    mass_part = inner_elements(pair_values, mass_pair)
    numerator, denominator = all_sum(
        jnp.stack([jnp.diagonal(stiff_part)[:modes], jnp.diagonal(mass_part)[:modes]])
    )
    quotient = numerator / denominator
    residual = stiff_x - quotient[:, None] * mass_x

    def stiff_image(vectors):
        values = edge_values(extend(vectors, send_edge_table))
        return give_back(edge_sum(element_terms(stiff_elem, values)), send_edge_table)

    center = 0.5 * (interval_high + interval_low)
    spread = 0.5 * (interval_high - interval_low)
    sigma = center / spread
    rho_now = 1.0 / sigma
    step_dir = residual / (center * edge_diag)
    smooth = step_dir
    for turn in range(CHEB_DEG - 1):
        rho_next = 1.0 / (2.0 * sigma - rho_now)
        remain = residual - stiff_image(smooth)
        step_dir = rho_next * rho_now * step_dir + 2.0 * rho_next / spread * remain / edge_diag
        smooth = smooth + step_dir
        rho_now = rho_next
    after = residual - stiff_image(smooth)
    gathered_res = scatter_cols(jnp.concatenate([after, -after], axis=1), grad_table)
    nodal_res = give_back(gathered_res, send_node_table)
    first = jacobi_weight * nodal_res / node_diag
    first_values = gather_cols(extend(first, send_node_table), node_table).reshape(modes, ndofs, elements)
    node_image = give_back(
        scatter_cols(element_terms(node_elem, first_values).reshape(modes, -1), node_table),
        send_node_table,
    )
    second = first + jacobi_weight * (nodal_res - node_image) / node_diag
    ends = gather_cols(extend(second, send_node_table), grad_table)
    w_block = smooth + ends[:, :owned_edges] - ends[:, owned_edges:]
    w_values = edge_values(extend(w_block, send_edge_table))
    stiff_wterm = element_terms(stiff_elem, w_values)
    mass_wterm = element_terms(mass_elem, w_values)
    basis_values = jnp.concatenate([pair_values[:modes], w_values, pair_values[modes:]], axis=0)
    w_rows = inner_elements(jnp.concatenate([stiff_wterm, mass_wterm], axis=0), basis_values)
    w_rows = w_rows.reshape(2, modes, -1)
    full_gram = all_sum(arrange(jnp.stack([stiff_part, mass_part]), w_rows, modes))
    total_edges = owned_edges * lax.axis_size("dom")
    return (w_block, full_gram[0] / total_edges, full_gram[1] / total_edges)


def solution(mesh):
    in_specs = (
        P(None, "dom"),
        P(None, "dom"),
        P(None, None, "dom"),
        P(None, None, "dom"),
        P(None, None, "dom"),
        P(None, "dom"),
        P(None, "dom"),
        P(None, "dom"),
        P(None, "dom"),
        P(None, "dom"),
    )
    out_specs = (P(None, "dom"), P(), P())
    return jax.shard_map(shards, mesh=mesh, in_specs=in_specs, out_specs=out_specs, check_vma=False)
```
